32 devices in a mesh: ctx: 8 (over y, x, core), tp: 4 (over z).
Axes of the slice: x: 2, y: 2, z: 4, core: 2. Of those that a mesh axis runs over, the one named last changes fastest.
Arguments:
- stream: bfloat16 [1024, 4096], P('ctx', 'tp'), may hold values from -52 to 52
- shutter: bfloat16 [1024, 4096], P('ctx', 'tp'), may hold values from -6 to 6
- feeder: bfloat16 [1024, 4096], P('ctx', 'tp'), may hold values from -6 to 6
- stencil: float32 [7, 4096], P(None, 'tp'), may hold values from -2 to 2
- valves: bfloat16 [1024, 4096], P('ctx', 'tp'), may hold values from -6 to 6
- intake: bfloat16 [1024, 4096], P('ctx', 'tp'), may hold values from -6 to 6
- kernel: float32 [128, 4096], P(None, 'tp'), may hold values from -0.5 to 0.5
- scaling: float32 [4096], P('tp'), may hold values from 0.1 to 1.9
- queries: bfloat16 [1024, 4096], P('ctx', 'tp'), may hold values from -87 to 87
- matchers: bfloat16 [1024, 4096], P('ctx', 'tp'), may hold values from -6 to 6
- segments: int32 [1024], replicated, may hold values from 0 to 3, never falling along the last dimension, each value on 1 to 768 neighbouring positions
- cotangent: bfloat16 [1024, 4096], P('ctx', 'tp'), may hold values from -6 to 6
Outputs:
- result: bfloat16 [1024, 4096], P('ctx', 'tp')
- stream_grad: bfloat16 [1024, 4096], P('ctx', 'tp')
- shutter_grad: bfloat16 [1024, 4096], P('ctx', 'tp')
- feeder_grad: bfloat16 [1024, 4096], P('ctx', 'tp')
- stencil_grad: float32 [7, 4096], P(None, 'tp')
- valves_grad: bfloat16 [1024, 4096], P('ctx', 'tp')
- intake_grad: bfloat16 [1024, 4096], P('ctx', 'tp')
- kernel_grad: float32 [128, 4096], P(None, 'tp')
- scaling_grad: float32 [4096], P('tp')
- queries_grad: bfloat16 [1024, 4096], P('ctx', 'tp')
- matchers_grad: bfloat16 [1024, 4096], P('ctx', 'tp')
The draws below stay inside these ranges and needn't reach their ends.
Inputs may be any that keep to these rules, and one draw needn't show every extreme that they name: `segments`: document numbers never fall along the context; each of the 4 documents covers 1 to 768 positions, and one covers exactly 768.
All inputs are finite; a program needn't handle non-finite values.
Results may differ from the reference program's by a relative error of at most 0.03.
Values may be sent and summed in bfloat16 or wider, within the bound.
No kernel may reach another device: no remote copies, remote signals or barrier semaphores. Data moves between devices by JAX's collectives and lax.ppermute only.
A program may use at most 192 MiB of HBM per device.

```python
import math
import jax
import jax.numpy as jnp
import numpy as np
from jax import lax

H = 32
HD = 128
D = 4096
KS = 7
KM = 128
SEGMENTS = 4
TOK_DEV = 128
TOKENS = 1024


def draw_stream(key, part):
    noise_key = jax.random.fold_in(jax.random.fold_in(key, 11), 0)
    column_pos = jnp.arange(D, dtype=jnp.float32) / max(D - 1, 1)
    noise = jnp.clip(jax.random.normal(noise_key, (TOKENS, D), jnp.float32), -6.0, 6.0)
    return (noise * jnp.power(3.0, column_pos)).astype(jnp.bfloat16)


def attention_pair(key):
    key_draw, query_draw = jax.random.split(jax.random.fold_in(key, 23), 2)
    key_rows = jnp.clip(jax.random.normal(key_draw, (TOKENS, D), jnp.float32), -6.0, 6.0)
    query_rows = jnp.clip(jax.random.normal(query_draw, (TOKENS, D), jnp.float32), -6.0, 6.0)
    return (query_rows, key_rows)


def draw_queries(key, part):
    return attention_pair(key)[0].astype(jnp.bfloat16)


def draw_matchers(key, part):
    return attention_pair(key)[1].astype(jnp.bfloat16)


def block_scale(stream_key, extent, shards, smallest, largest):
    level, own = 1.0, jax.random.fold_in(stream_key, 6)
    for dim, shards_of in shards:
        heights = jnp.exp(jax.random.uniform(jax.random.fold_in(own, dim), (shards_of,), jnp.float32, smallest / len(shards), largest / len(shards)))
        level = level * jnp.repeat(heights, extent[dim] // shards_of).reshape([-1 if axis == dim else 1 for axis in range(len(extent))])
    return level


def split_up(number_of, total, bound, skew):
    loads = [(1 << 20) // math.isqrt(standing ** skew) + 1 for standing in range(2, number_of + 1)]
    surplus, holding = total - bound - (number_of - 1), [1] * (number_of - 1)
    while surplus > 0:
        movable = [i for i in range(number_of - 1) if holding[i] < bound]
        mass, remaining = sum([loads[i] for i in movable]), surplus
        for i in movable:
            more = min(bound - holding[i], max(1, remaining * loads[i] // mass), surplus)
            holding[i] = holding[i] + more
            surplus = surplus - more
    return np.array([bound] + holding)


def ragged(stream_key, count, total, most, lean):
    if count == 2:
        one = jax.random.randint(stream_key, (), max(1, total - most), min(most, total - 1) + 1)
        return jnp.stack([one, total - one])
    lengths = jnp.asarray(split_up(count, total, most, lean), jnp.int32)
    couples = (count - 1) // 2
    source_of, taker = lengths[1:1 + 2 * couples:2], lengths[2:2 + 2 * couples:2]
    slack = jnp.minimum(source_of - 1, most - taker)
    moved = jax.random.randint(jax.random.fold_in(stream_key, 1), (couples,), 0, 1 << 20) % (slack + 1)
    lengths = lengths.at[1:1 + 2 * couples:2].set(source_of - moved).at[2:2 + 2 * couples:2].set(taker + moved)
    return lengths[jax.random.permutation(jax.random.fold_in(stream_key, 2), count)]


def centred(key, shape, width, reach, cuts=(), held_as=jnp.bfloat16):
    gain = block_scale(key, shape, cuts, -0.22, 0.18) if cuts else 1.0
    entries = jax.random.normal(key, shape, jnp.float32) * width * gain
    return jnp.minimum(jnp.maximum(entries, -reach), reach).astype(held_as)


def setup_inputs(seed: int = 0) -> dict:
    streams_of = jax.random.split(jax.random.key(seed), 13)
    stream = draw_stream(jax.random.fold_in(streams_of[12], 71), 0)
    shutter = centred(streams_of[1], (TOKENS, D), 1.0, 6.0, ((0, 8), (1, 4)))
    feeder = centred(streams_of[2], (TOKENS, D), 1.0, 6.0, ((0, 8), (1, 4)))
    stencil = centred(streams_of[3], (KS, D), KS ** -0.5, 2.0, ((1, 4),), jnp.float32)
    valves = centred(streams_of[4], (TOKENS, D), 1.0, 6.0, ((0, 8), (1, 4)))
    intake = centred(streams_of[5], (TOKENS, D), 1.0, 6.0, ((0, 8), (1, 4)))
    kernel = centred(streams_of[6], (KM, D), KM ** -0.5, 0.5, ((1, 4),), jnp.float32)
    scaling = jnp.clip(1.0 + 0.18 * jax.random.normal(streams_of[7], (D,), jnp.float32), 0.1, 1.9)
    queries = draw_queries(jax.random.fold_in(streams_of[12], 71), 0)
    matchers = draw_matchers(jax.random.fold_in(streams_of[12], 71), 0)
    segments = jnp.searchsorted(jnp.cumsum(ragged(streams_of[10], SEGMENTS, TOKENS, TOKENS - TOKENS // 4, 0)), jnp.arange(TOKENS), side="right").astype(jnp.int32)
    cotangent = centred(streams_of[11], (TOKENS, D), 1.0, 6.0, ((0, 8), (1, 4)))
    return {"stream": stream, "shutter": shutter, "feeder": feeder, "stencil": stencil, "valves": valves, "intake": intake, "kernel": kernel, "scaling": scaling, "queries": queries, "matchers": matchers, "segments": segments, "cotangent": cotangent}


epsilon = 1e-06

def causal_taps(padded, tap_rows):
    tap_count = tap_rows.shape[0]
    length = padded.shape[0] - tap_count + 1

    def add_tap(tap_index, accumulated):
        start_row = (tap_count - 1 - tap_index).astype(jnp.int32)
        window = lax.dynamic_slice_in_dim(padded, start_row, length, 0)
        return accumulated + tap_rows[tap_index] * window
    return lax.fori_loop(0, tap_count, add_tap, jnp.zeros((length, padded.shape[1]), jnp.float32))

def later_taps(padded, tap_rows):
    tap_count = tap_rows.shape[0]
    length = padded.shape[0] - tap_count + 1

    def add_tap(tap_index, accumulated):
        window = lax.dynamic_slice_in_dim(padded, tap_index.astype(jnp.int32), length, 0)
        return accumulated + tap_rows[tap_index] * window
    return lax.fori_loop(0, tap_count, add_tap, jnp.zeros((length, padded.shape[1]), jnp.float32))

def tap_grads(padded, grads):
    length = grads.shape[0]
    tap_count = padded.shape[0] - length + 1

    def one_tap(tap_index):
        start_row = (tap_count - 1 - tap_index).astype(jnp.int32)
        window = lax.dynamic_slice_in_dim(padded, start_row, length, 0)
        return lax.optimization_barrier(jnp.sum(window * grads, axis=0))
    return lax.map(one_tap, jnp.arange(tap_count, dtype=jnp.int32))

def reference(stream, shutter, feeder, stencil, valves, intake, kernel, scaling, queries, matchers, segments, cotangent):
    highest = lax.Precision.HIGHEST
    scale_factor = 1.0 / math.sqrt(HD)
    widened = stream.astype(jnp.float32)
    inner_one = feeder.astype(jnp.float32) * widened
    padded_one = jnp.concatenate([jnp.zeros((KS - 1, D), jnp.float32), inner_one], axis=0)
    conv_one = causal_taps(padded_one, stencil)
    first_out = (widened + shutter.astype(jnp.float32) * conv_one).astype(jnp.bfloat16)
    first_wide = first_out.astype(jnp.float32)
    inner_two = intake.astype(jnp.float32) * first_wide
    padded_two = jnp.concatenate([jnp.zeros((KM - 1, D), jnp.float32), inner_two], axis=0)
    conv_two = causal_taps(padded_two, kernel)
    second_out = (first_wide + valves.astype(jnp.float32) * conv_two).astype(jnp.bfloat16)
    second_wide = second_out.astype(jnp.float32)
    squares = lax.optimization_barrier(jnp.sum(second_wide * second_wide, axis=1))
    inverse_rms = lax.rsqrt(squares / D + epsilon)
    normed = (second_wide * inverse_rms[:, None] * scaling).astype(jnp.bfloat16)
    blocks = TOKENS // TOK_DEV
    query_blocks = queries.reshape(blocks, TOK_DEV, H, HD)
    cotangent_blocks = cotangent.reshape(blocks, TOK_DEV, H, HD)
    key_heads = matchers.astype(jnp.float32).reshape(TOKENS, H, HD)
    value_heads = normed.astype(jnp.float32).reshape(TOKENS, H, HD)
    key_pos = jnp.arange(TOKENS, dtype=jnp.int32)

    def one_block(accumulated, inputs):
        key_acc, value_acc = accumulated
        query_block, cotangent_block, block_index = inputs
        query_wide = query_block.astype(jnp.float32)
        cotangent_wide = cotangent_block.astype(jnp.float32)
        query_pos = block_index * TOK_DEV + jnp.arange(TOK_DEV, dtype=jnp.int32)
        query_seg = lax.dynamic_slice_in_dim(segments, (block_index * TOK_DEV).astype(jnp.int32), TOK_DEV, 0)
        visible = (key_pos[None, :] <= query_pos[:, None]) & (segments[None, :] == query_seg[:, None])
        scores = jnp.einsum('the,she->hts', query_wide, key_heads, precision=highest) * scale_factor
        scores = jnp.where(visible[None], scores, -jnp.inf)
        row_max = lax.optimization_barrier(jnp.max(scores, axis=2))
        logsum = row_max + jnp.log(lax.optimization_barrier(jnp.sum(jnp.exp(scores - row_max[:, :, None]), axis=2)))
        weights = jnp.exp(scores - logsum[:, :, None]).astype(jnp.bfloat16)
        weights_wide = weights.astype(jnp.float32)
        attended = jnp.einsum('hts,she->the', weights_wide, value_heads, precision=highest)
        weight_grad = jnp.einsum('the,she->hts', cotangent_wide, value_heads, precision=highest)
        row_delta = lax.optimization_barrier(jnp.sum(cotangent_wide * attended, axis=2)).T
        dscore = (scale_factor * weights_wide * (weight_grad - row_delta[:, :, None])).astype(jnp.bfloat16)
        dscore_wide = dscore.astype(jnp.float32)
        query_grad = jnp.einsum('hts,she->the', dscore_wide, key_heads, precision=highest)
        key_term = jnp.einsum('hts,the->she', dscore_wide, query_wide, precision=highest).astype(jnp.bfloat16)
        value_term = jnp.einsum('hts,the->she', weights_wide, cotangent_wide, precision=highest).astype(jnp.bfloat16)
        key_term = lax.optimization_barrier(key_term)
        value_term = lax.optimization_barrier(value_term)
        return ((key_acc + key_term.astype(jnp.float32), value_acc + value_term.astype(jnp.float32)), (attended, query_grad))
    initial = (jnp.zeros((TOKENS, H, HD), jnp.float32), jnp.zeros((TOKENS, H, HD), jnp.float32))
    sums, outputs = lax.scan(one_block, initial, (query_blocks, cotangent_blocks, jnp.arange(blocks, dtype=jnp.int32)))
    attended_all = outputs[0].reshape(TOKENS, D)
    queries_grad = outputs[1].reshape(TOKENS, D).astype(jnp.bfloat16)
    matchers_grad = sums[0].reshape(TOKENS, D).astype(jnp.bfloat16)
    value_grad = sums[1].reshape(TOKENS, D)
    result = (second_wide + attended_all).astype(jnp.bfloat16)
    normalizer = math.sqrt(TOKENS)
    gain_part = value_grad * scaling
    projected = lax.optimization_barrier(jnp.sum(gain_part * second_wide, axis=1))
    scaling_grad = lax.optimization_barrier(jnp.sum(value_grad * second_wide * inverse_rms[:, None], axis=0)) / normalizer
    second_grad = cotangent.astype(jnp.float32) + inverse_rms[:, None] * gain_part - second_wide * (inverse_rms ** 3 * projected / D)[:, None]
    valves_grad = (second_grad * conv_two).astype(jnp.bfloat16)
    dconv_two = second_grad * valves.astype(jnp.float32)
    dinner_two = later_taps(jnp.concatenate([dconv_two, jnp.zeros((KM - 1, D), jnp.float32)], axis=0), kernel)
    intake_grad = (dinner_two * first_wide).astype(jnp.bfloat16)
    kernel_grad = tap_grads(padded_two, dconv_two) / normalizer
    first_grad = second_grad + dinner_two * intake.astype(jnp.float32)
    shutter_grad = (first_grad * conv_one).astype(jnp.bfloat16)
    dconv_one = first_grad * shutter.astype(jnp.float32)
    dinner_one = later_taps(jnp.concatenate([dconv_one, jnp.zeros((KS - 1, D), jnp.float32)], axis=0), stencil)
    feeder_grad = (dinner_one * widened).astype(jnp.bfloat16)
    stencil_grad = tap_grads(padded_one, dconv_one) / normalizer
    stream_grad = (first_grad + dinner_one * feeder.astype(jnp.float32)).astype(jnp.bfloat16)
    return (result, stream_grad, shutter_grad, feeder_grad, stencil_grad, valves_grad, intake_grad, kernel_grad, scaling_grad, queries_grad, matchers_grad)
```

```python
import math

import jax
import jax.numpy as jnp
from jax import lax
from jax.sharding import PartitionSpec as P

HD = 128
D = 4096
KS = 7
KM = 128


epsilon = 1e-06


def as_sent(shard):

    def short(part):
        return part.astype(jnp.bfloat16) if part.dtype == jnp.float32 else part

    return jax.tree.map(short, shard)


def passed_along(value, axis, steps):
    count = lax.axis_size(axis)
    leading, last = (max(0, -steps), min(count, count - steps))
    return lax.ppermute(value, axis, [(source, source + steps) for source in range(leading, last)])


def depthwise(padded, tap_rows):
    return lax.conv_general_dilated(
        padded[None],
        tap_rows[:, None, :],
        (1,),
        "VALID",
        dimension_numbers=("NWC", "WIO", "NWC"),
        feature_group_count=padded.shape[1],
        precision=lax.Precision.HIGHEST,
    )[0]


def neighbor_rows(edge_rows, offset):
    return passed_along(as_sent(edge_rows), "ctx", offset).astype(edge_rows.dtype)


def butterfly_total(value, axis, sent_type=None):
    count = lax.axis_size(axis)
    if count & (count - 1):
        if sent_type is None:
            return lax.psum(value, axis)
        return lax.psum(value.astype(sent_type), axis).astype(value.dtype)
    step = 1
    while step < count:
        pairs = [(source, source ^ step) for source in range(count)]
        if sent_type is None:
            value = value + lax.ppermute(value, axis, pairs)
        else:
            rounded = value.astype(sent_type)
            value = rounded.astype(value.dtype) + lax.ppermute(rounded, axis, pairs).astype(value.dtype)
        step *= 2
    return value


def channel_total(partial_value):
    return butterfly_total(partial_value, "tp")


def shards(
    stream,
    shutter,
    feeder,
    stencil,
    valves,
    intake,
    kernel,
    scaling,
    queries,
    matchers,
    segments,
    cotangent,
):
    local_rows = stream.shape[0]
    width_local = stream.shape[1]
    head_count = width_local // HD
    total_rows = local_rows * lax.axis_size("ctx")
    position = lax.axis_index("ctx") * local_rows
    scale_factor = 1.0 / math.sqrt(HD)
    widened = stream.astype(jnp.float32)
    inner_one = feeder.astype(jnp.float32) * widened
    rim_one = neighbor_rows(inner_one[local_rows - (KS - 1) :], 1)
    padded_one = jnp.concatenate([rim_one, inner_one], axis=0)
    conv_one = depthwise(padded_one, stencil[::-1])
    first_out = (widened + shutter.astype(jnp.float32) * conv_one).astype(jnp.bfloat16)
    first_wide = first_out.astype(jnp.float32)
    inner_two = intake.astype(jnp.float32) * first_wide
    rim_two = neighbor_rows(inner_two[local_rows - (KM - 1) :], 1)
    padded_two = jnp.concatenate([rim_two, inner_two], axis=0)
    conv_two = depthwise(padded_two, kernel[::-1])
    second_out = (first_wide + valves.astype(jnp.float32) * conv_two).astype(jnp.bfloat16)
    second_wide = second_out.astype(jnp.float32)
    squares = channel_total(jnp.sum(second_wide * second_wide, axis=1))
    inverse_rms = lax.rsqrt(squares / D + epsilon)
    normed = (second_wide * inverse_rms[:, None] * scaling).astype(jnp.bfloat16)
    keys_whole, values_whole = (
        lax.all_gather(matchers, "ctx", axis=0, tiled=True),
        lax.all_gather(normed, "ctx", axis=0, tiled=True),
    )
    query_pos = position + jnp.arange(local_rows, dtype=jnp.int32)
    key_pos = jnp.arange(total_rows, dtype=jnp.int32)
    query_seg = lax.dynamic_slice_in_dim(segments, position, local_rows, 0)
    visible = (key_pos[None, :] <= query_pos[:, None]) & (segments[None, :] == query_seg[:, None])
    contract = (((1,), (1,)), ((), ()))
    weight_list = []
    dscore_list = []
    attended_list = []
    query_grad_list = []
    logsum_list = []
    delta_list = []
    for head_index in range(head_count):
        columns = slice(head_index * HD, (head_index + 1) * HD)
        query_head = queries[:, columns]
        key_head = keys_whole[:, columns]
        value_head = values_whole[:, columns]
        cotangent_head = cotangent[:, columns]
        scores = (
            lax.dot_general(query_head, key_head, contract, preferred_element_type=jnp.float32)
            * scale_factor
        )
        scores = jnp.where(visible, scores, -jnp.inf)
        row_max = jnp.max(scores, axis=1)
        logsum = row_max + jnp.log(jnp.sum(jnp.exp(scores - row_max[:, None]), axis=1))
        weights = jnp.exp(scores - logsum[:, None]).astype(jnp.bfloat16)
        attended = jnp.dot(weights, value_head, preferred_element_type=jnp.float32)
        weight_grad = lax.dot_general(
            cotangent_head, value_head, contract, preferred_element_type=jnp.float32
        )
        row_delta = jnp.sum(cotangent_head.astype(jnp.float32) * attended, axis=1)
        dscore = (
            scale_factor * weights.astype(jnp.float32) * (weight_grad - row_delta[:, None])
        ).astype(jnp.bfloat16)
        query_grad = jnp.dot(dscore, key_head, preferred_element_type=jnp.float32)
        weight_list.append(weights)
        dscore_list.append(dscore)
        attended_list.append(attended)
        query_grad_list.append(query_grad)
        logsum_list.append(logsum)
        delta_list.append(row_delta)
    attended_all = jnp.concatenate(attended_list, axis=1)
    result = (second_wide + attended_all).astype(jnp.bfloat16)
    queries_grad = jnp.concatenate(query_grad_list, axis=1).astype(jnp.bfloat16)
    query_heads = queries.reshape(local_rows, head_count, HD)
    cotangent_heads = cotangent.reshape(local_rows, head_count, HD)
    weights_all = jnp.stack(weight_list)
    dscore_all = jnp.stack(dscore_list)
    dscore_part = lax.slice_in_dim(dscore_all, 0, local_rows * lax.axis_size("ctx"), axis=2)
    key_part = jnp.einsum(
        "hts,the->she", dscore_part, query_heads, preferred_element_type=jnp.float32
    )
    value_part = jnp.einsum(
        "hts,the->she", weights_all, cotangent_heads, preferred_element_type=jnp.float32
    )
    summed = lax.psum_scatter(
        jnp.concatenate(
            [
                key_part.reshape(local_rows * lax.axis_size("ctx"), width_local),
                value_part.reshape(local_rows * lax.axis_size("ctx"), width_local),
            ],
            axis=1,
        ).astype(jnp.bfloat16),
        "ctx",
        scatter_dimension=0,
        tiled=True,
    ).astype(jnp.float32)
    matchers_grad = summed[:, :width_local].astype(jnp.bfloat16)
    value_grad = summed[:, width_local:]
    gain_part = value_grad * scaling
    projected = channel_total(jnp.sum(gain_part * second_wide, axis=1))
    scaling_part = jnp.sum(value_grad * second_wide * inverse_rms[:, None], axis=0)
    second_grad = (
        cotangent.astype(jnp.float32)
        + inverse_rms[:, None] * gain_part
        - second_wide * (inverse_rms**3 * projected / D)[:, None]
    )
    valves_grad = (second_grad * conv_two).astype(jnp.bfloat16)
    dconv_two = second_grad * valves.astype(jnp.float32)
    back_two = neighbor_rows(dconv_two[: KM - 1], -1)
    dinner_two = depthwise(jnp.concatenate([dconv_two, back_two], axis=0), kernel)
    intake_grad = (dinner_two * first_wide).astype(jnp.bfloat16)
    kernel_part = depthwise(padded_two, dconv_two)[::-1]
    first_grad = second_grad + dinner_two * intake.astype(jnp.float32)
    shutter_grad = (first_grad * conv_one).astype(jnp.bfloat16)
    dconv_one = first_grad * shutter.astype(jnp.float32)
    back_one = neighbor_rows(dconv_one[: KS - 1], -1)
    dinner_one = depthwise(jnp.concatenate([dconv_one, back_one], axis=0), stencil)
    feeder_grad = (dinner_one * widened).astype(jnp.bfloat16)
    stencil_part = depthwise(padded_one, dconv_one)[::-1]
    stream_grad = (first_grad + dinner_one * feeder.astype(jnp.float32)).astype(jnp.bfloat16)
    filter_sum = butterfly_total(
        jnp.concatenate([kernel_part, scaling_part[None]], axis=0), "ctx", jnp.bfloat16
    )
    kernel_sum = filter_sum[:KM]
    scaling_sum = filter_sum[KM]
    stencil_sum = butterfly_total(stencil_part, "ctx", jnp.bfloat16)
    normalizer = math.sqrt(total_rows)
    return (
        result,
        stream_grad,
        shutter_grad,
        feeder_grad,
        stencil_sum / normalizer,
        valves_grad,
        intake_grad,
        kernel_sum / normalizer,
        scaling_sum / normalizer,
        queries_grad,
        matchers_grad,
    )


def solution(mesh):
    placed = (
        P("ctx", "tp"),
        P("ctx", "tp"),
        P("ctx", "tp"),
        P(None, "tp"),
        P("ctx", "tp"),
        P("ctx", "tp"),
        P(None, "tp"),
        P("tp"),
        P("ctx", "tp"),
        P("ctx", "tp"),
        P(),
        P("ctx", "tp"),
    )
    return jax.shard_map(
        shards,
        mesh=mesh,
        in_specs=placed,
        out_specs=(
            P("ctx", "tp"),
            P("ctx", "tp"),
            P("ctx", "tp"),
            P("ctx", "tp"),
            P(None, "tp"),
            P("ctx", "tp"),
            P("ctx", "tp"),
            P(None, "tp"),
            P("tp"),
            P("ctx", "tp"),
            P("ctx", "tp"),
        ),
        check_vma=False,
    )
```

```python
import math

import jax
import jax.numpy as jnp
from jax import lax
from jax.sharding import PartitionSpec as P

HD = 128
D = 4096
KS = 7
KM = 128


epsilon = 1e-06


def as_sent(shard):

    def short(part):
        return part.astype(jnp.bfloat16) if part.dtype == jnp.float32 else part

    return jax.tree.map(short, shard)


def passed_along(value, axis, steps):
    count = lax.axis_size(axis)
    leading, last = (max(0, -steps), min(count, count - steps))
    return lax.ppermute(value, axis, [(source, source + steps) for source in range(leading, last)])


def depthwise(padded, tap_rows):
    return lax.conv_general_dilated(
        padded[None],
        tap_rows[:, None, :],
        (1,),
        "VALID",
        dimension_numbers=("NWC", "WIO", "NWC"),
        feature_group_count=padded.shape[1],
        precision=lax.Precision.HIGHEST,
    )[0]


def neighbor_rows(edge_rows, offset):
    return passed_along(as_sent(edge_rows), "ctx", offset).astype(edge_rows.dtype)


def butterfly_total(value, axis, sent_type=None):
    count = lax.axis_size(axis)
    if count & (count - 1):
        if sent_type is None:
            return lax.psum(value, axis)
        return lax.psum(value.astype(sent_type), axis).astype(value.dtype)
    step = 1
    while step < count:
        pairs = [(source, source ^ step) for source in range(count)]
        if sent_type is None:
            value = value + lax.ppermute(value, axis, pairs)
        else:
            rounded = value.astype(sent_type)
            value = rounded.astype(value.dtype) + lax.ppermute(rounded, axis, pairs).astype(value.dtype)
        step *= 2
    return value


def channel_total(partial_value):
    return butterfly_total(partial_value, "tp")


def shards(
    stream,
    shutter,
    feeder,
    stencil,
    valves,
    intake,
    kernel,
    scaling,
    queries,
    matchers,
    segments,
    cotangent,
):
    local_rows = stream.shape[0]
    width_local = stream.shape[1]
    head_count = width_local // HD
    total_rows = local_rows * lax.axis_size("ctx")
    position = lax.axis_index("ctx") * local_rows
    scale_factor = 1.0 / math.sqrt(HD)
    widened = stream.astype(jnp.float32)
    inner_one = feeder.astype(jnp.float32) * widened
    rim_one = neighbor_rows(inner_one[local_rows - (KS - 1) :], 1)
    padded_one = jnp.concatenate([rim_one, inner_one], axis=0)
    conv_one = depthwise(padded_one, stencil[::-1])
    first_out = (widened + shutter.astype(jnp.float32) * conv_one).astype(jnp.bfloat16)
    first_wide = first_out.astype(jnp.float32)
    inner_two = intake.astype(jnp.float32) * first_wide
    rim_two = neighbor_rows(inner_two[local_rows - (KM - 1) :], 1)
    padded_two = jnp.concatenate([rim_two, inner_two], axis=0)
    conv_two = depthwise(padded_two, kernel[::-1])
    second_out = (first_wide + valves.astype(jnp.float32) * conv_two).astype(jnp.bfloat16)
    second_wide = second_out.astype(jnp.float32)
    squares = channel_total(jnp.sum(second_wide * second_wide, axis=1))
    inverse_rms = lax.rsqrt(squares / D + epsilon)
    normed = (second_wide * inverse_rms[:, None] * scaling).astype(jnp.bfloat16)
    keys_whole, values_whole = (
        lax.all_gather(matchers, "ctx", axis=0, tiled=True),
        lax.all_gather(normed, "ctx", axis=0, tiled=True),
    )
    query_pos = position + jnp.arange(local_rows, dtype=jnp.int32)
    key_pos = jnp.arange(total_rows, dtype=jnp.int32)
    query_seg = lax.dynamic_slice_in_dim(segments, position, local_rows, 0)
    visible = (key_pos[None, :] <= query_pos[:, None]) & (segments[None, :] == query_seg[:, None])
    contract = (((1,), (1,)), ((), ()))
    weight_list = []
    dscore_list = []
    attended_list = []
    query_grad_list = []
    logsum_list = []
    delta_list = []
    for head_index in range(head_count):
        columns = slice(head_index * HD, (head_index + 1) * HD)
        query_head = queries[:, columns]
        key_head = keys_whole[:, columns]
        value_head = values_whole[:, columns]
        cotangent_head = cotangent[:, columns]
        scores = (
            lax.dot_general(query_head, key_head, contract, preferred_element_type=jnp.float32)
            * scale_factor
        )
        scores = jnp.where(visible, scores, -jnp.inf)
        row_max = jnp.max(scores, axis=1)
        logsum = row_max + jnp.log(jnp.sum(jnp.exp(scores - row_max[:, None]), axis=1))
        weights = jnp.exp(scores - logsum[:, None]).astype(jnp.bfloat16)
        attended = jnp.dot(weights, value_head, preferred_element_type=jnp.float32)
        weight_grad = lax.dot_general(
            cotangent_head, value_head, contract, preferred_element_type=jnp.float32
        )
        row_delta = jnp.sum(cotangent_head.astype(jnp.float32) * attended, axis=1)
        dscore = (
            scale_factor * weights.astype(jnp.float32) * (weight_grad - row_delta[:, None])
        ).astype(jnp.bfloat16)
        query_grad = jnp.dot(dscore, key_head, preferred_element_type=jnp.float32)
        weight_list.append(weights)
        dscore_list.append(dscore)
        attended_list.append(attended)
        query_grad_list.append(query_grad)
        logsum_list.append(logsum)
        delta_list.append(row_delta)
    attended_all = jnp.concatenate(attended_list, axis=1)
    result = (second_wide + attended_all).astype(jnp.bfloat16)
    queries_grad = jnp.concatenate(query_grad_list, axis=1).astype(jnp.bfloat16)
    query_heads = queries.reshape(local_rows, head_count, HD)
    cotangent_heads = cotangent.reshape(local_rows, head_count, HD)
    weights_all = jnp.stack(weight_list)
    dscore_all = jnp.stack(dscore_list)
    dscore_part = lax.slice_in_dim(dscore_all, 0, local_rows * lax.axis_size("ctx"), axis=2)
    key_part = jnp.einsum(
        "hts,the->she", dscore_part, query_heads, preferred_element_type=jnp.float32
    )
    value_part = jnp.einsum(
        "hts,the->she", weights_all, cotangent_heads, preferred_element_type=jnp.float32
    )
    ctx_rows = local_rows * lax.axis_size("ctx")
    value_grad = lax.psum_scatter(
        value_part.reshape(ctx_rows, width_local).astype(jnp.bfloat16),
        "ctx",
        scatter_dimension=0,
        tiled=True,
    ).astype(jnp.float32)
    key_part, value_grad = lax.optimization_barrier((key_part, value_grad))
    matchers_grad = lax.psum_scatter(
        key_part.reshape(ctx_rows, width_local).astype(jnp.bfloat16),
        "ctx",
        scatter_dimension=0,
        tiled=True,
    )
    gain_part = value_grad * scaling
    projected = channel_total(jnp.sum(gain_part * second_wide, axis=1))
    scaling_part = jnp.sum(value_grad * second_wide * inverse_rms[:, None], axis=0)
    second_grad = (
        cotangent.astype(jnp.float32)
        + inverse_rms[:, None] * gain_part
        - second_wide * (inverse_rms**3 * projected / D)[:, None]
    )
    valves_grad = (second_grad * conv_two).astype(jnp.bfloat16)
    dconv_two = second_grad * valves.astype(jnp.float32)
    back_two = neighbor_rows(dconv_two[: KM - 1], -1)
    dinner_two = depthwise(jnp.concatenate([dconv_two, back_two], axis=0), kernel)
    intake_grad = (dinner_two * first_wide).astype(jnp.bfloat16)
    kernel_part = depthwise(padded_two, dconv_two)[::-1]
    first_grad = second_grad + dinner_two * intake.astype(jnp.float32)
    shutter_grad = (first_grad * conv_one).astype(jnp.bfloat16)
    dconv_one = first_grad * shutter.astype(jnp.float32)
    back_one = neighbor_rows(dconv_one[: KS - 1], -1)
    dinner_one = depthwise(jnp.concatenate([dconv_one, back_one], axis=0), stencil)
    feeder_grad = (dinner_one * widened).astype(jnp.bfloat16)
    stencil_part = depthwise(padded_one, dconv_one)[::-1]
    stream_grad = (first_grad + dinner_one * feeder.astype(jnp.float32)).astype(jnp.bfloat16)
    filter_sum = butterfly_total(
        jnp.concatenate([kernel_part, scaling_part[None]], axis=0), "ctx", jnp.bfloat16
    )
    kernel_sum = filter_sum[:KM]
    scaling_sum = filter_sum[KM]
    stencil_sum = butterfly_total(stencil_part, "ctx", jnp.bfloat16)
    normalizer = math.sqrt(total_rows)
    return (
        result,
        stream_grad,
        shutter_grad,
        feeder_grad,
        stencil_sum / normalizer,
        valves_grad,
        intake_grad,
        kernel_sum / normalizer,
        scaling_sum / normalizer,
        queries_grad,
        matchers_grad,
    )


def solution(mesh):
    placed = (
        P("ctx", "tp"),
        P("ctx", "tp"),
        P("ctx", "tp"),
        P(None, "tp"),
        P("ctx", "tp"),
        P("ctx", "tp"),
        P(None, "tp"),
        P("tp"),
        P("ctx", "tp"),
        P("ctx", "tp"),
        P(),
        P("ctx", "tp"),
    )
    return jax.shard_map(
        shards,
        mesh=mesh,
        in_specs=placed,
        out_specs=(
            P("ctx", "tp"),
            P("ctx", "tp"),
            P("ctx", "tp"),
            P("ctx", "tp"),
            P(None, "tp"),
            P("ctx", "tp"),
            P("ctx", "tp"),
            P(None, "tp"),
            P("tp"),
            P("ctx", "tp"),
            P("ctx", "tp"),
        ),
        check_vma=False,
    )
```

```python
import functools
import math

import jax
import jax.numpy as jnp
from jax import lax
from jax.experimental import pallas as pl
from jax.sharding import PartitionSpec as P

HD = 128
D = 4096
KS = 7
KM = 128


epsilon = 1e-06


def as_sent(shard):

    def short(part):
        return part.astype(jnp.bfloat16) if part.dtype == jnp.float32 else part

    return jax.tree.map(short, shard)


def passed_along(value, axis, steps):
    count = lax.axis_size(axis)
    leading, last = (max(0, -steps), min(count, count - steps))
    return lax.ppermute(value, axis, [(source, source + steps) for source in range(leading, last)])


def depthwise(padded, tap_rows):
    return lax.conv_general_dilated(
        padded[None],
        tap_rows[:, None, :],
        (1,),
        "VALID",
        dimension_numbers=("NWC", "WIO", "NWC"),
        feature_group_count=padded.shape[1],
        precision=lax.Precision.HIGHEST,
    )[0]


def neighbor_rows(edge_rows, offset):
    return passed_along(as_sent(edge_rows), "ctx", offset).astype(edge_rows.dtype)


def butterfly_total(value, axis, sent_type=None):
    count = lax.axis_size(axis)
    if count & (count - 1):
        if sent_type is None:
            return lax.psum(value, axis)
        return lax.psum(value.astype(sent_type), axis).astype(value.dtype)
    step = 1
    while step < count:
        pairs = [(source, source ^ step) for source in range(count)]
        if sent_type is None:
            value = value + lax.ppermute(value, axis, pairs)
        else:
            rounded = value.astype(sent_type)
            value = rounded.astype(value.dtype) + lax.ppermute(rounded, axis, pairs).astype(value.dtype)
        step *= 2
    return value


def channel_total(partial_value):
    return butterfly_total(partial_value, "tp")


def attention_block(scale_factor, q_ref, k_ref, v_ref, cot_ref, vis_ref, dk_ref, dv_ref, att_ref, dq_ref):
    contract_last = (((1,), (1,)), ((), ()))
    contract_first = (((0,), (0,)), ((), ()))
    query_head = q_ref[...]
    key_head = k_ref[...]
    value_head = v_ref[...]
    cotangent_head = cot_ref[...]
    scores = (
        lax.dot_general(query_head, key_head, contract_last, preferred_element_type=jnp.float32)
        * scale_factor
    )
    scores = jnp.where(vis_ref[...] > 0.5, scores, -jnp.inf)
    row_max = jnp.max(scores, axis=1, keepdims=True)
    logsum = row_max + jnp.log(jnp.sum(jnp.exp(scores - row_max), axis=1, keepdims=True))
    weights = jnp.exp(scores - logsum).astype(jnp.bfloat16)
    attended = jnp.dot(weights, value_head, preferred_element_type=jnp.float32)
    weight_grad = lax.dot_general(
        cotangent_head, value_head, contract_last, preferred_element_type=jnp.float32
    )
    row_delta = jnp.sum(cotangent_head.astype(jnp.float32) * attended, axis=1, keepdims=True)
    dscore = (scale_factor * weights.astype(jnp.float32) * (weight_grad - row_delta)).astype(
        jnp.bfloat16
    )
    att_ref[...] = attended
    dq_ref[...] = jnp.dot(dscore, key_head, preferred_element_type=jnp.float32).astype(jnp.bfloat16)
    dk_ref[...] = lax.dot_general(
        dscore, query_head, contract_first, preferred_element_type=jnp.float32
    ).astype(jnp.bfloat16)
    dv_ref[...] = lax.dot_general(
        weights, cotangent_head, contract_first, preferred_element_type=jnp.float32
    ).astype(jnp.bfloat16)


def head_attention(queries, keys_whole, values_whole, cotangent, visible, scale_factor):
    local_rows, width_local = queries.shape
    total_rows = keys_whole.shape[0]
    local_spec = pl.BlockSpec((local_rows, HD), lambda h: (0, h))
    whole_spec = pl.BlockSpec((total_rows, HD), lambda h: (0, h))
    mask_spec = pl.BlockSpec((local_rows, total_rows), lambda h: (0, 0))
    return pl.pallas_call(
        functools.partial(attention_block, scale_factor),
        grid=(width_local // HD,),
        in_specs=[local_spec, whole_spec, whole_spec, local_spec, mask_spec],
        out_specs=[whole_spec, whole_spec, local_spec, local_spec],
        out_shape=[
            jax.ShapeDtypeStruct((total_rows, width_local), jnp.bfloat16),
            jax.ShapeDtypeStruct((total_rows, width_local), jnp.bfloat16),
            jax.ShapeDtypeStruct((local_rows, width_local), jnp.float32),
            jax.ShapeDtypeStruct((local_rows, width_local), jnp.bfloat16),
        ],
    )(queries, keys_whole, values_whole, cotangent, visible)


def shards(
    stream,
    shutter,
    feeder,
    stencil,
    valves,
    intake,
    kernel,
    scaling,
    queries,
    matchers,
    segments,
    cotangent,
):
    local_rows = stream.shape[0]
    width_local = stream.shape[1]
    head_count = width_local // HD
    total_rows = local_rows * lax.axis_size("ctx")
    position = lax.axis_index("ctx") * local_rows
    scale_factor = 1.0 / math.sqrt(HD)
    widened = stream.astype(jnp.float32)
    inner_one = feeder.astype(jnp.float32) * widened
    rim_one = neighbor_rows(inner_one[local_rows - (KS - 1) :], 1)
    padded_one = jnp.concatenate([rim_one, inner_one], axis=0)
    conv_one = depthwise(padded_one, stencil[::-1])
    first_out = (widened + shutter.astype(jnp.float32) * conv_one).astype(jnp.bfloat16)
    first_wide = first_out.astype(jnp.float32)
    inner_two = intake.astype(jnp.float32) * first_wide
    rim_two = neighbor_rows(inner_two[local_rows - (KM - 1) :], 1)
    padded_two = jnp.concatenate([rim_two, inner_two], axis=0)
    conv_two = depthwise(padded_two, kernel[::-1])
    second_out = (first_wide + valves.astype(jnp.float32) * conv_two).astype(jnp.bfloat16)
    second_wide = second_out.astype(jnp.float32)
    squares = channel_total(jnp.sum(second_wide * second_wide, axis=1))
    inverse_rms = lax.rsqrt(squares / D + epsilon)
    normed = (second_wide * inverse_rms[:, None] * scaling).astype(jnp.bfloat16)
    keys_whole, values_whole = (
        lax.all_gather(matchers, "ctx", axis=0, tiled=True),
        lax.all_gather(normed, "ctx", axis=0, tiled=True),
    )
    query_pos = position + jnp.arange(local_rows, dtype=jnp.int32)
    key_pos = jnp.arange(total_rows, dtype=jnp.int32)
    query_seg = lax.dynamic_slice_in_dim(segments, position, local_rows, 0)
    visible = (key_pos[None, :] <= query_pos[:, None]) & (segments[None, :] == query_seg[:, None])
    key_part, value_part, attended_all, queries_grad = head_attention(
        queries, keys_whole, values_whole, cotangent, visible.astype(jnp.float32), scale_factor
    )
    result = (second_wide + attended_all).astype(jnp.bfloat16)
    value_grad = lax.psum_scatter(
        value_part,
        "ctx",
        scatter_dimension=0,
        tiled=True,
    ).astype(jnp.float32)
    key_part, value_grad = lax.optimization_barrier((key_part, value_grad))
    matchers_grad = lax.psum_scatter(
        key_part,
        "ctx",
        scatter_dimension=0,
        tiled=True,
    )
    gain_part = value_grad * scaling
    projected = channel_total(jnp.sum(gain_part * second_wide, axis=1))
    scaling_part = jnp.sum(value_grad * second_wide * inverse_rms[:, None], axis=0)
    second_grad = (
        cotangent.astype(jnp.float32)
        + inverse_rms[:, None] * gain_part
        - second_wide * (inverse_rms**3 * projected / D)[:, None]
    )
    valves_grad = (second_grad * conv_two).astype(jnp.bfloat16)
    dconv_two = second_grad * valves.astype(jnp.float32)
    back_two = neighbor_rows(dconv_two[: KM - 1], -1)
    dinner_two = depthwise(jnp.concatenate([dconv_two, back_two], axis=0), kernel)
    intake_grad = (dinner_two * first_wide).astype(jnp.bfloat16)
    kernel_part = depthwise(padded_two, dconv_two)[::-1]
    first_grad = second_grad + dinner_two * intake.astype(jnp.float32)
    shutter_grad = (first_grad * conv_one).astype(jnp.bfloat16)
    dconv_one = first_grad * shutter.astype(jnp.float32)
    back_one = neighbor_rows(dconv_one[: KS - 1], -1)
    dinner_one = depthwise(jnp.concatenate([dconv_one, back_one], axis=0), stencil)
    feeder_grad = (dinner_one * widened).astype(jnp.bfloat16)
    stencil_part = depthwise(padded_one, dconv_one)[::-1]
    stream_grad = (first_grad + dinner_one * feeder.astype(jnp.float32)).astype(jnp.bfloat16)
    filter_sum = butterfly_total(
        jnp.concatenate([kernel_part, scaling_part[None]], axis=0), "ctx", jnp.bfloat16
    )
    kernel_sum = filter_sum[:KM]
    scaling_sum = filter_sum[KM]
    stencil_sum = butterfly_total(stencil_part, "ctx", jnp.bfloat16)
    normalizer = math.sqrt(total_rows)
    return (
        result,
        stream_grad,
        shutter_grad,
        feeder_grad,
        stencil_sum / normalizer,
        valves_grad,
        intake_grad,
        kernel_sum / normalizer,
        scaling_sum / normalizer,
        queries_grad,
        matchers_grad,
    )


def solution(mesh):
    placed = (
        P("ctx", "tp"),
        P("ctx", "tp"),
        P("ctx", "tp"),
        P(None, "tp"),
        P("ctx", "tp"),
        P("ctx", "tp"),
        P(None, "tp"),
        P("tp"),
        P("ctx", "tp"),
        P("ctx", "tp"),
        P(),
        P("ctx", "tp"),
    )
    return jax.shard_map(
        shards,
        mesh=mesh,
        in_specs=placed,
        out_specs=(
            P("ctx", "tp"),
            P("ctx", "tp"),
            P("ctx", "tp"),
            P("ctx", "tp"),
            P(None, "tp"),
            P("ctx", "tp"),
            P("ctx", "tp"),
            P(None, "tp"),
            P("tp"),
            P("ctx", "tp"),
            P("ctx", "tp"),
        ),
        check_vma=False,
    )
```

```python
import functools
import math

import jax
import jax.numpy as jnp
from jax import lax
from jax.experimental import pallas as pl
from jax.sharding import PartitionSpec as P

HD = 128
D = 4096
KS = 7
KM = 128


epsilon = 1e-06


def as_sent(shard):

    def short(part):
        return part.astype(jnp.bfloat16) if part.dtype == jnp.float32 else part

    return jax.tree.map(short, shard)


def passed_along(value, axis, steps):
    count = lax.axis_size(axis)
    leading, last = (max(0, -steps), min(count, count - steps))
    return lax.ppermute(value, axis, [(source, source + steps) for source in range(leading, last)])


def depthwise(padded, tap_rows):
    return lax.conv_general_dilated(
        padded[None],
        tap_rows[:, None, :],
        (1,),
        "VALID",
        dimension_numbers=("NWC", "WIO", "NWC"),
        feature_group_count=padded.shape[1],
        precision=lax.Precision.HIGHEST,
    )[0]


def neighbor_rows(edge_rows, offset):
    return passed_along(as_sent(edge_rows), "ctx", offset).astype(edge_rows.dtype)


def butterfly_total(value, axis, sent_type=None):
    count = lax.axis_size(axis)
    if count & (count - 1):
        if sent_type is None:
            return lax.psum(value, axis)
        return lax.psum(value.astype(sent_type), axis).astype(value.dtype)
    step = 1
    while step < count:
        pairs = [(source, source ^ step) for source in range(count)]
        if sent_type is None:
            value = value + lax.ppermute(value, axis, pairs)
        else:
            rounded = value.astype(sent_type)
            value = rounded.astype(value.dtype) + lax.ppermute(rounded, axis, pairs).astype(value.dtype)
        step *= 2
    return value


def channel_total(partial_value):
    return butterfly_total(partial_value, "tp")


def attention_block(scale_factor, q_ref, k_ref, v_ref, cot_ref, vis_ref, dk_ref, dv_ref, att_ref, dq_ref):
    contract_last = (((1,), (1,)), ((), ()))
    contract_first = (((0,), (0,)), ((), ()))
    query_head = q_ref[...]
    key_head = k_ref[...]
    value_head = v_ref[...]
    cotangent_head = cot_ref[...]
    scores = (
        lax.dot_general(query_head, key_head, contract_last, preferred_element_type=jnp.float32)
        * scale_factor
    )
    scores = jnp.where(vis_ref[...] > 0.5, scores, -jnp.inf)
    row_max = jnp.max(scores, axis=1, keepdims=True)
    logsum = row_max + jnp.log(jnp.sum(jnp.exp(scores - row_max), axis=1, keepdims=True))
    weights = jnp.exp(scores - logsum).astype(jnp.bfloat16)
    attended = jnp.dot(weights, value_head, preferred_element_type=jnp.float32)
    weight_grad = lax.dot_general(
        cotangent_head, value_head, contract_last, preferred_element_type=jnp.float32
    )
    row_delta = jnp.sum(cotangent_head.astype(jnp.float32) * attended, axis=1, keepdims=True)
    dscore = (scale_factor * weights.astype(jnp.float32) * (weight_grad - row_delta)).astype(
        jnp.bfloat16
    )
    att_ref[...] = attended
    dq_ref[...] = jnp.dot(dscore, key_head, preferred_element_type=jnp.float32).astype(jnp.bfloat16)
    dk_ref[...] = lax.dot_general(
        dscore, query_head, contract_first, preferred_element_type=jnp.float32
    ).astype(jnp.bfloat16)
    dv_ref[...] = lax.dot_general(
        weights, cotangent_head, contract_first, preferred_element_type=jnp.float32
    ).astype(jnp.bfloat16)


def head_attention(queries, keys_whole, values_whole, cotangent, visible, scale_factor):
    local_rows, width_local = queries.shape
    total_rows = keys_whole.shape[0]
    local_spec = pl.BlockSpec((local_rows, HD), lambda h: (0, h))
    whole_spec = pl.BlockSpec((total_rows, HD), lambda h: (0, h))
    mask_spec = pl.BlockSpec((local_rows, total_rows), lambda h: (0, 0))
    return pl.pallas_call(
        functools.partial(attention_block, scale_factor),
        grid=(width_local // HD,),
        in_specs=[local_spec, whole_spec, whole_spec, local_spec, mask_spec],
        out_specs=[whole_spec, whole_spec, local_spec, local_spec],
        out_shape=[
            jax.ShapeDtypeStruct((total_rows, width_local), jnp.bfloat16),
            jax.ShapeDtypeStruct((total_rows, width_local), jnp.bfloat16),
            jax.ShapeDtypeStruct((local_rows, width_local), jnp.float32),
            jax.ShapeDtypeStruct((local_rows, width_local), jnp.bfloat16),
        ],
    )(queries, keys_whole, values_whole, cotangent, visible)


def shards(
    stream,
    shutter,
    feeder,
    stencil,
    valves,
    intake,
    kernel,
    scaling,
    queries,
    matchers,
    segments,
    cotangent,
):
    local_rows = stream.shape[0]
    width_local = stream.shape[1]
    head_count = width_local // HD
    total_rows = local_rows * lax.axis_size("ctx")
    position = lax.axis_index("ctx") * local_rows
    scale_factor = 1.0 / math.sqrt(HD)
    widened = stream.astype(jnp.float32)
    inner_one = feeder.astype(jnp.float32) * widened
    rim_one = neighbor_rows(inner_one[local_rows - (KS - 1) :], 1)
    padded_one = jnp.concatenate([rim_one, inner_one], axis=0)
    conv_one = depthwise(padded_one, stencil[::-1])
    first_out = (widened + shutter.astype(jnp.float32) * conv_one).astype(jnp.bfloat16)
    first_wide = first_out.astype(jnp.float32)
    inner_two = intake.astype(jnp.float32) * first_wide
    rim_two = neighbor_rows(inner_two[local_rows - (KM - 1) :], 1)
    padded_two = jnp.concatenate([rim_two, inner_two], axis=0)
    conv_two = depthwise(padded_two, kernel[::-1])
    second_out = (first_wide + valves.astype(jnp.float32) * conv_two).astype(jnp.bfloat16)
    second_wide = second_out.astype(jnp.float32)
    squares = channel_total(jnp.sum(second_wide * second_wide, axis=1))
    inverse_rms = lax.rsqrt(squares / D + epsilon)
    normed = (second_wide * inverse_rms[:, None] * scaling).astype(jnp.bfloat16)
    ctx_count = lax.axis_size("ctx")
    ctx_index = lax.axis_index("ctx")
    keys_whole = lax.all_gather(matchers, "ctx", axis=0, tiled=True)
    reach = min(ctx_count - 1, (3 * total_rows // 4 - 1 + local_rows - 1) // local_rows)
    values_whole = lax.dynamic_update_slice_in_dim(
        jnp.zeros((total_rows, width_local), jnp.bfloat16), normed, position, 0
    )
    for distance in range(1, reach + 1):
        arrived = passed_along(normed, "ctx", distance)
        block_start = ((ctx_index - distance) % ctx_count) * local_rows
        values_whole = lax.dynamic_update_slice_in_dim(values_whole, arrived, block_start, 0)
    query_pos = position + jnp.arange(local_rows, dtype=jnp.int32)
    key_pos = jnp.arange(total_rows, dtype=jnp.int32)
    query_seg = lax.dynamic_slice_in_dim(segments, position, local_rows, 0)
    visible = (key_pos[None, :] <= query_pos[:, None]) & (segments[None, :] == query_seg[:, None])
    key_part, value_part, attended_all, queries_grad = head_attention(
        queries, keys_whole, values_whole, cotangent, visible.astype(jnp.float32), scale_factor
    )
    result = (second_wide + attended_all).astype(jnp.bfloat16)
    value_grad = lax.dynamic_slice_in_dim(value_part, position, local_rows, 0).astype(jnp.float32)
    for distance in range(1, reach + 1):
        block_start = ((ctx_index - distance) % ctx_count) * local_rows
        leaving = lax.dynamic_slice_in_dim(value_part, block_start, local_rows, 0)
        value_grad = value_grad + passed_along(leaving, "ctx", -distance).astype(jnp.float32)
    key_part, value_grad = lax.optimization_barrier((key_part, value_grad))
    matchers_grad = lax.psum_scatter(
        key_part,
        "ctx",
        scatter_dimension=0,
        tiled=True,
    )
    gain_part = value_grad * scaling
    projected = channel_total(jnp.sum(gain_part * second_wide, axis=1))
    scaling_part = jnp.sum(value_grad * second_wide * inverse_rms[:, None], axis=0)
    second_grad = (
        cotangent.astype(jnp.float32)
        + inverse_rms[:, None] * gain_part
        - second_wide * (inverse_rms**3 * projected / D)[:, None]
    )
    valves_grad = (second_grad * conv_two).astype(jnp.bfloat16)
    dconv_two = second_grad * valves.astype(jnp.float32)
    back_two = neighbor_rows(dconv_two[: KM - 1], -1)
    dinner_two = depthwise(jnp.concatenate([dconv_two, back_two], axis=0), kernel)
    intake_grad = (dinner_two * first_wide).astype(jnp.bfloat16)
    kernel_part = depthwise(padded_two, dconv_two)[::-1]
    first_grad = second_grad + dinner_two * intake.astype(jnp.float32)
    shutter_grad = (first_grad * conv_one).astype(jnp.bfloat16)
    dconv_one = first_grad * shutter.astype(jnp.float32)
    back_one = neighbor_rows(dconv_one[: KS - 1], -1)
    dinner_one = depthwise(jnp.concatenate([dconv_one, back_one], axis=0), stencil)
    feeder_grad = (dinner_one * widened).astype(jnp.bfloat16)
    stencil_part = depthwise(padded_one, dconv_one)[::-1]
    stream_grad = (first_grad + dinner_one * feeder.astype(jnp.float32)).astype(jnp.bfloat16)
    filter_sum = butterfly_total(
        jnp.concatenate([kernel_part, scaling_part[None]], axis=0), "ctx", jnp.bfloat16
    )
    kernel_sum = filter_sum[:KM]
    scaling_sum = filter_sum[KM]
    stencil_sum = butterfly_total(stencil_part, "ctx", jnp.bfloat16)
    normalizer = math.sqrt(total_rows)
    return (
        result,
        stream_grad,
        shutter_grad,
        feeder_grad,
        stencil_sum / normalizer,
        valves_grad,
        intake_grad,
        kernel_sum / normalizer,
        scaling_sum / normalizer,
        queries_grad,
        matchers_grad,
    )


def solution(mesh):
    placed = (
        P("ctx", "tp"),
        P("ctx", "tp"),
        P("ctx", "tp"),
        P(None, "tp"),
        P("ctx", "tp"),
        P("ctx", "tp"),
        P(None, "tp"),
        P("tp"),
        P("ctx", "tp"),
        P("ctx", "tp"),
        P(),
        P("ctx", "tp"),
    )
    return jax.shard_map(
        shards,
        mesh=mesh,
        in_specs=placed,
        out_specs=(
            P("ctx", "tp"),
            P("ctx", "tp"),
            P("ctx", "tp"),
            P("ctx", "tp"),
            P(None, "tp"),
            P("ctx", "tp"),
            P("ctx", "tp"),
            P(None, "tp"),
            P("tp"),
            P("ctx", "tp"),
            P("ctx", "tp"),
        ),
        check_vma=False,
    )
```

```python
import functools
import math

import jax
import jax.numpy as jnp
from jax import lax
from jax.experimental import pallas as pl
from jax.sharding import PartitionSpec as P

HD = 128
D = 4096
KS = 7
KM = 128


epsilon = 1e-06


def as_sent(shard):

    def short(part):
        return part.astype(jnp.bfloat16) if part.dtype == jnp.float32 else part

    return jax.tree.map(short, shard)


def passed_along(value, axis, steps):
    count = lax.axis_size(axis)
    leading, last = (max(0, -steps), min(count, count - steps))
    return lax.ppermute(value, axis, [(source, source + steps) for source in range(leading, last)])


def depthwise(padded, tap_rows):
    return lax.conv_general_dilated(
        padded[None],
        tap_rows[:, None, :],
        (1,),
        "VALID",
        dimension_numbers=("NWC", "WIO", "NWC"),
        feature_group_count=padded.shape[1],
        precision=lax.Precision.HIGHEST,
    )[0]


def neighbor_rows(edge_rows, offset):
    return passed_along(as_sent(edge_rows), "ctx", offset).astype(edge_rows.dtype)


def butterfly_total(value, axis, sent_type=None):
    count = lax.axis_size(axis)
    if count & (count - 1):
        if sent_type is None:
            return lax.psum(value, axis)
        return lax.psum(value.astype(sent_type), axis).astype(value.dtype)
    step = 1
    while step < count:
        pairs = [(source, source ^ step) for source in range(count)]
        if sent_type is None:
            value = value + lax.ppermute(value, axis, pairs)
        else:
            rounded = value.astype(sent_type)
            value = rounded.astype(value.dtype) + lax.ppermute(rounded, axis, pairs).astype(value.dtype)
        step *= 2
    return value


def channel_total(partial_value):
    return butterfly_total(partial_value, "tp")


def head_weights(scale_factor, query_head, key_head, visible):
    contract_last = (((1,), (1,)), ((), ()))
    scores = (
        lax.dot_general(query_head, key_head, contract_last, preferred_element_type=jnp.float32)
        * scale_factor
    )
    scores = jnp.where(visible > 0.5, scores, -jnp.inf)
    row_max = jnp.max(scores, axis=1, keepdims=True)
    logsum = row_max + jnp.log(jnp.sum(jnp.exp(scores - row_max), axis=1, keepdims=True))
    return jnp.exp(scores - logsum).astype(jnp.bfloat16)


def value_block(scale_factor, q_ref, k_ref, cot_ref, vis_ref, dv_ref):
    contract_first = (((0,), (0,)), ((), ()))
    weights = head_weights(scale_factor, q_ref[...], k_ref[...], vis_ref[...])
    dv_ref[...] = lax.dot_general(
        weights, cot_ref[...], contract_first, preferred_element_type=jnp.float32
    ).astype(jnp.bfloat16)


def attention_block(scale_factor, q_ref, k_ref, v_ref, cot_ref, vis_ref, dk_ref, att_ref, dq_ref):
    contract_last = (((1,), (1,)), ((), ()))
    contract_first = (((0,), (0,)), ((), ()))
    query_head = q_ref[...]
    key_head = k_ref[...]
    value_head = v_ref[...]
    cotangent_head = cot_ref[...]
    weights = head_weights(scale_factor, query_head, key_head, vis_ref[...])
    attended = jnp.dot(weights, value_head, preferred_element_type=jnp.float32)
    weight_grad = lax.dot_general(
        cotangent_head, value_head, contract_last, preferred_element_type=jnp.float32
    )
    row_delta = jnp.sum(cotangent_head.astype(jnp.float32) * attended, axis=1, keepdims=True)
    dscore = (scale_factor * weights.astype(jnp.float32) * (weight_grad - row_delta)).astype(
        jnp.bfloat16
    )
    att_ref[...] = attended
    dq_ref[...] = jnp.dot(dscore, key_head, preferred_element_type=jnp.float32).astype(jnp.bfloat16)
    dk_ref[...] = lax.dot_general(
        dscore, query_head, contract_first, preferred_element_type=jnp.float32
    ).astype(jnp.bfloat16)


def head_specs(local_rows, total_rows):
    local_spec = pl.BlockSpec((local_rows, HD), lambda h: (0, h))
    whole_spec = pl.BlockSpec((total_rows, HD), lambda h: (0, h))
    mask_spec = pl.BlockSpec((local_rows, total_rows), lambda h: (0, 0))
    return local_spec, whole_spec, mask_spec


def head_values_grad(queries, keys_whole, cotangent, visible, scale_factor):
    local_rows, width_local = queries.shape
    total_rows = keys_whole.shape[0]
    local_spec, whole_spec, mask_spec = head_specs(local_rows, total_rows)
    return pl.pallas_call(
        functools.partial(value_block, scale_factor),
        grid=(width_local // HD,),
        in_specs=[local_spec, whole_spec, local_spec, mask_spec],
        out_specs=whole_spec,
        out_shape=jax.ShapeDtypeStruct((total_rows, width_local), jnp.bfloat16),
    )(queries, keys_whole, cotangent, visible)


def head_attention(queries, keys_whole, values_whole, cotangent, visible, scale_factor):
    local_rows, width_local = queries.shape
    total_rows = keys_whole.shape[0]
    local_spec, whole_spec, mask_spec = head_specs(local_rows, total_rows)
    return pl.pallas_call(
        functools.partial(attention_block, scale_factor),
        grid=(width_local // HD,),
        in_specs=[local_spec, whole_spec, whole_spec, local_spec, mask_spec],
        out_specs=[whole_spec, local_spec, local_spec],
        out_shape=[
            jax.ShapeDtypeStruct((total_rows, width_local), jnp.bfloat16),
            jax.ShapeDtypeStruct((local_rows, width_local), jnp.float32),
            jax.ShapeDtypeStruct((local_rows, width_local), jnp.bfloat16),
        ],
    )(queries, keys_whole, values_whole, cotangent, visible)


def shards(
    stream,
    shutter,
    feeder,
    stencil,
    valves,
    intake,
    kernel,
    scaling,
    queries,
    matchers,
    segments,
    cotangent,
):
    local_rows = stream.shape[0]
    width_local = stream.shape[1]
    head_count = width_local // HD
    total_rows = local_rows * lax.axis_size("ctx")
    position = lax.axis_index("ctx") * local_rows
    scale_factor = 1.0 / math.sqrt(HD)
    widened = stream.astype(jnp.float32)
    inner_one = feeder.astype(jnp.float32) * widened
    rim_one = neighbor_rows(inner_one[local_rows - (KS - 1) :], 1)
    padded_one = jnp.concatenate([rim_one, inner_one], axis=0)
    conv_one = depthwise(padded_one, stencil[::-1])
    first_out = (widened + shutter.astype(jnp.float32) * conv_one).astype(jnp.bfloat16)
    first_wide = first_out.astype(jnp.float32)
    inner_two = intake.astype(jnp.float32) * first_wide
    rim_two = neighbor_rows(inner_two[local_rows - (KM - 1) :], 1)
    padded_two = jnp.concatenate([rim_two, inner_two], axis=0)
    conv_two = depthwise(padded_two, kernel[::-1])
    second_out = (first_wide + valves.astype(jnp.float32) * conv_two).astype(jnp.bfloat16)
    second_wide = second_out.astype(jnp.float32)
    squares = channel_total(jnp.sum(second_wide * second_wide, axis=1))
    inverse_rms = lax.rsqrt(squares / D + epsilon)
    normed = (second_wide * inverse_rms[:, None] * scaling).astype(jnp.bfloat16)
    ctx_count = lax.axis_size("ctx")
    ctx_index = lax.axis_index("ctx")
    keys_whole = lax.all_gather(matchers, "ctx", axis=0, tiled=True)
    reach = min(ctx_count - 1, (3 * total_rows // 4 - 1 + local_rows - 1) // local_rows)
    values_whole = lax.dynamic_update_slice_in_dim(
        jnp.zeros((total_rows, width_local), jnp.bfloat16), normed, position, 0
    )
    for distance in range(1, reach + 1):
        arrived = passed_along(normed, "ctx", distance)
        block_start = ((ctx_index - distance) % ctx_count) * local_rows
        values_whole = lax.dynamic_update_slice_in_dim(values_whole, arrived, block_start, 0)
    query_pos = position + jnp.arange(local_rows, dtype=jnp.int32)
    key_pos = jnp.arange(total_rows, dtype=jnp.int32)
    query_seg = lax.dynamic_slice_in_dim(segments, position, local_rows, 0)
    visible = (key_pos[None, :] <= query_pos[:, None]) & (segments[None, :] == query_seg[:, None])
    mask = visible.astype(jnp.float32)
    value_part = head_values_grad(queries, keys_whole, cotangent, mask, scale_factor)
    key_part, attended_all, queries_grad = head_attention(
        queries, keys_whole, values_whole, cotangent, mask, scale_factor
    )
    result = (second_wide + attended_all).astype(jnp.bfloat16)
    value_grad = lax.dynamic_slice_in_dim(value_part, position, local_rows, 0).astype(jnp.float32)
    for distance in range(1, reach + 1):
        block_start = ((ctx_index - distance) % ctx_count) * local_rows
        leaving = lax.dynamic_slice_in_dim(value_part, block_start, local_rows, 0)
        value_grad = value_grad + passed_along(leaving, "ctx", -distance).astype(jnp.float32)
    key_part, value_grad = lax.optimization_barrier((key_part, value_grad))
    matchers_grad = lax.psum_scatter(
        key_part,
        "ctx",
        scatter_dimension=0,
        tiled=True,
    )
    gain_part = value_grad * scaling
    projected = channel_total(jnp.sum(gain_part * second_wide, axis=1))
    scaling_part = jnp.sum(value_grad * second_wide * inverse_rms[:, None], axis=0)
    second_grad = (
        cotangent.astype(jnp.float32)
        + inverse_rms[:, None] * gain_part
        - second_wide * (inverse_rms**3 * projected / D)[:, None]
    )
    valves_grad = (second_grad * conv_two).astype(jnp.bfloat16)
    dconv_two = second_grad * valves.astype(jnp.float32)
    back_two = neighbor_rows(dconv_two[: KM - 1], -1)
    dinner_two = depthwise(jnp.concatenate([dconv_two, back_two], axis=0), kernel)
    intake_grad = (dinner_two * first_wide).astype(jnp.bfloat16)
    kernel_part = depthwise(padded_two, dconv_two)[::-1]
    first_grad = second_grad + dinner_two * intake.astype(jnp.float32)
    shutter_grad = (first_grad * conv_one).astype(jnp.bfloat16)
    dconv_one = first_grad * shutter.astype(jnp.float32)
    back_one = neighbor_rows(dconv_one[: KS - 1], -1)
    dinner_one = depthwise(jnp.concatenate([dconv_one, back_one], axis=0), stencil)
    feeder_grad = (dinner_one * widened).astype(jnp.bfloat16)
    stencil_part = depthwise(padded_one, dconv_one)[::-1]
    stream_grad = (first_grad + dinner_one * feeder.astype(jnp.float32)).astype(jnp.bfloat16)
    filter_sum = butterfly_total(
        jnp.concatenate([kernel_part, scaling_part[None]], axis=0), "ctx", jnp.bfloat16
    )
    kernel_sum = filter_sum[:KM]
    scaling_sum = filter_sum[KM]
    stencil_sum = butterfly_total(stencil_part, "ctx", jnp.bfloat16)
    normalizer = math.sqrt(total_rows)
    return (
        result,
        stream_grad,
        shutter_grad,
        feeder_grad,
        stencil_sum / normalizer,
        valves_grad,
        intake_grad,
        kernel_sum / normalizer,
        scaling_sum / normalizer,
        queries_grad,
        matchers_grad,
    )


def solution(mesh):
    placed = (
        P("ctx", "tp"),
        P("ctx", "tp"),
        P("ctx", "tp"),
        P(None, "tp"),
        P("ctx", "tp"),
        P("ctx", "tp"),
        P(None, "tp"),
        P("tp"),
        P("ctx", "tp"),
        P("ctx", "tp"),
        P(),
        P("ctx", "tp"),
    )
    return jax.shard_map(
        shards,
        mesh=mesh,
        in_specs=placed,
        out_specs=(
            P("ctx", "tp"),
            P("ctx", "tp"),
            P("ctx", "tp"),
            P("ctx", "tp"),
            P(None, "tp"),
            P("ctx", "tp"),
            P("ctx", "tp"),
            P(None, "tp"),
            P("tp"),
            P("ctx", "tp"),
            P("ctx", "tp"),
        ),
        check_vma=False,
    )
```

```python
import functools
import math

import jax
import jax.numpy as jnp
from jax import lax
from jax.experimental import pallas as pl
from jax.sharding import PartitionSpec as P

HD = 128
D = 4096
KS = 7
KM = 128


epsilon = 1e-06


def as_sent(shard):

    def short(part):
        return part.astype(jnp.bfloat16) if part.dtype == jnp.float32 else part

    return jax.tree.map(short, shard)


def passed_along(value, axis, steps):
    count = lax.axis_size(axis)
    leading, last = (max(0, -steps), min(count, count - steps))
    return lax.ppermute(value, axis, [(source, source + steps) for source in range(leading, last)])


def depthwise(padded, tap_rows):
    return lax.conv_general_dilated(
        padded[None],
        tap_rows[:, None, :],
        (1,),
        "VALID",
        dimension_numbers=("NWC", "WIO", "NWC"),
        feature_group_count=padded.shape[1],
        precision=lax.Precision.HIGHEST,
    )[0]


def neighbor_rows(edge_rows, offset):
    return passed_along(as_sent(edge_rows), "ctx", offset).astype(edge_rows.dtype)


def butterfly_total(value, axis, sent_type=None):
    count = lax.axis_size(axis)
    if count & (count - 1):
        if sent_type is None:
            return lax.psum(value, axis)
        return lax.psum(value.astype(sent_type), axis).astype(value.dtype)
    step = 1
    while step < count:
        pairs = [(source, source ^ step) for source in range(count)]
        if sent_type is None:
            value = value + lax.ppermute(value, axis, pairs)
        else:
            rounded = value.astype(sent_type)
            value = rounded.astype(value.dtype) + lax.ppermute(rounded, axis, pairs).astype(value.dtype)
        step *= 2
    return value


def channel_total(partial_value):
    return butterfly_total(partial_value, "tp")


def head_weights(scale_factor, query_head, key_head, visible):
    contract_last = (((1,), (1,)), ((), ()))
    scores = (
        lax.dot_general(query_head, key_head, contract_last, preferred_element_type=jnp.float32)
        * scale_factor
    )
    scores = jnp.where(visible > 0.5, scores, -jnp.inf)
    row_max = jnp.max(scores, axis=1, keepdims=True)
    logsum = row_max + jnp.log(jnp.sum(jnp.exp(scores - row_max), axis=1, keepdims=True))
    return jnp.exp(scores - logsum).astype(jnp.bfloat16)


def value_block(scale_factor, q_ref, k_ref, cot_ref, vis_ref, dv_ref):
    contract_first = (((0,), (0,)), ((), ()))
    weights = head_weights(scale_factor, q_ref[...], k_ref[...], vis_ref[...])
    dv_ref[...] = lax.dot_general(
        weights, cot_ref[...], contract_first, preferred_element_type=jnp.float32
    ).astype(jnp.bfloat16)


def attention_block(scale_factor, q_ref, k_ref, v_ref, cot_ref, vis_ref, dk_ref, att_ref, dq_ref):
    contract_last = (((1,), (1,)), ((), ()))
    contract_first = (((0,), (0,)), ((), ()))
    query_head = q_ref[...]
    key_head = k_ref[...]
    value_head = v_ref[...]
    cotangent_head = cot_ref[...]
    weights = head_weights(scale_factor, query_head, key_head, vis_ref[...])
    attended = jnp.dot(weights, value_head, preferred_element_type=jnp.float32)
    weight_grad = lax.dot_general(
        cotangent_head, value_head, contract_last, preferred_element_type=jnp.float32
    )
    row_delta = jnp.sum(cotangent_head.astype(jnp.float32) * attended, axis=1, keepdims=True)
    dscore = (scale_factor * weights.astype(jnp.float32) * (weight_grad - row_delta)).astype(
        jnp.bfloat16
    )
    att_ref[...] = attended
    dq_ref[...] = jnp.dot(dscore, key_head, preferred_element_type=jnp.float32).astype(jnp.bfloat16)
    dk_ref[...] = lax.dot_general(
        dscore, query_head, contract_first, preferred_element_type=jnp.float32
    ).astype(jnp.bfloat16)


def head_specs(local_rows, total_rows):
    local_spec = pl.BlockSpec((local_rows, HD), lambda h: (0, h))
    whole_spec = pl.BlockSpec((total_rows, HD), lambda h: (0, h))
    mask_spec = pl.BlockSpec((local_rows, total_rows), lambda h: (0, 0))
    return local_spec, whole_spec, mask_spec


def head_values_grad(queries, keys_whole, cotangent, visible, scale_factor):
    local_rows, width_local = queries.shape
    total_rows = keys_whole.shape[0]
    local_spec, whole_spec, mask_spec = head_specs(local_rows, total_rows)
    return pl.pallas_call(
        functools.partial(value_block, scale_factor),
        grid=(width_local // HD,),
        in_specs=[local_spec, whole_spec, local_spec, mask_spec],
        out_specs=whole_spec,
        out_shape=jax.ShapeDtypeStruct((total_rows, width_local), jnp.bfloat16),
    )(queries, keys_whole, cotangent, visible)


def head_attention(queries, keys_whole, values_whole, cotangent, visible, scale_factor):
    local_rows, width_local = queries.shape
    total_rows = keys_whole.shape[0]
    local_spec, whole_spec, mask_spec = head_specs(local_rows, total_rows)
    return pl.pallas_call(
        functools.partial(attention_block, scale_factor),
        grid=(width_local // HD,),
        in_specs=[local_spec, whole_spec, whole_spec, local_spec, mask_spec],
        out_specs=[whole_spec, local_spec, local_spec],
        out_shape=[
            jax.ShapeDtypeStruct((total_rows, width_local), jnp.bfloat16),
            jax.ShapeDtypeStruct((local_rows, width_local), jnp.float32),
            jax.ShapeDtypeStruct((local_rows, width_local), jnp.bfloat16),
        ],
    )(queries, keys_whole, values_whole, cotangent, visible)


def shards(
    stream,
    shutter,
    feeder,
    stencil,
    valves,
    intake,
    kernel,
    scaling,
    queries,
    matchers,
    segments,
    cotangent,
):
    local_rows = stream.shape[0]
    width_local = stream.shape[1]
    head_count = width_local // HD
    total_rows = local_rows * lax.axis_size("ctx")
    position = lax.axis_index("ctx") * local_rows
    scale_factor = 1.0 / math.sqrt(HD)
    widened = stream.astype(jnp.float32)
    inner_one = feeder.astype(jnp.float32) * widened
    rim_one = neighbor_rows(inner_one[local_rows - (KS - 1) :], 1)
    padded_one = jnp.concatenate([rim_one, inner_one], axis=0)
    conv_one = depthwise(padded_one, stencil[::-1])
    first_out = (widened + shutter.astype(jnp.float32) * conv_one).astype(jnp.bfloat16)
    first_wide = first_out.astype(jnp.float32)
    inner_two = intake.astype(jnp.float32) * first_wide
    rim_two = neighbor_rows(inner_two[local_rows - (KM - 1) :], 1)
    padded_two = jnp.concatenate([rim_two, inner_two], axis=0)
    conv_two = depthwise(padded_two, kernel[::-1])
    second_out = (first_wide + valves.astype(jnp.float32) * conv_two).astype(jnp.bfloat16)
    second_wide = second_out.astype(jnp.float32)
    squares = channel_total(jnp.sum(second_wide * second_wide, axis=1))
    inverse_rms = lax.rsqrt(squares / D + epsilon)
    normed = (second_wide * inverse_rms[:, None] * scaling).astype(jnp.bfloat16)
    ctx_count = lax.axis_size("ctx")
    ctx_index = lax.axis_index("ctx")
    keys_whole = lax.all_gather(matchers, "ctx", axis=0, tiled=True)
    reach = min(ctx_count - 1, (3 * total_rows // 4 - 1 + local_rows - 1) // local_rows)
    query_pos = position + jnp.arange(local_rows, dtype=jnp.int32)
    key_pos = jnp.arange(total_rows, dtype=jnp.int32)
    query_seg = lax.dynamic_slice_in_dim(segments, position, local_rows, 0)
    visible = (key_pos[None, :] <= query_pos[:, None]) & (segments[None, :] == query_seg[:, None])
    mask = visible.astype(jnp.float32)
    value_part = head_values_grad(queries, keys_whole, cotangent, mask, scale_factor)
    value_grad = lax.dynamic_slice_in_dim(value_part, position, local_rows, 0).astype(jnp.float32)
    for distance in range(1, reach + 1):
        block_start = ((ctx_index - distance) % ctx_count) * local_rows
        leaving = lax.dynamic_slice_in_dim(value_part, block_start, local_rows, 0)
        value_grad = value_grad + passed_along(leaving, "ctx", -distance).astype(jnp.float32)
    values_whole = lax.all_gather(normed, "ctx", axis=0, tiled=True)
    key_part, attended_all, queries_grad = head_attention(
        queries, keys_whole, values_whole, cotangent, mask, scale_factor
    )
    result = (second_wide + attended_all).astype(jnp.bfloat16)
    key_part, value_grad = lax.optimization_barrier((key_part, value_grad))
    matchers_grad = lax.psum_scatter(
        key_part,
        "ctx",
        scatter_dimension=0,
        tiled=True,
    )
    gain_part = value_grad * scaling
    projected = channel_total(jnp.sum(gain_part * second_wide, axis=1))
    scaling_part = jnp.sum(value_grad * second_wide * inverse_rms[:, None], axis=0)
    second_grad = (
        cotangent.astype(jnp.float32)
        + inverse_rms[:, None] * gain_part
        - second_wide * (inverse_rms**3 * projected / D)[:, None]
    )
    valves_grad = (second_grad * conv_two).astype(jnp.bfloat16)
    dconv_two = second_grad * valves.astype(jnp.float32)
    back_two = neighbor_rows(dconv_two[: KM - 1], -1)
    dinner_two = depthwise(jnp.concatenate([dconv_two, back_two], axis=0), kernel)
    intake_grad = (dinner_two * first_wide).astype(jnp.bfloat16)
    kernel_part = depthwise(padded_two, dconv_two)[::-1]
    first_grad = second_grad + dinner_two * intake.astype(jnp.float32)
    shutter_grad = (first_grad * conv_one).astype(jnp.bfloat16)
    dconv_one = first_grad * shutter.astype(jnp.float32)
    back_one = neighbor_rows(dconv_one[: KS - 1], -1)
    dinner_one = depthwise(jnp.concatenate([dconv_one, back_one], axis=0), stencil)
    feeder_grad = (dinner_one * widened).astype(jnp.bfloat16)
    stencil_part = depthwise(padded_one, dconv_one)[::-1]
    stream_grad = (first_grad + dinner_one * feeder.astype(jnp.float32)).astype(jnp.bfloat16)
    filter_sum = butterfly_total(
        jnp.concatenate([kernel_part, scaling_part[None]], axis=0), "ctx", jnp.bfloat16
    )
    kernel_sum = filter_sum[:KM]
    scaling_sum = filter_sum[KM]
    stencil_sum = butterfly_total(stencil_part, "ctx", jnp.bfloat16)
    normalizer = math.sqrt(total_rows)
    return (
        result,
        stream_grad,
        shutter_grad,
        feeder_grad,
        stencil_sum / normalizer,
        valves_grad,
        intake_grad,
        kernel_sum / normalizer,
        scaling_sum / normalizer,
        queries_grad,
        matchers_grad,
    )


def solution(mesh):
    placed = (
        P("ctx", "tp"),
        P("ctx", "tp"),
        P("ctx", "tp"),
        P(None, "tp"),
        P("ctx", "tp"),
        P("ctx", "tp"),
        P(None, "tp"),
        P("tp"),
        P("ctx", "tp"),
        P("ctx", "tp"),
        P(),
        P("ctx", "tp"),
    )
    return jax.shard_map(
        shards,
        mesh=mesh,
        in_specs=placed,
        out_specs=(
            P("ctx", "tp"),
            P("ctx", "tp"),
            P("ctx", "tp"),
            P("ctx", "tp"),
            P(None, "tp"),
            P("ctx", "tp"),
            P("ctx", "tp"),
            P(None, "tp"),
            P("tp"),
            P("ctx", "tp"),
            P("ctx", "tp"),
        ),
        check_vma=False,
    )
```

```python
import functools
import math

import jax
import jax.numpy as jnp
from jax import lax
from jax.experimental import pallas as pl
from jax.sharding import PartitionSpec as P

HD = 128
D = 4096
KS = 7
KM = 128


epsilon = 1e-06


def as_sent(shard):

    def short(part):
        return part.astype(jnp.bfloat16) if part.dtype == jnp.float32 else part

    return jax.tree.map(short, shard)


def passed_along(value, axis, steps):
    count = lax.axis_size(axis)
    leading, last = (max(0, -steps), min(count, count - steps))
    return lax.ppermute(value, axis, [(source, source + steps) for source in range(leading, last)])


def depthwise(padded, tap_rows):
    return lax.conv_general_dilated(
        padded[None],
        tap_rows[:, None, :],
        (1,),
        "VALID",
        dimension_numbers=("NWC", "WIO", "NWC"),
        feature_group_count=padded.shape[1],
        precision=lax.Precision.HIGHEST,
    )[0]


def neighbor_rows(edge_rows, offset):
    return passed_along(as_sent(edge_rows), "ctx", offset).astype(edge_rows.dtype)


def butterfly_total(value, axis, sent_type=None):
    count = lax.axis_size(axis)
    if count & (count - 1):
        if sent_type is None:
            return lax.psum(value, axis)
        return lax.psum(value.astype(sent_type), axis).astype(value.dtype)
    step = 1
    while step < count:
        pairs = [(source, source ^ step) for source in range(count)]
        if sent_type is None:
            value = value + lax.ppermute(value, axis, pairs)
        else:
            rounded = value.astype(sent_type)
            value = rounded.astype(value.dtype) + lax.ppermute(rounded, axis, pairs).astype(value.dtype)
        step *= 2
    return value


def exchange_total(value, axis):
    count = lax.axis_size(axis)
    index = lax.axis_index(axis)
    stacked = jnp.zeros((count,) + value.shape, value.dtype)
    stacked = lax.dynamic_update_index_in_dim(stacked, value, index, 0)
    for shift in range(1, count):
        pairs = [(source, (source + shift) % count) for source in range(count)]
        arrived = lax.ppermute(value, axis, pairs)
        stacked = lax.dynamic_update_index_in_dim(stacked, arrived, (index - shift) % count, 0)
    return jnp.sum(stacked, axis=0)


def channel_total(partial_value):
    if lax.axis_size("tp") <= 4:
        return exchange_total(partial_value, "tp")
    return butterfly_total(partial_value, "tp")


def head_weights(scale_factor, query_head, key_head, visible):
    contract_last = (((1,), (1,)), ((), ()))
    scores = (
        lax.dot_general(query_head, key_head, contract_last, preferred_element_type=jnp.float32)
        * scale_factor
    )
    scores = jnp.where(visible > 0.5, scores, -jnp.inf)
    row_max = jnp.max(scores, axis=1, keepdims=True)
    logsum = row_max + jnp.log(jnp.sum(jnp.exp(scores - row_max), axis=1, keepdims=True))
    return jnp.exp(scores - logsum).astype(jnp.bfloat16)


def value_block(scale_factor, q_ref, k_ref, cot_ref, vis_ref, dv_ref):
    contract_first = (((0,), (0,)), ((), ()))
    weights = head_weights(scale_factor, q_ref[...], k_ref[...], vis_ref[...])
    dv_ref[...] = lax.dot_general(
        weights, cot_ref[...], contract_first, preferred_element_type=jnp.float32
    ).astype(jnp.bfloat16)


def attention_block(scale_factor, q_ref, k_ref, v_ref, cot_ref, vis_ref, dk_ref, att_ref, dq_ref):
    contract_last = (((1,), (1,)), ((), ()))
    contract_first = (((0,), (0,)), ((), ()))
    query_head = q_ref[...]
    key_head = k_ref[...]
    value_head = v_ref[...]
    cotangent_head = cot_ref[...]
    weights = head_weights(scale_factor, query_head, key_head, vis_ref[...])
    attended = jnp.dot(weights, value_head, preferred_element_type=jnp.float32)
    weight_grad = lax.dot_general(
        cotangent_head, value_head, contract_last, preferred_element_type=jnp.float32
    )
    row_delta = jnp.sum(cotangent_head.astype(jnp.float32) * attended, axis=1, keepdims=True)
    dscore = (scale_factor * weights.astype(jnp.float32) * (weight_grad - row_delta)).astype(
        jnp.bfloat16
    )
    att_ref[...] = attended
    dq_ref[...] = jnp.dot(dscore, key_head, preferred_element_type=jnp.float32).astype(jnp.bfloat16)
    dk_ref[...] = lax.dot_general(
        dscore, query_head, contract_first, preferred_element_type=jnp.float32
    ).astype(jnp.bfloat16)


def head_specs(local_rows, total_rows):
    local_spec = pl.BlockSpec((local_rows, HD), lambda h: (0, h))
    whole_spec = pl.BlockSpec((total_rows, HD), lambda h: (0, h))
    mask_spec = pl.BlockSpec((local_rows, total_rows), lambda h: (0, 0))
    return local_spec, whole_spec, mask_spec


def head_values_grad(queries, keys_whole, cotangent, visible, scale_factor):
    local_rows, width_local = queries.shape
    total_rows = keys_whole.shape[0]
    local_spec, whole_spec, mask_spec = head_specs(local_rows, total_rows)
    return pl.pallas_call(
        functools.partial(value_block, scale_factor),
        grid=(width_local // HD,),
        in_specs=[local_spec, whole_spec, local_spec, mask_spec],
        out_specs=whole_spec,
        out_shape=jax.ShapeDtypeStruct((total_rows, width_local), jnp.bfloat16),
    )(queries, keys_whole, cotangent, visible)


def head_attention(queries, keys_whole, values_whole, cotangent, visible, scale_factor):
    local_rows, width_local = queries.shape
    total_rows = keys_whole.shape[0]
    local_spec, whole_spec, mask_spec = head_specs(local_rows, total_rows)
    return pl.pallas_call(
        functools.partial(attention_block, scale_factor),
        grid=(width_local // HD,),
        in_specs=[local_spec, whole_spec, whole_spec, local_spec, mask_spec],
        out_specs=[whole_spec, local_spec, local_spec],
        out_shape=[
            jax.ShapeDtypeStruct((total_rows, width_local), jnp.bfloat16),
            jax.ShapeDtypeStruct((local_rows, width_local), jnp.float32),
            jax.ShapeDtypeStruct((local_rows, width_local), jnp.bfloat16),
        ],
    )(queries, keys_whole, values_whole, cotangent, visible)


def shards(
    stream,
    shutter,
    feeder,
    stencil,
    valves,
    intake,
    kernel,
    scaling,
    queries,
    matchers,
    segments,
    cotangent,
):
    local_rows = stream.shape[0]
    width_local = stream.shape[1]
    head_count = width_local // HD
    total_rows = local_rows * lax.axis_size("ctx")
    position = lax.axis_index("ctx") * local_rows
    scale_factor = 1.0 / math.sqrt(HD)
    widened = stream.astype(jnp.float32)
    inner_one = feeder.astype(jnp.float32) * widened
    rim_one = neighbor_rows(inner_one[local_rows - (KS - 1) :], 1)
    padded_one = jnp.concatenate([rim_one, inner_one], axis=0)
    conv_one = depthwise(padded_one, stencil[::-1])
    first_out = (widened + shutter.astype(jnp.float32) * conv_one).astype(jnp.bfloat16)
    first_wide = first_out.astype(jnp.float32)
    inner_two = intake.astype(jnp.float32) * first_wide
    rim_two = neighbor_rows(inner_two[local_rows - (KM - 1) :], 1)
    padded_two = jnp.concatenate([rim_two, inner_two], axis=0)
    conv_two = depthwise(padded_two, kernel[::-1])
    second_out = (first_wide + valves.astype(jnp.float32) * conv_two).astype(jnp.bfloat16)
    second_wide = second_out.astype(jnp.float32)
    squares = channel_total(jnp.sum(second_wide * second_wide, axis=1))
    inverse_rms = lax.rsqrt(squares / D + epsilon)
    normed = (second_wide * inverse_rms[:, None] * scaling).astype(jnp.bfloat16)
    ctx_count = lax.axis_size("ctx")
    ctx_index = lax.axis_index("ctx")
    keys_whole = lax.all_gather(matchers, "ctx", axis=0, tiled=True)
    reach = min(ctx_count - 1, (3 * total_rows // 4 - 1 + local_rows - 1) // local_rows)
    query_pos = position + jnp.arange(local_rows, dtype=jnp.int32)
    key_pos = jnp.arange(total_rows, dtype=jnp.int32)
    query_seg = lax.dynamic_slice_in_dim(segments, position, local_rows, 0)
    visible = (key_pos[None, :] <= query_pos[:, None]) & (segments[None, :] == query_seg[:, None])
    mask = visible.astype(jnp.float32)
    value_part = head_values_grad(queries, keys_whole, cotangent, mask, scale_factor)
    value_grad = lax.dynamic_slice_in_dim(value_part, position, local_rows, 0).astype(jnp.float32)
    for distance in range(1, reach + 1):
        block_start = ((ctx_index - distance) % ctx_count) * local_rows
        leaving = lax.dynamic_slice_in_dim(value_part, block_start, local_rows, 0)
        value_grad = value_grad + passed_along(leaving, "ctx", -distance).astype(jnp.float32)
    values_whole = lax.all_gather(normed, "ctx", axis=0, tiled=True)
    key_part, attended_all, queries_grad = head_attention(
        queries, keys_whole, values_whole, cotangent, mask, scale_factor
    )
    result = (second_wide + attended_all).astype(jnp.bfloat16)
    key_part, value_grad = lax.optimization_barrier((key_part, value_grad))
    matchers_grad = lax.psum_scatter(
        key_part,
        "ctx",
        scatter_dimension=0,
        tiled=True,
    )
    gain_part = value_grad * scaling
    projected = channel_total(jnp.sum(gain_part * second_wide, axis=1))
    scaling_part = jnp.sum(value_grad * second_wide * inverse_rms[:, None], axis=0)
    second_grad = (
        cotangent.astype(jnp.float32)
        + inverse_rms[:, None] * gain_part
        - second_wide * (inverse_rms**3 * projected / D)[:, None]
    )
    valves_grad = (second_grad * conv_two).astype(jnp.bfloat16)
    dconv_two = second_grad * valves.astype(jnp.float32)
    back_two = neighbor_rows(dconv_two[: KM - 1], -1)
    dinner_two = depthwise(jnp.concatenate([dconv_two, back_two], axis=0), kernel)
    intake_grad = (dinner_two * first_wide).astype(jnp.bfloat16)
    kernel_part = depthwise(padded_two, dconv_two)[::-1]
    first_grad = second_grad + dinner_two * intake.astype(jnp.float32)
    shutter_grad = (first_grad * conv_one).astype(jnp.bfloat16)
    dconv_one = first_grad * shutter.astype(jnp.float32)
    back_one = neighbor_rows(dconv_one[: KS - 1], -1)
    dinner_one = depthwise(jnp.concatenate([dconv_one, back_one], axis=0), stencil)
    feeder_grad = (dinner_one * widened).astype(jnp.bfloat16)
    stencil_part = depthwise(padded_one, dconv_one)[::-1]
    stream_grad = (first_grad + dinner_one * feeder.astype(jnp.float32)).astype(jnp.bfloat16)
    filter_sum = butterfly_total(
        jnp.concatenate([kernel_part, scaling_part[None], stencil_part], axis=0), "ctx", jnp.bfloat16
    )
    kernel_sum = filter_sum[:KM]
    scaling_sum = filter_sum[KM]
    stencil_sum = filter_sum[KM + 1 :]
    normalizer = math.sqrt(total_rows)
    return (
        result,
        stream_grad,
        shutter_grad,
        feeder_grad,
        stencil_sum / normalizer,
        valves_grad,
        intake_grad,
        kernel_sum / normalizer,
        scaling_sum / normalizer,
        queries_grad,
        matchers_grad,
    )


def solution(mesh):
    placed = (
        P("ctx", "tp"),
        P("ctx", "tp"),
        P("ctx", "tp"),
        P(None, "tp"),
        P("ctx", "tp"),
        P("ctx", "tp"),
        P(None, "tp"),
        P("tp"),
        P("ctx", "tp"),
        P("ctx", "tp"),
        P(),
        P("ctx", "tp"),
    )
    return jax.shard_map(
        shards,
        mesh=mesh,
        in_specs=placed,
        out_specs=(
            P("ctx", "tp"),
            P("ctx", "tp"),
            P("ctx", "tp"),
            P("ctx", "tp"),
            P(None, "tp"),
            P("ctx", "tp"),
            P("ctx", "tp"),
            P(None, "tp"),
            P("tp"),
            P("ctx", "tp"),
            P("ctx", "tp"),
        ),
        check_vma=False,
    )
```

```python
import functools
import math

import jax
import jax.numpy as jnp
from jax import lax
from jax.experimental import pallas as pl
from jax.sharding import PartitionSpec as P

HD = 128
D = 4096
KS = 7
KM = 128


epsilon = 1e-06


def as_sent(shard):

    def short(part):
        return part.astype(jnp.bfloat16) if part.dtype == jnp.float32 else part

    return jax.tree.map(short, shard)


def passed_along(value, axis, steps):
    count = lax.axis_size(axis)
    leading, last = (max(0, -steps), min(count, count - steps))
    return lax.ppermute(value, axis, [(source, source + steps) for source in range(leading, last)])


def depthwise(padded, tap_rows):
    return lax.conv_general_dilated(
        padded[None],
        tap_rows[:, None, :],
        (1,),
        "VALID",
        dimension_numbers=("NWC", "WIO", "NWC"),
        feature_group_count=padded.shape[1],
        precision=lax.Precision.HIGHEST,
    )[0]


def neighbor_rows(edge_rows, offset):
    return passed_along(as_sent(edge_rows), "ctx", offset).astype(edge_rows.dtype)


def butterfly_total(value, axis, sent_type=None):
    count = lax.axis_size(axis)
    if count & (count - 1):
        if sent_type is None:
            return lax.psum(value, axis)
        return lax.psum(value.astype(sent_type), axis).astype(value.dtype)
    step = 1
    while step < count:
        pairs = [(source, source ^ step) for source in range(count)]
        if sent_type is None:
            value = value + lax.ppermute(value, axis, pairs)
        else:
            rounded = value.astype(sent_type)
            value = rounded.astype(value.dtype) + lax.ppermute(rounded, axis, pairs).astype(value.dtype)
        step *= 2
    return value


def exchange_total(value, axis):
    count = lax.axis_size(axis)
    index = lax.axis_index(axis)
    stacked = jnp.zeros((count,) + value.shape, value.dtype)
    stacked = lax.dynamic_update_index_in_dim(stacked, value, index, 0)
    for shift in range(1, count):
        pairs = [(source, (source + shift) % count) for source in range(count)]
        arrived = lax.ppermute(value, axis, pairs)
        stacked = lax.dynamic_update_index_in_dim(stacked, arrived, (index - shift) % count, 0)
    return jnp.sum(stacked, axis=0)


def channel_total(partial_value):
    if lax.axis_size("tp") <= 4:
        return exchange_total(partial_value, "tp")
    return butterfly_total(partial_value, "tp")


def head_weights(scale_factor, query_head, key_head, visible):
    contract_last = (((1,), (1,)), ((), ()))
    scores = (
        lax.dot_general(query_head, key_head, contract_last, preferred_element_type=jnp.float32)
        * scale_factor
    )
    scores = jnp.where(visible > 0.5, scores, -jnp.inf)
    row_max = jnp.max(scores, axis=1, keepdims=True)
    raised = jnp.exp(scores - row_max)
    return (raised * (1.0 / jnp.sum(raised, axis=1, keepdims=True))).astype(jnp.bfloat16)


def value_block(scale_factor, q_ref, k_ref, cot_ref, vis_ref, dv_ref, w_ref):
    contract_first = (((0,), (0,)), ((), ()))
    weights = head_weights(scale_factor, q_ref[...], k_ref[...], vis_ref[...])
    w_ref[0] = weights
    dv_ref[...] = lax.dot_general(
        weights, cot_ref[...], contract_first, preferred_element_type=jnp.float32
    ).astype(jnp.bfloat16)


def attention_block(scale_factor, q_ref, k_ref, v_ref, cot_ref, w_ref, dk_ref, att_ref, dq_ref):
    contract_last = (((1,), (1,)), ((), ()))
    contract_first = (((0,), (0,)), ((), ()))
    query_head = q_ref[...]
    key_head = k_ref[...]
    value_head = v_ref[...]
    cotangent_head = cot_ref[...]
    weights = w_ref[0]
    attended = jnp.dot(weights, value_head, preferred_element_type=jnp.float32)
    weight_grad = lax.dot_general(
        cotangent_head, value_head, contract_last, preferred_element_type=jnp.float32
    )
    row_delta = jnp.sum(cotangent_head.astype(jnp.float32) * attended, axis=1, keepdims=True)
    dscore = (scale_factor * weights.astype(jnp.float32) * (weight_grad - row_delta)).astype(
        jnp.bfloat16
    )
    att_ref[...] = attended
    dq_ref[...] = jnp.dot(dscore, key_head, preferred_element_type=jnp.float32).astype(jnp.bfloat16)
    dk_ref[...] = lax.dot_general(
        dscore, query_head, contract_first, preferred_element_type=jnp.float32
    ).astype(jnp.bfloat16)


def head_specs(local_rows, total_rows):
    local_spec = pl.BlockSpec((local_rows, HD), lambda h: (0, h))
    whole_spec = pl.BlockSpec((total_rows, HD), lambda h: (0, h))
    weight_spec = pl.BlockSpec((1, local_rows, total_rows), lambda h: (h, 0, 0))
    return local_spec, whole_spec, weight_spec


def head_values_grad(queries, keys_whole, cotangent, visible, scale_factor):
    local_rows, width_local = queries.shape
    total_rows = keys_whole.shape[0]
    local_spec, whole_spec, weight_spec = head_specs(local_rows, total_rows)
    mask_spec = pl.BlockSpec((local_rows, total_rows), lambda h: (0, 0))
    return pl.pallas_call(
        functools.partial(value_block, scale_factor),
        grid=(width_local // HD,),
        in_specs=[local_spec, whole_spec, local_spec, mask_spec],
        out_specs=[whole_spec, weight_spec],
        out_shape=[
            jax.ShapeDtypeStruct((total_rows, width_local), jnp.bfloat16),
            jax.ShapeDtypeStruct((width_local // HD, local_rows, total_rows), jnp.bfloat16),
        ],
    )(queries, keys_whole, cotangent, visible)


def head_attention(queries, keys_whole, values_whole, cotangent, weights, scale_factor):
    local_rows, width_local = queries.shape
    total_rows = keys_whole.shape[0]
    local_spec, whole_spec, weight_spec = head_specs(local_rows, total_rows)
    return pl.pallas_call(
        functools.partial(attention_block, scale_factor),
        grid=(width_local // HD,),
        in_specs=[local_spec, whole_spec, whole_spec, local_spec, weight_spec],
        out_specs=[whole_spec, local_spec, local_spec],
        out_shape=[
            jax.ShapeDtypeStruct((total_rows, width_local), jnp.bfloat16),
            jax.ShapeDtypeStruct((local_rows, width_local), jnp.float32),
            jax.ShapeDtypeStruct((local_rows, width_local), jnp.bfloat16),
        ],
    )(queries, keys_whole, values_whole, cotangent, weights)


def shards(
    stream,
    shutter,
    feeder,
    stencil,
    valves,
    intake,
    kernel,
    scaling,
    queries,
    matchers,
    segments,
    cotangent,
):
    local_rows = stream.shape[0]
    width_local = stream.shape[1]
    head_count = width_local // HD
    total_rows = local_rows * lax.axis_size("ctx")
    position = lax.axis_index("ctx") * local_rows
    scale_factor = 1.0 / math.sqrt(HD)
    widened = stream.astype(jnp.float32)
    inner_one = feeder.astype(jnp.float32) * widened
    rim_one = neighbor_rows(inner_one[local_rows - (KS - 1) :], 1)
    padded_one = jnp.concatenate([rim_one, inner_one], axis=0)
    conv_one = depthwise(padded_one, stencil[::-1])
    first_out = (widened + shutter.astype(jnp.float32) * conv_one).astype(jnp.bfloat16)
    first_wide = first_out.astype(jnp.float32)
    inner_two = intake.astype(jnp.float32) * first_wide
    rim_two = neighbor_rows(inner_two[local_rows - (KM - 1) :], 1)
    padded_two = jnp.concatenate([rim_two, inner_two], axis=0)
    conv_two = depthwise(padded_two, kernel[::-1])
    second_out = (first_wide + valves.astype(jnp.float32) * conv_two).astype(jnp.bfloat16)
    second_wide = second_out.astype(jnp.float32)
    squares = channel_total(jnp.sum(second_wide * second_wide, axis=1))
    inverse_rms = lax.rsqrt(squares / D + epsilon)
    normed = (second_wide * inverse_rms[:, None] * scaling).astype(jnp.bfloat16)
    ctx_count = lax.axis_size("ctx")
    ctx_index = lax.axis_index("ctx")
    keys_whole = lax.all_gather(matchers, "ctx", axis=0, tiled=True)
    reach = min(ctx_count - 1, (3 * total_rows // 4 - 1 + local_rows - 1) // local_rows)
    query_pos = position + jnp.arange(local_rows, dtype=jnp.int32)
    key_pos = jnp.arange(total_rows, dtype=jnp.int32)
    query_seg = lax.dynamic_slice_in_dim(segments, position, local_rows, 0)
    visible = (key_pos[None, :] <= query_pos[:, None]) & (segments[None, :] == query_seg[:, None])
    mask = visible.astype(jnp.float32)
    value_part, weights_all = head_values_grad(queries, keys_whole, cotangent, mask, scale_factor)
    value_grad = lax.dynamic_slice_in_dim(value_part, position, local_rows, 0).astype(jnp.float32)
    for distance in range(1, reach + 1):
        block_start = ((ctx_index - distance) % ctx_count) * local_rows
        leaving = lax.dynamic_slice_in_dim(value_part, block_start, local_rows, 0)
        value_grad = value_grad + passed_along(leaving, "ctx", -distance).astype(jnp.float32)
    values_whole = lax.all_gather(normed, "ctx", axis=0, tiled=True)
    key_part, attended_all, queries_grad = head_attention(
        queries, keys_whole, values_whole, cotangent, weights_all, scale_factor
    )
    result = (second_wide + attended_all).astype(jnp.bfloat16)
    key_part, value_grad = lax.optimization_barrier((key_part, value_grad))
    matchers_grad = lax.psum_scatter(
        key_part,
        "ctx",
        scatter_dimension=0,
        tiled=True,
    )
    gain_part = value_grad * scaling
    projected = channel_total(jnp.sum(gain_part * second_wide, axis=1))
    scaling_part = jnp.sum(value_grad * second_wide * inverse_rms[:, None], axis=0)
    second_grad = (
        cotangent.astype(jnp.float32)
        + inverse_rms[:, None] * gain_part
        - second_wide * (inverse_rms**3 * projected / D)[:, None]
    )
    valves_grad = (second_grad * conv_two).astype(jnp.bfloat16)
    dconv_two = second_grad * valves.astype(jnp.float32)
    back_two = neighbor_rows(dconv_two[: KM - 1], -1)
    dinner_two = depthwise(jnp.concatenate([dconv_two, back_two], axis=0), kernel)
    intake_grad = (dinner_two * first_wide).astype(jnp.bfloat16)
    kernel_part = depthwise(padded_two, dconv_two)[::-1]
    first_grad = second_grad + dinner_two * intake.astype(jnp.float32)
    shutter_grad = (first_grad * conv_one).astype(jnp.bfloat16)
    dconv_one = first_grad * shutter.astype(jnp.float32)
    back_one = neighbor_rows(dconv_one[: KS - 1], -1)
    dinner_one = depthwise(jnp.concatenate([dconv_one, back_one], axis=0), stencil)
    feeder_grad = (dinner_one * widened).astype(jnp.bfloat16)
    stencil_part = depthwise(padded_one, dconv_one)[::-1]
    stream_grad = (first_grad + dinner_one * feeder.astype(jnp.float32)).astype(jnp.bfloat16)
    filter_sum = butterfly_total(
        jnp.concatenate([kernel_part, scaling_part[None], stencil_part], axis=0), "ctx", jnp.bfloat16
    )
    kernel_sum = filter_sum[:KM]
    scaling_sum = filter_sum[KM]
    stencil_sum = filter_sum[KM + 1 :]
    normalizer = math.sqrt(total_rows)
    return (
        result,
        stream_grad,
        shutter_grad,
        feeder_grad,
        stencil_sum / normalizer,
        valves_grad,
        intake_grad,
        kernel_sum / normalizer,
        scaling_sum / normalizer,
        queries_grad,
        matchers_grad,
    )


def solution(mesh):
    placed = (
        P("ctx", "tp"),
        P("ctx", "tp"),
        P("ctx", "tp"),
        P(None, "tp"),
        P("ctx", "tp"),
        P("ctx", "tp"),
        P(None, "tp"),
        P("tp"),
        P("ctx", "tp"),
        P("ctx", "tp"),
        P(),
        P("ctx", "tp"),
    )
    return jax.shard_map(
        shards,
        mesh=mesh,
        in_specs=placed,
        out_specs=(
            P("ctx", "tp"),
            P("ctx", "tp"),
            P("ctx", "tp"),
            P("ctx", "tp"),
            P(None, "tp"),
            P("ctx", "tp"),
            P("ctx", "tp"),
            P(None, "tp"),
            P("tp"),
            P("ctx", "tp"),
            P("ctx", "tp"),
        ),
        check_vma=False,
    )
```

```python
import functools
import math

import jax
import jax.numpy as jnp
from jax import lax
from jax.experimental import pallas as pl
from jax.sharding import PartitionSpec as P

HD = 128
D = 4096
KS = 7
KM = 128


epsilon = 1e-06


def as_sent(shard):

    def short(part):
        return part.astype(jnp.bfloat16) if part.dtype == jnp.float32 else part

    return jax.tree.map(short, shard)


def passed_along(value, axis, steps):
    count = lax.axis_size(axis)
    leading, last = (max(0, -steps), min(count, count - steps))
    return lax.ppermute(value, axis, [(source, source + steps) for source in range(leading, last)])


def depthwise(padded, tap_rows):
    return lax.conv_general_dilated(
        padded[None],
        tap_rows[:, None, :],
        (1,),
        "VALID",
        dimension_numbers=("NWC", "WIO", "NWC"),
        feature_group_count=padded.shape[1],
        precision=lax.Precision.HIGHEST,
    )[0]


def neighbor_rows(edge_rows, offset):
    return passed_along(as_sent(edge_rows), "ctx", offset).astype(edge_rows.dtype)


def butterfly_total(value, axis, sent_type=None):
    count = lax.axis_size(axis)
    if count & (count - 1):
        if sent_type is None:
            return lax.psum(value, axis)
        return lax.psum(value.astype(sent_type), axis).astype(value.dtype)
    step = 1
    while step < count:
        pairs = [(source, source ^ step) for source in range(count)]
        if sent_type is None:
            value = value + lax.ppermute(value, axis, pairs)
        else:
            rounded = value.astype(sent_type)
            value = rounded.astype(value.dtype) + lax.ppermute(rounded, axis, pairs).astype(value.dtype)
        step *= 2
    return value


def exchange_total(value, axis):
    count = lax.axis_size(axis)
    index = lax.axis_index(axis)
    stacked = jnp.zeros((count,) + value.shape, value.dtype)
    stacked = lax.dynamic_update_index_in_dim(stacked, value, index, 0)
    for shift in range(1, count):
        pairs = [(source, (source + shift) % count) for source in range(count)]
        arrived = lax.ppermute(value, axis, pairs)
        stacked = lax.dynamic_update_index_in_dim(stacked, arrived, (index - shift) % count, 0)
    return jnp.sum(stacked, axis=0)


def channel_total(partial_value):
    if lax.axis_size("tp") <= 4:
        return exchange_total(partial_value, "tp")
    return butterfly_total(partial_value, "tp")


def head_weights(scale_factor, query_head, key_head, visible):
    contract_last = (((1,), (1,)), ((), ()))
    scores = (
        lax.dot_general(query_head, key_head, contract_last, preferred_element_type=jnp.float32)
        * scale_factor
    )
    scores = jnp.where(visible > 0.5, scores, -jnp.inf)
    row_max = jnp.max(scores, axis=1, keepdims=True)
    logsum = row_max + jnp.log(jnp.sum(jnp.exp(scores - row_max), axis=1, keepdims=True))
    return jnp.exp(scores - logsum).astype(jnp.bfloat16)


def value_block(scale_factor, q_ref, k_ref, cot_ref, vis_ref, dv_ref):
    contract_first = (((0,), (0,)), ((), ()))
    weights = head_weights(scale_factor, q_ref[...], k_ref[...], vis_ref[...])
    dv_ref[...] = lax.dot_general(
        weights, cot_ref[...], contract_first, preferred_element_type=jnp.float32
    ).astype(jnp.bfloat16)


def attention_block(scale_factor, q_ref, k_ref, v_ref, cot_ref, vis_ref, dk_ref, att_ref, dq_ref):
    contract_last = (((1,), (1,)), ((), ()))
    contract_first = (((0,), (0,)), ((), ()))
    query_head = q_ref[...]
    key_head = k_ref[...]
    value_head = v_ref[...]
    cotangent_head = cot_ref[...]
    weights = head_weights(scale_factor, query_head, key_head, vis_ref[...])
    attended = jnp.dot(weights, value_head, preferred_element_type=jnp.float32)
    weight_grad = lax.dot_general(
        cotangent_head, value_head, contract_last, preferred_element_type=jnp.float32
    )
    row_delta = jnp.sum(cotangent_head.astype(jnp.float32) * attended, axis=1, keepdims=True)
    dscore = (scale_factor * weights.astype(jnp.float32) * (weight_grad - row_delta)).astype(
        jnp.bfloat16
    )
    att_ref[...] = attended
    dq_ref[...] = jnp.dot(dscore, key_head, preferred_element_type=jnp.float32).astype(jnp.bfloat16)
    dk_ref[...] = lax.dot_general(
        dscore, query_head, contract_first, preferred_element_type=jnp.float32
    ).astype(jnp.bfloat16)


def head_specs(local_rows, total_rows):
    local_spec = pl.BlockSpec((local_rows, HD), lambda h: (0, h))
    whole_spec = pl.BlockSpec((total_rows, HD), lambda h: (0, h))
    mask_spec = pl.BlockSpec((local_rows, total_rows), lambda h: (0, 0))
    return local_spec, whole_spec, mask_spec


def head_values_grad(queries, keys_whole, cotangent, visible, scale_factor):
    local_rows, width_local = queries.shape
    total_rows = keys_whole.shape[0]
    local_spec, whole_spec, mask_spec = head_specs(local_rows, total_rows)
    return pl.pallas_call(
        functools.partial(value_block, scale_factor),
        grid=(width_local // HD,),
        in_specs=[local_spec, whole_spec, local_spec, mask_spec],
        out_specs=whole_spec,
        out_shape=jax.ShapeDtypeStruct((total_rows, width_local), jnp.bfloat16),
    )(queries, keys_whole, cotangent, visible)


def head_attention(queries, keys_whole, values_whole, cotangent, visible, scale_factor):
    local_rows, width_local = queries.shape
    total_rows = keys_whole.shape[0]
    local_spec, whole_spec, mask_spec = head_specs(local_rows, total_rows)
    return pl.pallas_call(
        functools.partial(attention_block, scale_factor),
        grid=(width_local // HD,),
        in_specs=[local_spec, whole_spec, whole_spec, local_spec, mask_spec],
        out_specs=[whole_spec, local_spec, local_spec],
        out_shape=[
            jax.ShapeDtypeStruct((total_rows, width_local), jnp.bfloat16),
            jax.ShapeDtypeStruct((local_rows, width_local), jnp.float32),
            jax.ShapeDtypeStruct((local_rows, width_local), jnp.bfloat16),
        ],
    )(queries, keys_whole, values_whole, cotangent, visible)


def shards(
    stream,
    shutter,
    feeder,
    stencil,
    valves,
    intake,
    kernel,
    scaling,
    queries,
    matchers,
    segments,
    cotangent,
):
    local_rows = stream.shape[0]
    width_local = stream.shape[1]
    head_count = width_local // HD
    total_rows = local_rows * lax.axis_size("ctx")
    position = lax.axis_index("ctx") * local_rows
    scale_factor = 1.0 / math.sqrt(HD)
    widened = stream.astype(jnp.float32)
    inner_one = feeder.astype(jnp.float32) * widened
    rim_one = neighbor_rows(inner_one[local_rows - (KS - 1) :], 1)
    padded_one = jnp.concatenate([rim_one, inner_one], axis=0)
    conv_one = depthwise(padded_one, stencil[::-1])
    first_out = (widened + shutter.astype(jnp.float32) * conv_one).astype(jnp.bfloat16)
    first_wide = first_out.astype(jnp.float32)
    inner_two = intake.astype(jnp.float32) * first_wide
    rim_two = neighbor_rows(inner_two[local_rows - (KM - 1) :], 1)
    padded_two = jnp.concatenate([rim_two, inner_two], axis=0)
    conv_two = depthwise(padded_two, kernel[::-1])
    second_out = (first_wide + valves.astype(jnp.float32) * conv_two).astype(jnp.bfloat16)
    second_wide = second_out.astype(jnp.float32)
    squares = channel_total(jnp.sum(second_wide * second_wide, axis=1))
    inverse_rms = lax.rsqrt(squares / D + epsilon)
    normed = (second_wide * inverse_rms[:, None] * scaling).astype(jnp.bfloat16)
    ctx_count = lax.axis_size("ctx")
    ctx_index = lax.axis_index("ctx")
    keys_whole = lax.all_gather(matchers, "ctx", axis=0, tiled=True)
    reach = min(ctx_count - 1, (3 * total_rows // 4 - 1 + local_rows - 1) // local_rows)
    query_pos = position + jnp.arange(local_rows, dtype=jnp.int32)
    key_pos = jnp.arange(total_rows, dtype=jnp.int32)
    query_seg = lax.dynamic_slice_in_dim(segments, position, local_rows, 0)
    visible = (key_pos[None, :] <= query_pos[:, None]) & (segments[None, :] == query_seg[:, None])
    mask = visible.astype(jnp.float32)
    value_part = head_values_grad(queries, keys_whole, cotangent, mask, scale_factor)
    value_grad = (
        lax.all_to_all(value_part, "ctx", 0, 0, tiled=True)
        .reshape(ctx_count, local_rows, width_local)
        .astype(jnp.float32)
        .sum(axis=0)
    )
    values_whole = lax.all_gather(normed, "ctx", axis=0, tiled=True)
    key_part, attended_all, queries_grad = head_attention(
        queries, keys_whole, values_whole, cotangent, mask, scale_factor
    )
    result = (second_wide + attended_all).astype(jnp.bfloat16)
    key_part, value_grad = lax.optimization_barrier((key_part, value_grad))
    matchers_grad = lax.psum_scatter(
        key_part,
        "ctx",
        scatter_dimension=0,
        tiled=True,
    )
    gain_part = value_grad * scaling
    projected = channel_total(jnp.sum(gain_part * second_wide, axis=1))
    scaling_part = jnp.sum(value_grad * second_wide * inverse_rms[:, None], axis=0)
    second_grad = (
        cotangent.astype(jnp.float32)
        + inverse_rms[:, None] * gain_part
        - second_wide * (inverse_rms**3 * projected / D)[:, None]
    )
    valves_grad = (second_grad * conv_two).astype(jnp.bfloat16)
    dconv_two = second_grad * valves.astype(jnp.float32)
    back_two = neighbor_rows(dconv_two[: KM - 1], -1)
    dinner_two = depthwise(jnp.concatenate([dconv_two, back_two], axis=0), kernel)
    intake_grad = (dinner_two * first_wide).astype(jnp.bfloat16)
    kernel_part = depthwise(padded_two, dconv_two)[::-1]
    first_grad = second_grad + dinner_two * intake.astype(jnp.float32)
    shutter_grad = (first_grad * conv_one).astype(jnp.bfloat16)
    dconv_one = first_grad * shutter.astype(jnp.float32)
    back_one = neighbor_rows(dconv_one[: KS - 1], -1)
    dinner_one = depthwise(jnp.concatenate([dconv_one, back_one], axis=0), stencil)
    feeder_grad = (dinner_one * widened).astype(jnp.bfloat16)
    stencil_part = depthwise(padded_one, dconv_one)[::-1]
    stream_grad = (first_grad + dinner_one * feeder.astype(jnp.float32)).astype(jnp.bfloat16)
    filter_sum = butterfly_total(
        jnp.concatenate([kernel_part, scaling_part[None], stencil_part], axis=0), "ctx", jnp.bfloat16
    )
    kernel_sum = filter_sum[:KM]
    scaling_sum = filter_sum[KM]
    stencil_sum = filter_sum[KM + 1 :]
    normalizer = math.sqrt(total_rows)
    return (
        result,
        stream_grad,
        shutter_grad,
        feeder_grad,
        stencil_sum / normalizer,
        valves_grad,
        intake_grad,
        kernel_sum / normalizer,
        scaling_sum / normalizer,
        queries_grad,
        matchers_grad,
    )


def solution(mesh):
    placed = (
        P("ctx", "tp"),
        P("ctx", "tp"),
        P("ctx", "tp"),
        P(None, "tp"),
        P("ctx", "tp"),
        P("ctx", "tp"),
        P(None, "tp"),
        P("tp"),
        P("ctx", "tp"),
        P("ctx", "tp"),
        P(),
        P("ctx", "tp"),
    )
    return jax.shard_map(
        shards,
        mesh=mesh,
        in_specs=placed,
        out_specs=(
            P("ctx", "tp"),
            P("ctx", "tp"),
            P("ctx", "tp"),
            P("ctx", "tp"),
            P(None, "tp"),
            P("ctx", "tp"),
            P("ctx", "tp"),
            P(None, "tp"),
            P("tp"),
            P("ctx", "tp"),
            P("ctx", "tp"),
        ),
        check_vma=False,
    )
```

```python
import functools
import math

import jax
import jax.numpy as jnp
from jax import lax
from jax.experimental import pallas as pl
from jax.sharding import PartitionSpec as P

HD = 128
D = 4096
KS = 7
KM = 128


epsilon = 1e-06


def as_sent(shard):

    def short(part):
        return part.astype(jnp.bfloat16) if part.dtype == jnp.float32 else part

    return jax.tree.map(short, shard)


def passed_along(value, axis, steps):
    count = lax.axis_size(axis)
    leading, last = (max(0, -steps), min(count, count - steps))
    return lax.ppermute(value, axis, [(source, source + steps) for source in range(leading, last)])


def depthwise(padded, tap_rows):
    return lax.conv_general_dilated(
        padded[None],
        tap_rows[:, None, :],
        (1,),
        "VALID",
        dimension_numbers=("NWC", "WIO", "NWC"),
        feature_group_count=padded.shape[1],
        precision=lax.Precision.HIGHEST,
    )[0]


def neighbor_rows(edge_rows, offset):
    return passed_along(as_sent(edge_rows), "ctx", offset).astype(edge_rows.dtype)


def butterfly_total(value, axis, sent_type=None):
    count = lax.axis_size(axis)
    if count & (count - 1):
        if sent_type is None:
            return lax.psum(value, axis)
        return lax.psum(value.astype(sent_type), axis).astype(value.dtype)
    step = 1
    while step < count:
        pairs = [(source, source ^ step) for source in range(count)]
        if sent_type is None:
            value = value + lax.ppermute(value, axis, pairs)
        else:
            rounded = value.astype(sent_type)
            value = rounded.astype(value.dtype) + lax.ppermute(rounded, axis, pairs).astype(value.dtype)
        step *= 2
    return value


def exchange_total(value, axis):
    count = lax.axis_size(axis)
    index = lax.axis_index(axis)
    stacked = jnp.zeros((count,) + value.shape, value.dtype)
    stacked = lax.dynamic_update_index_in_dim(stacked, value, index, 0)
    for shift in range(1, count):
        pairs = [(source, (source + shift) % count) for source in range(count)]
        arrived = lax.ppermute(value, axis, pairs)
        stacked = lax.dynamic_update_index_in_dim(stacked, arrived, (index - shift) % count, 0)
    return jnp.sum(stacked, axis=0)


def channel_total(partial_value):
    if lax.axis_size("tp") <= 4:
        return exchange_total(partial_value, "tp")
    return butterfly_total(partial_value, "tp")


def head_weights(scale_factor, query_head, key_head, visible):
    contract_last = (((1,), (1,)), ((), ()))
    scores = (
        lax.dot_general(query_head, key_head, contract_last, preferred_element_type=jnp.float32)
        * scale_factor
    )
    scores = jnp.where(visible > 0.5, scores, -jnp.inf)
    row_max = jnp.max(scores, axis=1, keepdims=True)
    logsum = row_max + jnp.log(jnp.sum(jnp.exp(scores - row_max), axis=1, keepdims=True))
    return jnp.exp(scores - logsum).astype(jnp.bfloat16)


def value_block(scale_factor, q_ref, k_ref, cot_ref, vis_ref, dv_ref):
    contract_first = (((0,), (0,)), ((), ()))
    weights = head_weights(scale_factor, q_ref[...], k_ref[...], vis_ref[...])
    dv_ref[...] = lax.dot_general(
        weights, cot_ref[...], contract_first, preferred_element_type=jnp.float32
    ).astype(jnp.bfloat16)


def attention_block(scale_factor, q_ref, k_ref, v_ref, cot_ref, vis_ref, dk_ref, att_ref, dq_ref):
    contract_last = (((1,), (1,)), ((), ()))
    contract_first = (((0,), (0,)), ((), ()))
    query_head = q_ref[...]
    key_head = k_ref[...]
    value_head = v_ref[...]
    cotangent_head = cot_ref[...]
    weights = head_weights(scale_factor, query_head, key_head, vis_ref[...])
    attended = jnp.dot(weights, value_head, preferred_element_type=jnp.float32)
    weight_grad = lax.dot_general(
        cotangent_head, value_head, contract_last, preferred_element_type=jnp.float32
    )
    row_delta = jnp.sum(cotangent_head.astype(jnp.float32) * attended, axis=1, keepdims=True)
    dscore = (scale_factor * weights.astype(jnp.float32) * (weight_grad - row_delta)).astype(
        jnp.bfloat16
    )
    att_ref[...] = attended
    dq_ref[...] = jnp.dot(dscore, key_head, preferred_element_type=jnp.float32).astype(jnp.bfloat16)
    dk_ref[...] = lax.dot_general(
        dscore, query_head, contract_first, preferred_element_type=jnp.float32
    ).astype(jnp.bfloat16)


def head_specs(local_rows, total_rows):
    local_spec = pl.BlockSpec((local_rows, HD), lambda h: (0, h))
    whole_spec = pl.BlockSpec((total_rows, HD), lambda h: (0, h))
    mask_spec = pl.BlockSpec((local_rows, total_rows), lambda h: (0, 0))
    return local_spec, whole_spec, mask_spec


def head_values_grad(queries, keys_whole, cotangent, visible, scale_factor):
    local_rows, width_local = queries.shape
    total_rows = keys_whole.shape[0]
    local_spec, whole_spec, mask_spec = head_specs(local_rows, total_rows)
    return pl.pallas_call(
        functools.partial(value_block, scale_factor),
        grid=(width_local // HD,),
        in_specs=[local_spec, whole_spec, local_spec, mask_spec],
        out_specs=whole_spec,
        out_shape=jax.ShapeDtypeStruct((total_rows, width_local), jnp.bfloat16),
    )(queries, keys_whole, cotangent, visible)


def head_attention(queries, keys_whole, values_whole, cotangent, visible, scale_factor):
    local_rows, width_local = queries.shape
    total_rows = keys_whole.shape[0]
    local_spec, whole_spec, mask_spec = head_specs(local_rows, total_rows)
    return pl.pallas_call(
        functools.partial(attention_block, scale_factor),
        grid=(width_local // HD,),
        in_specs=[local_spec, whole_spec, whole_spec, local_spec, mask_spec],
        out_specs=[whole_spec, local_spec, local_spec],
        out_shape=[
            jax.ShapeDtypeStruct((total_rows, width_local), jnp.bfloat16),
            jax.ShapeDtypeStruct((local_rows, width_local), jnp.float32),
            jax.ShapeDtypeStruct((local_rows, width_local), jnp.bfloat16),
        ],
    )(queries, keys_whole, values_whole, cotangent, visible)


def shards(
    stream,
    shutter,
    feeder,
    stencil,
    valves,
    intake,
    kernel,
    scaling,
    queries,
    matchers,
    segments,
    cotangent,
):
    local_rows = stream.shape[0]
    width_local = stream.shape[1]
    head_count = width_local // HD
    total_rows = local_rows * lax.axis_size("ctx")
    position = lax.axis_index("ctx") * local_rows
    scale_factor = 1.0 / math.sqrt(HD)
    widened = stream.astype(jnp.float32)
    inner_one = feeder.astype(jnp.float32) * widened
    rim_one = neighbor_rows(inner_one[local_rows - (KS - 1) :], 1)
    padded_one = jnp.concatenate([rim_one, inner_one], axis=0)
    conv_one = depthwise(padded_one, stencil[::-1])
    first_out = (widened + shutter.astype(jnp.float32) * conv_one).astype(jnp.bfloat16)
    first_wide = first_out.astype(jnp.float32)
    inner_two = intake.astype(jnp.float32) * first_wide
    rim_two = neighbor_rows(inner_two[local_rows - (KM - 1) :], 1)
    padded_two = jnp.concatenate([rim_two, inner_two], axis=0)
    conv_two = depthwise(padded_two, kernel[::-1])
    second_out = (first_wide + valves.astype(jnp.float32) * conv_two).astype(jnp.bfloat16)
    second_wide = second_out.astype(jnp.float32)
    squares = channel_total(jnp.sum(second_wide * second_wide, axis=1))
    inverse_rms = lax.rsqrt(squares / D + epsilon)
    normed = (second_wide * inverse_rms[:, None] * scaling).astype(jnp.bfloat16)
    ctx_count = lax.axis_size("ctx")
    ctx_index = lax.axis_index("ctx")
    keys_whole = lax.all_gather(matchers, "ctx", axis=0, tiled=True)
    reach = min(ctx_count - 1, (3 * total_rows // 4 - 1 + local_rows - 1) // local_rows)
    query_pos = position + jnp.arange(local_rows, dtype=jnp.int32)
    key_pos = jnp.arange(total_rows, dtype=jnp.int32)
    query_seg = lax.dynamic_slice_in_dim(segments, position, local_rows, 0)
    visible = (key_pos[None, :] <= query_pos[:, None]) & (segments[None, :] == query_seg[:, None])
    mask = visible.astype(jnp.float32)
    value_part = head_values_grad(queries, keys_whole, cotangent, mask, scale_factor)
    value_grad = (
        lax.all_to_all(value_part, "ctx", 0, 0, tiled=True)
        .reshape(ctx_count, local_rows, width_local)
        .astype(jnp.float32)
        .sum(axis=0)
    )
    values_whole = lax.all_gather(normed, "ctx", axis=0, tiled=True)
    gain_part = value_grad * scaling
    projected = channel_total(jnp.sum(gain_part * second_wide, axis=1))
    scaling_part = jnp.sum(value_grad * second_wide * inverse_rms[:, None], axis=0)
    second_grad = (
        cotangent.astype(jnp.float32)
        + inverse_rms[:, None] * gain_part
        - second_wide * (inverse_rms**3 * projected / D)[:, None]
    )
    valves_grad = (second_grad * conv_two).astype(jnp.bfloat16)
    dconv_two = second_grad * valves.astype(jnp.float32)
    back_two = neighbor_rows(dconv_two[: KM - 1], -1)
    dinner_two = depthwise(jnp.concatenate([dconv_two, back_two], axis=0), kernel)
    values_whole, _ = lax.optimization_barrier((values_whole, dinner_two))
    key_part, attended_all, queries_grad = head_attention(
        queries, keys_whole, values_whole, cotangent, mask, scale_factor
    )
    result = (second_wide + attended_all).astype(jnp.bfloat16)
    matchers_grad = lax.psum_scatter(
        key_part,
        "ctx",
        scatter_dimension=0,
        tiled=True,
    )
    intake_grad = (dinner_two * first_wide).astype(jnp.bfloat16)
    kernel_part = depthwise(padded_two, dconv_two)[::-1]
    first_grad = second_grad + dinner_two * intake.astype(jnp.float32)
    shutter_grad = (first_grad * conv_one).astype(jnp.bfloat16)
    dconv_one = first_grad * shutter.astype(jnp.float32)
    back_one = neighbor_rows(dconv_one[: KS - 1], -1)
    dinner_one = depthwise(jnp.concatenate([dconv_one, back_one], axis=0), stencil)
    feeder_grad = (dinner_one * widened).astype(jnp.bfloat16)
    stencil_part = depthwise(padded_one, dconv_one)[::-1]
    stream_grad = (first_grad + dinner_one * feeder.astype(jnp.float32)).astype(jnp.bfloat16)
    filter_sum = butterfly_total(
        jnp.concatenate([kernel_part, scaling_part[None], stencil_part], axis=0), "ctx", jnp.bfloat16
    )
    kernel_sum = filter_sum[:KM]
    scaling_sum = filter_sum[KM]
    stencil_sum = filter_sum[KM + 1 :]
    normalizer = math.sqrt(total_rows)
    return (
        result,
        stream_grad,
        shutter_grad,
        feeder_grad,
        stencil_sum / normalizer,
        valves_grad,
        intake_grad,
        kernel_sum / normalizer,
        scaling_sum / normalizer,
        queries_grad,
        matchers_grad,
    )


def solution(mesh):
    placed = (
        P("ctx", "tp"),
        P("ctx", "tp"),
        P("ctx", "tp"),
        P(None, "tp"),
        P("ctx", "tp"),
        P("ctx", "tp"),
        P(None, "tp"),
        P("tp"),
        P("ctx", "tp"),
        P("ctx", "tp"),
        P(),
        P("ctx", "tp"),
    )
    return jax.shard_map(
        shards,
        mesh=mesh,
        in_specs=placed,
        out_specs=(
            P("ctx", "tp"),
            P("ctx", "tp"),
            P("ctx", "tp"),
            P("ctx", "tp"),
            P(None, "tp"),
            P("ctx", "tp"),
            P("ctx", "tp"),
            P(None, "tp"),
            P("tp"),
            P("ctx", "tp"),
            P("ctx", "tp"),
        ),
        check_vma=False,
    )
```

```python
import functools
import math

import jax
import jax.numpy as jnp
from jax import lax
from jax.experimental import pallas as pl
from jax.sharding import PartitionSpec as P

HD = 128
D = 4096
KS = 7
KM = 128


epsilon = 1e-06


def as_sent(shard):

    def short(part):
        return part.astype(jnp.bfloat16) if part.dtype == jnp.float32 else part

    return jax.tree.map(short, shard)


def passed_along(value, axis, steps):
    count = lax.axis_size(axis)
    leading, last = (max(0, -steps), min(count, count - steps))
    return lax.ppermute(value, axis, [(source, source + steps) for source in range(leading, last)])


def depthwise(padded, tap_rows):
    return lax.conv_general_dilated(
        padded[None],
        tap_rows[:, None, :],
        (1,),
        "VALID",
        dimension_numbers=("NWC", "WIO", "NWC"),
        feature_group_count=padded.shape[1],
        precision=lax.Precision.HIGHEST,
    )[0]


def neighbor_rows(edge_rows, offset):
    return passed_along(as_sent(edge_rows), "ctx", offset).astype(edge_rows.dtype)


def butterfly_total(value, axis, sent_type=None):
    count = lax.axis_size(axis)
    if count & (count - 1):
        if sent_type is None:
            return lax.psum(value, axis)
        return lax.psum(value.astype(sent_type), axis).astype(value.dtype)
    step = 1
    while step < count:
        pairs = [(source, source ^ step) for source in range(count)]
        if sent_type is None:
            value = value + lax.ppermute(value, axis, pairs)
        else:
            rounded = value.astype(sent_type)
            value = rounded.astype(value.dtype) + lax.ppermute(rounded, axis, pairs).astype(value.dtype)
        step *= 2
    return value


def exchange_total(value, axis):
    count = lax.axis_size(axis)
    index = lax.axis_index(axis)
    stacked = jnp.zeros((count,) + value.shape, value.dtype)
    stacked = lax.dynamic_update_index_in_dim(stacked, value, index, 0)
    for shift in range(1, count):
        pairs = [(source, (source + shift) % count) for source in range(count)]
        arrived = lax.ppermute(value, axis, pairs)
        stacked = lax.dynamic_update_index_in_dim(stacked, arrived, (index - shift) % count, 0)
    return jnp.sum(stacked, axis=0)


def channel_total(partial_value):
    if lax.axis_size("tp") <= 4:
        return exchange_total(partial_value, "tp")
    return butterfly_total(partial_value, "tp")


def head_weights(scale_factor, query_head, key_head, visible):
    contract_last = (((1,), (1,)), ((), ()))
    scores = (
        lax.dot_general(query_head, key_head, contract_last, preferred_element_type=jnp.float32)
        * scale_factor
    )
    scores = jnp.where(visible > 0.5, scores, -jnp.inf)
    row_max = jnp.max(scores, axis=1, keepdims=True)
    logsum = row_max + jnp.log(jnp.sum(jnp.exp(scores - row_max), axis=1, keepdims=True))
    return jnp.exp(scores - logsum).astype(jnp.bfloat16)


def value_block(scale_factor, q_ref, k_ref, cot_ref, vis_ref, dv_ref):
    contract_first = (((0,), (0,)), ((), ()))
    weights = head_weights(scale_factor, q_ref[...], k_ref[...], vis_ref[...])
    dv_ref[...] = lax.dot_general(
        weights, cot_ref[...], contract_first, preferred_element_type=jnp.float32
    ).astype(jnp.bfloat16)


def attention_block(scale_factor, q_ref, k_ref, v_ref, cot_ref, vis_ref, dk_ref, att_ref, dq_ref):
    contract_last = (((1,), (1,)), ((), ()))
    contract_first = (((0,), (0,)), ((), ()))
    query_head = q_ref[...]
    key_head = k_ref[...]
    value_head = v_ref[...]
    cotangent_head = cot_ref[...]
    weights = head_weights(scale_factor, query_head, key_head, vis_ref[...])
    attended = jnp.dot(weights, value_head, preferred_element_type=jnp.float32)
    weight_grad = lax.dot_general(
        cotangent_head, value_head, contract_last, preferred_element_type=jnp.float32
    )
    row_delta = jnp.sum(cotangent_head.astype(jnp.float32) * attended, axis=1, keepdims=True)
    dscore = (scale_factor * weights.astype(jnp.float32) * (weight_grad - row_delta)).astype(
        jnp.bfloat16
    )
    att_ref[...] = attended
    dq_ref[...] = jnp.dot(dscore, key_head, preferred_element_type=jnp.float32).astype(jnp.bfloat16)
    dk_ref[...] = lax.dot_general(
        dscore, query_head, contract_first, preferred_element_type=jnp.float32
    ).astype(jnp.bfloat16)


def head_specs(local_rows, total_rows):
    local_spec = pl.BlockSpec((local_rows, HD), lambda h: (0, h))
    whole_spec = pl.BlockSpec((total_rows, HD), lambda h: (0, h))
    mask_spec = pl.BlockSpec((local_rows, total_rows), lambda h: (0, 0))
    return local_spec, whole_spec, mask_spec


def head_values_grad(queries, keys_whole, cotangent, visible, scale_factor):
    local_rows, width_local = queries.shape
    total_rows = keys_whole.shape[0]
    local_spec, whole_spec, mask_spec = head_specs(local_rows, total_rows)
    return pl.pallas_call(
        functools.partial(value_block, scale_factor),
        grid=(width_local // HD,),
        in_specs=[local_spec, whole_spec, local_spec, mask_spec],
        out_specs=whole_spec,
        out_shape=jax.ShapeDtypeStruct((total_rows, width_local), jnp.bfloat16),
    )(queries, keys_whole, cotangent, visible)


def head_attention(queries, keys_whole, values_whole, cotangent, visible, scale_factor):
    local_rows, width_local = queries.shape
    total_rows = keys_whole.shape[0]
    local_spec, whole_spec, mask_spec = head_specs(local_rows, total_rows)
    return pl.pallas_call(
        functools.partial(attention_block, scale_factor),
        grid=(width_local // HD,),
        in_specs=[local_spec, whole_spec, whole_spec, local_spec, mask_spec],
        out_specs=[whole_spec, local_spec, local_spec],
        out_shape=[
            jax.ShapeDtypeStruct((total_rows, width_local), jnp.bfloat16),
            jax.ShapeDtypeStruct((local_rows, width_local), jnp.float32),
            jax.ShapeDtypeStruct((local_rows, width_local), jnp.bfloat16),
        ],
    )(queries, keys_whole, values_whole, cotangent, visible)


def shards(
    stream,
    shutter,
    feeder,
    stencil,
    valves,
    intake,
    kernel,
    scaling,
    queries,
    matchers,
    segments,
    cotangent,
):
    local_rows = stream.shape[0]
    width_local = stream.shape[1]
    head_count = width_local // HD
    total_rows = local_rows * lax.axis_size("ctx")
    position = lax.axis_index("ctx") * local_rows
    scale_factor = 1.0 / math.sqrt(HD)
    widened = stream.astype(jnp.float32)
    inner_one = feeder.astype(jnp.float32) * widened
    rim_one = neighbor_rows(inner_one[local_rows - (KS - 1) :], 1)
    padded_one = jnp.concatenate([rim_one, inner_one], axis=0)
    conv_one = depthwise(padded_one, stencil[::-1])
    first_out = (widened + shutter.astype(jnp.float32) * conv_one).astype(jnp.bfloat16)
    first_wide = first_out.astype(jnp.float32)
    inner_two = intake.astype(jnp.float32) * first_wide
    rim_two = neighbor_rows(inner_two[local_rows - (KM - 1) :], 1)
    padded_two = jnp.concatenate([rim_two, inner_two], axis=0)
    conv_two = depthwise(padded_two, kernel[::-1])
    second_out = (first_wide + valves.astype(jnp.float32) * conv_two).astype(jnp.bfloat16)
    second_wide = second_out.astype(jnp.float32)
    squares = channel_total(jnp.sum(second_wide * second_wide, axis=1))
    inverse_rms = lax.rsqrt(squares / D + epsilon)
    normed = (second_wide * inverse_rms[:, None] * scaling).astype(jnp.bfloat16)
    ctx_count = lax.axis_size("ctx")
    ctx_index = lax.axis_index("ctx")
    keys_whole = lax.all_gather(matchers, "ctx", axis=0, tiled=True)
    reach = min(ctx_count - 1, (3 * total_rows // 4 - 1 + local_rows - 1) // local_rows)
    query_pos = position + jnp.arange(local_rows, dtype=jnp.int32)
    key_pos = jnp.arange(total_rows, dtype=jnp.int32)
    query_seg = lax.dynamic_slice_in_dim(segments, position, local_rows, 0)
    visible = (key_pos[None, :] <= query_pos[:, None]) & (segments[None, :] == query_seg[:, None])
    mask = visible.astype(jnp.float32)
    held_queries, normed = lax.optimization_barrier((queries, normed))
    value_part = head_values_grad(held_queries, keys_whole, cotangent, mask, scale_factor)
    value_grad = (
        lax.all_to_all(value_part, "ctx", 0, 0, tiled=True)
        .reshape(ctx_count, local_rows, width_local)
        .astype(jnp.float32)
        .sum(axis=0)
    )
    values_whole = lax.all_gather(normed, "ctx", axis=0, tiled=True)
    gain_part = value_grad * scaling
    projected = channel_total(jnp.sum(gain_part * second_wide, axis=1))
    scaling_part = jnp.sum(value_grad * second_wide * inverse_rms[:, None], axis=0)
    second_grad = (
        cotangent.astype(jnp.float32)
        + inverse_rms[:, None] * gain_part
        - second_wide * (inverse_rms**3 * projected / D)[:, None]
    )
    values_whole, _ = lax.optimization_barrier((values_whole, second_grad))
    key_part, attended_all, queries_grad = head_attention(
        queries, keys_whole, values_whole, cotangent, mask, scale_factor
    )
    result = (second_wide + attended_all).astype(jnp.bfloat16)
    matchers_grad = lax.psum_scatter(
        key_part,
        "ctx",
        scatter_dimension=0,
        tiled=True,
    )
    valves_grad = (second_grad * conv_two).astype(jnp.bfloat16)
    dconv_two = second_grad * valves.astype(jnp.float32)
    back_two = neighbor_rows(dconv_two[: KM - 1], -1)
    dinner_two = depthwise(jnp.concatenate([dconv_two, back_two], axis=0), kernel)
    intake_grad = (dinner_two * first_wide).astype(jnp.bfloat16)
    kernel_part = depthwise(padded_two, dconv_two)[::-1]
    first_grad = second_grad + dinner_two * intake.astype(jnp.float32)
    shutter_grad = (first_grad * conv_one).astype(jnp.bfloat16)
    dconv_one = first_grad * shutter.astype(jnp.float32)
    back_one = neighbor_rows(dconv_one[: KS - 1], -1)
    dinner_one = depthwise(jnp.concatenate([dconv_one, back_one], axis=0), stencil)
    feeder_grad = (dinner_one * widened).astype(jnp.bfloat16)
    stencil_part = depthwise(padded_one, dconv_one)[::-1]
    stream_grad = (first_grad + dinner_one * feeder.astype(jnp.float32)).astype(jnp.bfloat16)
    filter_sum = butterfly_total(
        jnp.concatenate([kernel_part, scaling_part[None], stencil_part], axis=0), "ctx", jnp.bfloat16
    )
    kernel_sum = filter_sum[:KM]
    scaling_sum = filter_sum[KM]
    stencil_sum = filter_sum[KM + 1 :]
    normalizer = math.sqrt(total_rows)
    return (
        result,
        stream_grad,
        shutter_grad,
        feeder_grad,
        stencil_sum / normalizer,
        valves_grad,
        intake_grad,
        kernel_sum / normalizer,
        scaling_sum / normalizer,
        queries_grad,
        matchers_grad,
    )


def solution(mesh):
    placed = (
        P("ctx", "tp"),
        P("ctx", "tp"),
        P("ctx", "tp"),
        P(None, "tp"),
        P("ctx", "tp"),
        P("ctx", "tp"),
        P(None, "tp"),
        P("tp"),
        P("ctx", "tp"),
        P("ctx", "tp"),
        P(),
        P("ctx", "tp"),
    )
    return jax.shard_map(
        shards,
        mesh=mesh,
        in_specs=placed,
        out_specs=(
            P("ctx", "tp"),
            P("ctx", "tp"),
            P("ctx", "tp"),
            P("ctx", "tp"),
            P(None, "tp"),
            P("ctx", "tp"),
            P("ctx", "tp"),
            P(None, "tp"),
            P("tp"),
            P("ctx", "tp"),
            P("ctx", "tp"),
        ),
        check_vma=False,
    )
```

```python
import functools
import math

import jax
import jax.numpy as jnp
from jax import lax
from jax.experimental import pallas as pl
from jax.sharding import PartitionSpec as P

HD = 128
D = 4096
KS = 7
KM = 128


epsilon = 1e-06


def as_sent(shard):

    def short(part):
        return part.astype(jnp.bfloat16) if part.dtype == jnp.float32 else part

    return jax.tree.map(short, shard)


def passed_along(value, axis, steps):
    count = lax.axis_size(axis)
    leading, last = (max(0, -steps), min(count, count - steps))
    return lax.ppermute(value, axis, [(source, source + steps) for source in range(leading, last)])


def depthwise(padded, tap_rows):
    return lax.conv_general_dilated(
        padded[None],
        tap_rows[:, None, :],
        (1,),
        "VALID",
        dimension_numbers=("NWC", "WIO", "NWC"),
        feature_group_count=padded.shape[1],
        precision=lax.Precision.HIGHEST,
    )[0]


def neighbor_rows(edge_rows, offset):
    return passed_along(as_sent(edge_rows), "ctx", offset).astype(edge_rows.dtype)


def butterfly_total(value, axis, sent_type=None):
    count = lax.axis_size(axis)
    if count & (count - 1):
        if sent_type is None:
            return lax.psum(value, axis)
        return lax.psum(value.astype(sent_type), axis).astype(value.dtype)
    step = 1
    while step < count:
        pairs = [(source, source ^ step) for source in range(count)]
        if sent_type is None:
            value = value + lax.ppermute(value, axis, pairs)
        else:
            rounded = value.astype(sent_type)
            value = rounded.astype(value.dtype) + lax.ppermute(rounded, axis, pairs).astype(value.dtype)
        step *= 2
    return value


def exchange_total(value, axis):
    count = lax.axis_size(axis)
    index = lax.axis_index(axis)
    stacked = jnp.zeros((count,) + value.shape, value.dtype)
    stacked = lax.dynamic_update_index_in_dim(stacked, value, index, 0)
    for shift in range(1, count):
        pairs = [(source, (source + shift) % count) for source in range(count)]
        arrived = lax.ppermute(value, axis, pairs)
        stacked = lax.dynamic_update_index_in_dim(stacked, arrived, (index - shift) % count, 0)
    return jnp.sum(stacked, axis=0)


def channel_total(partial_value):
    if lax.axis_size("tp") <= 4:
        return exchange_total(partial_value, "tp")
    return butterfly_total(partial_value, "tp")


def head_weights(scale_factor, query_head, key_head, visible):
    contract_last = (((1,), (1,)), ((), ()))
    scores = (
        lax.dot_general(query_head, key_head, contract_last, preferred_element_type=jnp.float32)
        * scale_factor
    )
    scores = jnp.where(visible, scores, -jnp.inf)
    row_max = jnp.max(scores, axis=1, keepdims=True)
    raised = jnp.exp(scores - row_max)
    return (raised * (1.0 / jnp.sum(raised, axis=1, keepdims=True))).astype(jnp.bfloat16)


def value_block(scale_factor, q_ref, k_ref, cot_ref, vis_ref, dv_ref, w_ref):
    contract_first = (((0,), (0,)), ((), ()))
    visible = vis_ref[...] > 0.5
    for head in range(w_ref.shape[0]):
        columns = slice(head * HD, (head + 1) * HD)
        weights = head_weights(scale_factor, q_ref[:, columns], k_ref[:, columns], visible)
        w_ref[head] = weights
        dv_ref[:, columns] = lax.dot_general(
            weights, cot_ref[:, columns], contract_first, preferred_element_type=jnp.float32
        ).astype(jnp.bfloat16)


def attention_block(scale_factor, q_ref, k_ref, v_ref, cot_ref, w_ref, dk_ref, att_ref, dq_ref):
    contract_last = (((1,), (1,)), ((), ()))
    contract_first = (((0,), (0,)), ((), ()))
    for head in range(w_ref.shape[0]):
        columns = slice(head * HD, (head + 1) * HD)
        query_head = q_ref[:, columns]
        key_head = k_ref[:, columns]
        value_head = v_ref[:, columns]
        cotangent_head = cot_ref[:, columns]
        weights = w_ref[head]
        attended = jnp.dot(weights, value_head, preferred_element_type=jnp.float32)
        weight_grad = lax.dot_general(
            cotangent_head, value_head, contract_last, preferred_element_type=jnp.float32
        )
        row_delta = jnp.sum(cotangent_head.astype(jnp.float32) * attended, axis=1, keepdims=True)
        dscore = (scale_factor * weights.astype(jnp.float32) * (weight_grad - row_delta)).astype(
            jnp.bfloat16
        )
        att_ref[:, columns] = attended
        dq_ref[:, columns] = jnp.dot(
            dscore, key_head, preferred_element_type=jnp.float32
        ).astype(jnp.bfloat16)
        dk_ref[:, columns] = lax.dot_general(
            dscore, query_head, contract_first, preferred_element_type=jnp.float32
        ).astype(jnp.bfloat16)


def head_specs(local_rows, total_rows, width_local):
    group = 2 if (width_local // HD) % 2 == 0 else 1
    local_spec = pl.BlockSpec((local_rows, group * HD), lambda h: (0, h))
    whole_spec = pl.BlockSpec((total_rows, group * HD), lambda h: (0, h))
    weight_spec = pl.BlockSpec((group, local_rows, total_rows), lambda h: (h, 0, 0))
    return local_spec, whole_spec, weight_spec, width_local // (group * HD)


def head_values_grad(queries, keys_whole, cotangent, visible, scale_factor):
    local_rows, width_local = queries.shape
    total_rows = keys_whole.shape[0]
    local_spec, whole_spec, weight_spec, steps = head_specs(local_rows, total_rows, width_local)
    mask_spec = pl.BlockSpec((local_rows, total_rows), lambda h: (0, 0))
    return pl.pallas_call(
        functools.partial(value_block, scale_factor),
        grid=(steps,),
        in_specs=[local_spec, whole_spec, local_spec, mask_spec],
        out_specs=[whole_spec, weight_spec],
        out_shape=[
            jax.ShapeDtypeStruct((total_rows, width_local), jnp.bfloat16),
            jax.ShapeDtypeStruct((width_local // HD, local_rows, total_rows), jnp.bfloat16),
        ],
    )(queries, keys_whole, cotangent, visible)


def head_attention(queries, keys_whole, values_whole, cotangent, weights, scale_factor):
    local_rows, width_local = queries.shape
    total_rows = keys_whole.shape[0]
    local_spec, whole_spec, weight_spec, steps = head_specs(local_rows, total_rows, width_local)
    return pl.pallas_call(
        functools.partial(attention_block, scale_factor),
        grid=(steps,),
        in_specs=[local_spec, whole_spec, whole_spec, local_spec, weight_spec],
        out_specs=[whole_spec, local_spec, local_spec],
        out_shape=[
            jax.ShapeDtypeStruct((total_rows, width_local), jnp.bfloat16),
            jax.ShapeDtypeStruct((local_rows, width_local), jnp.float32),
            jax.ShapeDtypeStruct((local_rows, width_local), jnp.bfloat16),
        ],
    )(queries, keys_whole, values_whole, cotangent, weights)


def shards(
    stream,
    shutter,
    feeder,
    stencil,
    valves,
    intake,
    kernel,
    scaling,
    queries,
    matchers,
    segments,
    cotangent,
):
    local_rows = stream.shape[0]
    width_local = stream.shape[1]
    head_count = width_local // HD
    total_rows = local_rows * lax.axis_size("ctx")
    position = lax.axis_index("ctx") * local_rows
    scale_factor = 1.0 / math.sqrt(HD)
    widened = stream.astype(jnp.float32)
    inner_one = feeder.astype(jnp.float32) * widened
    rim_one = neighbor_rows(inner_one[local_rows - (KS - 1) :], 1)
    padded_one = jnp.concatenate([rim_one, inner_one], axis=0)
    conv_one = depthwise(padded_one, stencil[::-1])
    first_out = (widened + shutter.astype(jnp.float32) * conv_one).astype(jnp.bfloat16)
    first_wide = first_out.astype(jnp.float32)
    inner_two = intake.astype(jnp.float32) * first_wide
    rim_two = neighbor_rows(inner_two[local_rows - (KM - 1) :], 1)
    padded_two = jnp.concatenate([rim_two, inner_two], axis=0)
    conv_two = depthwise(padded_two, kernel[::-1])
    second_out = (first_wide + valves.astype(jnp.float32) * conv_two).astype(jnp.bfloat16)
    second_wide = second_out.astype(jnp.float32)
    squares = channel_total(jnp.sum(second_wide * second_wide, axis=1))
    inverse_rms = lax.rsqrt(squares / D + epsilon)
    normed = (second_wide * inverse_rms[:, None] * scaling).astype(jnp.bfloat16)
    ctx_count = lax.axis_size("ctx")
    ctx_index = lax.axis_index("ctx")
    keys_whole = lax.all_gather(matchers, "ctx", axis=0, tiled=True)
    reach = min(ctx_count - 1, (3 * total_rows // 4 - 1 + local_rows - 1) // local_rows)
    query_pos = position + jnp.arange(local_rows, dtype=jnp.int32)
    key_pos = jnp.arange(total_rows, dtype=jnp.int32)
    query_seg = lax.dynamic_slice_in_dim(segments, position, local_rows, 0)
    visible = (key_pos[None, :] <= query_pos[:, None]) & (segments[None, :] == query_seg[:, None])
    mask = visible.astype(jnp.float32)
    value_part, weights_all = head_values_grad(queries, keys_whole, cotangent, mask, scale_factor)
    value_grad = (
        lax.all_to_all(value_part, "ctx", 0, 0, tiled=True)
        .reshape(ctx_count, local_rows, width_local)
        .astype(jnp.float32)
        .sum(axis=0)
    )
    values_whole = lax.all_gather(normed, "ctx", axis=0, tiled=True)
    key_part, attended_all, queries_grad = head_attention(
        queries, keys_whole, values_whole, cotangent, weights_all, scale_factor
    )
    result = (second_wide + attended_all).astype(jnp.bfloat16)
    key_part, value_grad = lax.optimization_barrier((key_part, value_grad))
    matchers_grad = lax.psum_scatter(
        key_part,
        "ctx",
        scatter_dimension=0,
        tiled=True,
    )
    gain_part = value_grad * scaling
    projected = channel_total(jnp.sum(gain_part * second_wide, axis=1))
    scaling_part = jnp.sum(value_grad * second_wide * inverse_rms[:, None], axis=0)
    second_grad = (
        cotangent.astype(jnp.float32)
        + inverse_rms[:, None] * gain_part
        - second_wide * (inverse_rms**3 * projected / D)[:, None]
    )
    valves_grad = (second_grad * conv_two).astype(jnp.bfloat16)
    dconv_two = second_grad * valves.astype(jnp.float32)
    back_two = neighbor_rows(dconv_two[: KM - 1], -1)
    dinner_two = depthwise(jnp.concatenate([dconv_two, back_two], axis=0), kernel)
    intake_grad = (dinner_two * first_wide).astype(jnp.bfloat16)
    kernel_part = depthwise(padded_two, dconv_two)[::-1]
    first_grad = second_grad + dinner_two * intake.astype(jnp.float32)
    shutter_grad = (first_grad * conv_one).astype(jnp.bfloat16)
    dconv_one = first_grad * shutter.astype(jnp.float32)
    back_one = neighbor_rows(dconv_one[: KS - 1], -1)
    dinner_one = depthwise(jnp.concatenate([dconv_one, back_one], axis=0), stencil)
    feeder_grad = (dinner_one * widened).astype(jnp.bfloat16)
    stencil_part = depthwise(padded_one, dconv_one)[::-1]
    stream_grad = (first_grad + dinner_one * feeder.astype(jnp.float32)).astype(jnp.bfloat16)
    filter_sum = butterfly_total(
        jnp.concatenate([kernel_part, scaling_part[None], stencil_part], axis=0), "ctx", jnp.bfloat16
    )
    kernel_sum = filter_sum[:KM]
    scaling_sum = filter_sum[KM]
    stencil_sum = filter_sum[KM + 1 :]
    normalizer = math.sqrt(total_rows)
    return (
        result,
        stream_grad,
        shutter_grad,
        feeder_grad,
        stencil_sum / normalizer,
        valves_grad,
        intake_grad,
        kernel_sum / normalizer,
        scaling_sum / normalizer,
        queries_grad,
        matchers_grad,
    )


def solution(mesh):
    placed = (
        P("ctx", "tp"),
        P("ctx", "tp"),
        P("ctx", "tp"),
        P(None, "tp"),
        P("ctx", "tp"),
        P("ctx", "tp"),
        P(None, "tp"),
        P("tp"),
        P("ctx", "tp"),
        P("ctx", "tp"),
        P(),
        P("ctx", "tp"),
    )
    return jax.shard_map(
        shards,
        mesh=mesh,
        in_specs=placed,
        out_specs=(
            P("ctx", "tp"),
            P("ctx", "tp"),
            P("ctx", "tp"),
            P("ctx", "tp"),
            P(None, "tp"),
            P("ctx", "tp"),
            P("ctx", "tp"),
            P(None, "tp"),
            P("tp"),
            P("ctx", "tp"),
            P("ctx", "tp"),
        ),
        check_vma=False,
    )
```

```python
import functools
import math

import jax
import jax.numpy as jnp
from jax import lax
from jax.experimental import pallas as pl
from jax.sharding import PartitionSpec as P

HD = 128
D = 4096
KS = 7
KM = 128


epsilon = 1e-06


def as_sent(shard):

    def short(part):
        return part.astype(jnp.bfloat16) if part.dtype == jnp.float32 else part

    return jax.tree.map(short, shard)


def passed_along(value, axis, steps):
    count = lax.axis_size(axis)
    leading, last = (max(0, -steps), min(count, count - steps))
    return lax.ppermute(value, axis, [(source, source + steps) for source in range(leading, last)])


def depthwise(padded, tap_rows):
    return lax.conv_general_dilated(
        padded[None],
        tap_rows[:, None, :],
        (1,),
        "VALID",
        dimension_numbers=("NWC", "WIO", "NWC"),
        feature_group_count=padded.shape[1],
        precision=lax.Precision.HIGHEST,
    )[0]


def neighbor_rows(edge_rows, offset):
    return passed_along(as_sent(edge_rows), "ctx", offset).astype(edge_rows.dtype)


def butterfly_total(value, axis, sent_type=None):
    count = lax.axis_size(axis)
    if count & (count - 1):
        if sent_type is None:
            return lax.psum(value, axis)
        return lax.psum(value.astype(sent_type), axis).astype(value.dtype)
    step = 1
    while step < count:
        pairs = [(source, source ^ step) for source in range(count)]
        if sent_type is None:
            value = value + lax.ppermute(value, axis, pairs)
        else:
            rounded = value.astype(sent_type)
            value = rounded.astype(value.dtype) + lax.ppermute(rounded, axis, pairs).astype(value.dtype)
        step *= 2
    return value


def exchange_total(value, axis):
    count = lax.axis_size(axis)
    index = lax.axis_index(axis)
    stacked = jnp.zeros((count,) + value.shape, value.dtype)
    stacked = lax.dynamic_update_index_in_dim(stacked, value, index, 0)
    for shift in range(1, count):
        pairs = [(source, (source + shift) % count) for source in range(count)]
        arrived = lax.ppermute(value, axis, pairs)
        stacked = lax.dynamic_update_index_in_dim(stacked, arrived, (index - shift) % count, 0)
    return jnp.sum(stacked, axis=0)


def channel_total(partial_value):
    if lax.axis_size("tp") <= 4:
        return exchange_total(partial_value, "tp")
    return butterfly_total(partial_value, "tp")


def head_weights(scale_factor, query_head, key_head, visible):
    contract_last = (((1,), (1,)), ((), ()))
    scores = (
        lax.dot_general(query_head, key_head, contract_last, preferred_element_type=jnp.float32)
        * scale_factor
    )
    scores = jnp.where(visible, scores, -jnp.inf)
    row_max = jnp.max(scores, axis=1, keepdims=True)
    raised = jnp.exp(scores - row_max)
    return (raised * (1.0 / jnp.sum(raised, axis=1, keepdims=True))).astype(jnp.bfloat16)


def value_block(scale_factor, q_ref, k_ref, cot_ref, vis_ref, dv_ref, w_ref):
    contract_first = (((0,), (0,)), ((), ()))
    visible = vis_ref[...] > 0.5
    for head in range(w_ref.shape[0]):
        columns = slice(head * HD, (head + 1) * HD)
        weights = head_weights(scale_factor, q_ref[:, columns], k_ref[:, columns], visible)
        w_ref[head] = weights
        dv_ref[:, columns] = lax.dot_general(
            weights, cot_ref[:, columns], contract_first, preferred_element_type=jnp.float32
        ).astype(jnp.bfloat16)


def attention_block(scale_factor, q_ref, k_ref, v_ref, cot_ref, w_ref, dk_ref, att_ref, dq_ref):
    contract_last = (((1,), (1,)), ((), ()))
    contract_first = (((0,), (0,)), ((), ()))
    for head in range(w_ref.shape[0]):
        columns = slice(head * HD, (head + 1) * HD)
        query_head = q_ref[:, columns]
        key_head = k_ref[:, columns]
        value_head = v_ref[:, columns]
        cotangent_head = cot_ref[:, columns]
        weights = w_ref[head]
        attended = jnp.dot(weights, value_head, preferred_element_type=jnp.float32)
        weight_grad = lax.dot_general(
            cotangent_head, value_head, contract_last, preferred_element_type=jnp.float32
        )
        row_delta = jnp.sum(cotangent_head.astype(jnp.float32) * attended, axis=1, keepdims=True)
        dscore = (scale_factor * weights.astype(jnp.float32) * (weight_grad - row_delta)).astype(
            jnp.bfloat16
        )
        att_ref[:, columns] = attended
        dq_ref[:, columns] = jnp.dot(
            dscore, key_head, preferred_element_type=jnp.float32
        ).astype(jnp.bfloat16)
        dk_ref[:, columns] = lax.dot_general(
            dscore, query_head, contract_first, preferred_element_type=jnp.float32
        ).astype(jnp.bfloat16)


def head_specs(local_rows, total_rows, width_local):
    group = 2 if (width_local // HD) % 2 == 0 else 1
    local_spec = pl.BlockSpec((local_rows, group * HD), lambda h: (0, h))
    whole_spec = pl.BlockSpec((total_rows, group * HD), lambda h: (0, h))
    weight_spec = pl.BlockSpec((group, local_rows, total_rows), lambda h: (h, 0, 0))
    return local_spec, whole_spec, weight_spec, width_local // (group * HD)


def head_values_grad(queries, keys_whole, cotangent, visible, scale_factor):
    local_rows, width_local = queries.shape
    total_rows = keys_whole.shape[0]
    local_spec, whole_spec, weight_spec, steps = head_specs(local_rows, total_rows, width_local)
    mask_spec = pl.BlockSpec((local_rows, total_rows), lambda h: (0, 0))
    return pl.pallas_call(
        functools.partial(value_block, scale_factor),
        grid=(steps,),
        in_specs=[local_spec, whole_spec, local_spec, mask_spec],
        out_specs=[whole_spec, weight_spec],
        out_shape=[
            jax.ShapeDtypeStruct((total_rows, width_local), jnp.bfloat16),
            jax.ShapeDtypeStruct((width_local // HD, local_rows, total_rows), jnp.bfloat16),
        ],
    )(queries, keys_whole, cotangent, visible)


def head_attention(queries, keys_whole, values_whole, cotangent, weights, scale_factor):
    local_rows, width_local = queries.shape
    total_rows = keys_whole.shape[0]
    local_spec, whole_spec, weight_spec, steps = head_specs(local_rows, total_rows, width_local)
    return pl.pallas_call(
        functools.partial(attention_block, scale_factor),
        grid=(steps,),
        in_specs=[local_spec, whole_spec, whole_spec, local_spec, weight_spec],
        out_specs=[whole_spec, local_spec, local_spec],
        out_shape=[
            jax.ShapeDtypeStruct((total_rows, width_local), jnp.bfloat16),
            jax.ShapeDtypeStruct((local_rows, width_local), jnp.float32),
            jax.ShapeDtypeStruct((local_rows, width_local), jnp.bfloat16),
        ],
    )(queries, keys_whole, values_whole, cotangent, weights)


def shards(
    stream,
    shutter,
    feeder,
    stencil,
    valves,
    intake,
    kernel,
    scaling,
    queries,
    matchers,
    segments,
    cotangent,
):
    local_rows = stream.shape[0]
    width_local = stream.shape[1]
    head_count = width_local // HD
    total_rows = local_rows * lax.axis_size("ctx")
    position = lax.axis_index("ctx") * local_rows
    scale_factor = 1.0 / math.sqrt(HD)
    widened = stream.astype(jnp.float32)
    inner_one = feeder.astype(jnp.float32) * widened
    rim_one = neighbor_rows(inner_one[local_rows - (KS - 1) :], 1)
    padded_one = jnp.concatenate([rim_one, inner_one], axis=0)
    conv_one = depthwise(padded_one, stencil[::-1])
    first_out = (widened + shutter.astype(jnp.float32) * conv_one).astype(jnp.bfloat16)
    first_wide = first_out.astype(jnp.float32)
    inner_two = intake.astype(jnp.float32) * first_wide
    rim_two = neighbor_rows(inner_two[local_rows - (KM - 1) :], 1)
    padded_two = jnp.concatenate([rim_two, inner_two], axis=0)
    conv_two = depthwise(padded_two, kernel[::-1])
    second_out = (first_wide + valves.astype(jnp.float32) * conv_two).astype(jnp.bfloat16)
    second_wide = second_out.astype(jnp.float32)
    squares = channel_total(jnp.sum(second_wide * second_wide, axis=1))
    inverse_rms = lax.rsqrt(squares / D + epsilon)
    normed = (second_wide * inverse_rms[:, None] * scaling).astype(jnp.bfloat16)
    ctx_count = lax.axis_size("ctx")
    ctx_index = lax.axis_index("ctx")
    keys_whole = lax.all_to_all(
        jnp.tile(matchers, (ctx_count, 1)), "ctx", 0, 0, tiled=True
    )
    reach = min(ctx_count - 1, (3 * total_rows // 4 - 1 + local_rows - 1) // local_rows)
    query_pos = position + jnp.arange(local_rows, dtype=jnp.int32)
    key_pos = jnp.arange(total_rows, dtype=jnp.int32)
    query_seg = lax.dynamic_slice_in_dim(segments, position, local_rows, 0)
    visible = (key_pos[None, :] <= query_pos[:, None]) & (segments[None, :] == query_seg[:, None])
    mask = visible.astype(jnp.float32)
    value_part, weights_all = head_values_grad(queries, keys_whole, cotangent, mask, scale_factor)
    value_grad = (
        lax.all_to_all(value_part, "ctx", 0, 0, tiled=True)
        .reshape(ctx_count, local_rows, width_local)
        .astype(jnp.float32)
        .sum(axis=0)
    )
    values_whole = lax.all_gather(normed, "ctx", axis=0, tiled=True)
    key_part, attended_all, queries_grad = head_attention(
        queries, keys_whole, values_whole, cotangent, weights_all, scale_factor
    )
    result = (second_wide + attended_all).astype(jnp.bfloat16)
    key_part, value_grad = lax.optimization_barrier((key_part, value_grad))
    matchers_grad = lax.psum_scatter(
        key_part,
        "ctx",
        scatter_dimension=0,
        tiled=True,
    )
    gain_part = value_grad * scaling
    projected = channel_total(jnp.sum(gain_part * second_wide, axis=1))
    scaling_part = jnp.sum(value_grad * second_wide * inverse_rms[:, None], axis=0)
    second_grad = (
        cotangent.astype(jnp.float32)
        + inverse_rms[:, None] * gain_part
        - second_wide * (inverse_rms**3 * projected / D)[:, None]
    )
    valves_grad = (second_grad * conv_two).astype(jnp.bfloat16)
    dconv_two = second_grad * valves.astype(jnp.float32)
    back_two = neighbor_rows(dconv_two[: KM - 1], -1)
    dinner_two = depthwise(jnp.concatenate([dconv_two, back_two], axis=0), kernel)
    intake_grad = (dinner_two * first_wide).astype(jnp.bfloat16)
    kernel_part = depthwise(padded_two, dconv_two)[::-1]
    first_grad = second_grad + dinner_two * intake.astype(jnp.float32)
    shutter_grad = (first_grad * conv_one).astype(jnp.bfloat16)
    dconv_one = first_grad * shutter.astype(jnp.float32)
    back_one = neighbor_rows(dconv_one[: KS - 1], -1)
    dinner_one = depthwise(jnp.concatenate([dconv_one, back_one], axis=0), stencil)
    feeder_grad = (dinner_one * widened).astype(jnp.bfloat16)
    stencil_part = depthwise(padded_one, dconv_one)[::-1]
    stream_grad = (first_grad + dinner_one * feeder.astype(jnp.float32)).astype(jnp.bfloat16)
    filter_sum = butterfly_total(
        jnp.concatenate([kernel_part, scaling_part[None], stencil_part], axis=0), "ctx", jnp.bfloat16
    )
    kernel_sum = filter_sum[:KM]
    scaling_sum = filter_sum[KM]
    stencil_sum = filter_sum[KM + 1 :]
    normalizer = math.sqrt(total_rows)
    return (
        result,
        stream_grad,
        shutter_grad,
        feeder_grad,
        stencil_sum / normalizer,
        valves_grad,
        intake_grad,
        kernel_sum / normalizer,
        scaling_sum / normalizer,
        queries_grad,
        matchers_grad,
    )


def solution(mesh):
    placed = (
        P("ctx", "tp"),
        P("ctx", "tp"),
        P("ctx", "tp"),
        P(None, "tp"),
        P("ctx", "tp"),
        P("ctx", "tp"),
        P(None, "tp"),
        P("tp"),
        P("ctx", "tp"),
        P("ctx", "tp"),
        P(),
        P("ctx", "tp"),
    )
    return jax.shard_map(
        shards,
        mesh=mesh,
        in_specs=placed,
        out_specs=(
            P("ctx", "tp"),
            P("ctx", "tp"),
            P("ctx", "tp"),
            P("ctx", "tp"),
            P(None, "tp"),
            P("ctx", "tp"),
            P("ctx", "tp"),
            P(None, "tp"),
            P("tp"),
            P("ctx", "tp"),
            P("ctx", "tp"),
        ),
        check_vma=False,
    )
```

```python
import functools
import math

import jax
import jax.numpy as jnp
from jax import lax
from jax.experimental import pallas as pl
from jax.sharding import PartitionSpec as P

HD = 128
D = 4096
KS = 7
KM = 128


epsilon = 1e-06


def as_sent(shard):

    def short(part):
        return part.astype(jnp.bfloat16) if part.dtype == jnp.float32 else part

    return jax.tree.map(short, shard)


def passed_along(value, axis, steps):
    count = lax.axis_size(axis)
    leading, last = (max(0, -steps), min(count, count - steps))
    return lax.ppermute(value, axis, [(source, source + steps) for source in range(leading, last)])


def depthwise(padded, tap_rows):
    return lax.conv_general_dilated(
        padded[None],
        tap_rows[:, None, :],
        (1,),
        "VALID",
        dimension_numbers=("NWC", "WIO", "NWC"),
        feature_group_count=padded.shape[1],
        precision=lax.Precision.HIGHEST,
    )[0]


def neighbor_rows(edge_rows, offset):
    return passed_along(as_sent(edge_rows), "ctx", offset).astype(edge_rows.dtype)


def butterfly_total(value, axis, sent_type=None):
    count = lax.axis_size(axis)
    if count & (count - 1):
        if sent_type is None:
            return lax.psum(value, axis)
        return lax.psum(value.astype(sent_type), axis).astype(value.dtype)
    step = 1
    while step < count:
        pairs = [(source, source ^ step) for source in range(count)]
        if sent_type is None:
            value = value + lax.ppermute(value, axis, pairs)
        else:
            rounded = value.astype(sent_type)
            value = rounded.astype(value.dtype) + lax.ppermute(rounded, axis, pairs).astype(value.dtype)
        step *= 2
    return value


def exchange_total(value, axis):
    count = lax.axis_size(axis)
    index = lax.axis_index(axis)
    stacked = jnp.zeros((count,) + value.shape, value.dtype)
    stacked = lax.dynamic_update_index_in_dim(stacked, value, index, 0)
    for shift in range(1, count):
        pairs = [(source, (source + shift) % count) for source in range(count)]
        arrived = lax.ppermute(value, axis, pairs)
        stacked = lax.dynamic_update_index_in_dim(stacked, arrived, (index - shift) % count, 0)
    return jnp.sum(stacked, axis=0)


def channel_total(partial_value):
    if lax.axis_size("tp") <= 4:
        return exchange_total(partial_value, "tp")
    return butterfly_total(partial_value, "tp")


def head_weights(scale_factor, query_head, key_head, visible):
    contract_last = (((1,), (1,)), ((), ()))
    scores = (
        lax.dot_general(query_head, key_head, contract_last, preferred_element_type=jnp.float32)
        * scale_factor
    )
    scores = jnp.where(visible, scores, -jnp.inf)
    row_max = jnp.max(scores, axis=1, keepdims=True)
    raised = jnp.exp(scores - row_max)
    return (raised * (1.0 / jnp.sum(raised, axis=1, keepdims=True))).astype(jnp.bfloat16)


def value_block(scale_factor, q_ref, k_ref, cot_ref, vis_ref, dv_ref, w_ref):
    contract_first = (((0,), (0,)), ((), ()))
    visible = vis_ref[...] > 0.5
    for head in range(w_ref.shape[0]):
        columns = slice(head * HD, (head + 1) * HD)
        weights = head_weights(scale_factor, q_ref[:, columns], k_ref[:, columns], visible)
        w_ref[head] = weights
        dv_ref[:, columns] = lax.dot_general(
            weights, cot_ref[:, columns], contract_first, preferred_element_type=jnp.float32
        ).astype(jnp.bfloat16)


def attention_block(scale_factor, q_ref, k_ref, v_ref, cot_ref, w_ref, dk_ref, att_ref, dq_ref):
    contract_last = (((1,), (1,)), ((), ()))
    contract_first = (((0,), (0,)), ((), ()))
    for head in range(w_ref.shape[0]):
        columns = slice(head * HD, (head + 1) * HD)
        query_head = q_ref[:, columns]
        key_head = k_ref[:, columns]
        value_head = v_ref[:, columns]
        cotangent_head = cot_ref[:, columns]
        weights = w_ref[head]
        attended = jnp.dot(weights, value_head, preferred_element_type=jnp.float32)
        weight_grad = lax.dot_general(
            cotangent_head, value_head, contract_last, preferred_element_type=jnp.float32
        )
        row_delta = jnp.sum(cotangent_head.astype(jnp.float32) * attended, axis=1, keepdims=True)
        dscore = (scale_factor * weights.astype(jnp.float32) * (weight_grad - row_delta)).astype(
            jnp.bfloat16
        )
        att_ref[:, columns] = attended
        dq_ref[:, columns] = jnp.dot(
            dscore, key_head, preferred_element_type=jnp.float32
        ).astype(jnp.bfloat16)
        dk_ref[:, columns] = lax.dot_general(
            dscore, query_head, contract_first, preferred_element_type=jnp.float32
        ).astype(jnp.bfloat16)


def head_specs(local_rows, total_rows, width_local):
    group = 2 if (width_local // HD) % 2 == 0 else 1
    local_spec = pl.BlockSpec((local_rows, group * HD), lambda h: (0, h))
    whole_spec = pl.BlockSpec((total_rows, group * HD), lambda h: (0, h))
    weight_spec = pl.BlockSpec((group, local_rows, total_rows), lambda h: (h, 0, 0))
    return local_spec, whole_spec, weight_spec, width_local // (group * HD)


def head_values_grad(queries, keys_whole, cotangent, visible, scale_factor):
    local_rows, width_local = queries.shape
    total_rows = keys_whole.shape[0]
    local_spec, whole_spec, weight_spec, steps = head_specs(local_rows, total_rows, width_local)
    mask_spec = pl.BlockSpec((local_rows, total_rows), lambda h: (0, 0))
    return pl.pallas_call(
        functools.partial(value_block, scale_factor),
        grid=(steps,),
        in_specs=[local_spec, whole_spec, local_spec, mask_spec],
        out_specs=[whole_spec, weight_spec],
        out_shape=[
            jax.ShapeDtypeStruct((total_rows, width_local), jnp.bfloat16),
            jax.ShapeDtypeStruct((width_local // HD, local_rows, total_rows), jnp.bfloat16),
        ],
    )(queries, keys_whole, cotangent, visible)


def head_attention(queries, keys_whole, values_whole, cotangent, weights, scale_factor):
    local_rows, width_local = queries.shape
    total_rows = keys_whole.shape[0]
    local_spec, whole_spec, weight_spec, steps = head_specs(local_rows, total_rows, width_local)
    return pl.pallas_call(
        functools.partial(attention_block, scale_factor),
        grid=(steps,),
        in_specs=[local_spec, whole_spec, whole_spec, local_spec, weight_spec],
        out_specs=[whole_spec, local_spec, local_spec],
        out_shape=[
            jax.ShapeDtypeStruct((total_rows, width_local), jnp.bfloat16),
            jax.ShapeDtypeStruct((local_rows, width_local), jnp.float32),
            jax.ShapeDtypeStruct((local_rows, width_local), jnp.bfloat16),
        ],
    )(queries, keys_whole, values_whole, cotangent, weights)


def shards(
    stream,
    shutter,
    feeder,
    stencil,
    valves,
    intake,
    kernel,
    scaling,
    queries,
    matchers,
    segments,
    cotangent,
):
    local_rows = stream.shape[0]
    width_local = stream.shape[1]
    head_count = width_local // HD
    total_rows = local_rows * lax.axis_size("ctx")
    position = lax.axis_index("ctx") * local_rows
    scale_factor = 1.0 / math.sqrt(HD)
    widened = stream.astype(jnp.float32)
    inner_one = feeder.astype(jnp.float32) * widened
    rim_one = neighbor_rows(inner_one[local_rows - (KS - 1) :], 1)
    padded_one = jnp.concatenate([rim_one, inner_one], axis=0)
    conv_one = depthwise(padded_one, stencil[::-1])
    first_out = (widened + shutter.astype(jnp.float32) * conv_one).astype(jnp.bfloat16)
    first_wide = first_out.astype(jnp.float32)
    inner_two = intake.astype(jnp.float32) * first_wide
    rim_two = neighbor_rows(inner_two[local_rows - (KM - 1) :], 1)
    padded_two = jnp.concatenate([rim_two, inner_two], axis=0)
    conv_two = depthwise(padded_two, kernel[::-1])
    second_out = (first_wide + valves.astype(jnp.float32) * conv_two).astype(jnp.bfloat16)
    second_wide = second_out.astype(jnp.float32)
    squares = channel_total(jnp.sum(second_wide * second_wide, axis=1))
    inverse_rms = lax.rsqrt(squares / D + epsilon)
    normed = (second_wide * inverse_rms[:, None] * scaling).astype(jnp.bfloat16)
    ctx_count = lax.axis_size("ctx")
    ctx_index = lax.axis_index("ctx")
    keys_whole = lax.all_gather(matchers, "ctx", axis=0, tiled=True)
    reach = min(ctx_count - 1, (3 * total_rows // 4 - 1 + local_rows - 1) // local_rows)
    query_pos = position + jnp.arange(local_rows, dtype=jnp.int32)
    key_pos = jnp.arange(total_rows, dtype=jnp.int32)
    query_seg = lax.dynamic_slice_in_dim(segments, position, local_rows, 0)
    visible = (key_pos[None, :] <= query_pos[:, None]) & (segments[None, :] == query_seg[:, None])
    mask = visible.astype(jnp.float32)
    value_part, weights_all = head_values_grad(queries, keys_whole, cotangent, mask, scale_factor)
    values_whole = lax.all_gather(normed, "ctx", axis=0, tiled=True)
    value_part, values_whole = lax.optimization_barrier((value_part, values_whole))
    value_grad = (
        lax.all_to_all(value_part, "ctx", 0, 0, tiled=True)
        .reshape(ctx_count, local_rows, width_local)
        .astype(jnp.float32)
        .sum(axis=0)
    )
    key_part, attended_all, queries_grad = head_attention(
        queries, keys_whole, values_whole, cotangent, weights_all, scale_factor
    )
    result = (second_wide + attended_all).astype(jnp.bfloat16)
    key_part, value_grad = lax.optimization_barrier((key_part, value_grad))
    matchers_grad = lax.psum_scatter(
        key_part,
        "ctx",
        scatter_dimension=0,
        tiled=True,
    )
    gain_part = value_grad * scaling
    projected = channel_total(jnp.sum(gain_part * second_wide, axis=1))
    scaling_part = jnp.sum(value_grad * second_wide * inverse_rms[:, None], axis=0)
    second_grad = (
        cotangent.astype(jnp.float32)
        + inverse_rms[:, None] * gain_part
        - second_wide * (inverse_rms**3 * projected / D)[:, None]
    )
    valves_grad = (second_grad * conv_two).astype(jnp.bfloat16)
    dconv_two = second_grad * valves.astype(jnp.float32)
    back_two = neighbor_rows(dconv_two[: KM - 1], -1)
    dinner_two = depthwise(jnp.concatenate([dconv_two, back_two], axis=0), kernel)
    intake_grad = (dinner_two * first_wide).astype(jnp.bfloat16)
    kernel_part = depthwise(padded_two, dconv_two)[::-1]
    first_grad = second_grad + dinner_two * intake.astype(jnp.float32)
    shutter_grad = (first_grad * conv_one).astype(jnp.bfloat16)
    dconv_one = first_grad * shutter.astype(jnp.float32)
    back_one = neighbor_rows(dconv_one[: KS - 1], -1)
    dinner_one = depthwise(jnp.concatenate([dconv_one, back_one], axis=0), stencil)
    feeder_grad = (dinner_one * widened).astype(jnp.bfloat16)
    stencil_part = depthwise(padded_one, dconv_one)[::-1]
    stream_grad = (first_grad + dinner_one * feeder.astype(jnp.float32)).astype(jnp.bfloat16)
    filter_sum = butterfly_total(
        jnp.concatenate([kernel_part, scaling_part[None], stencil_part], axis=0), "ctx", jnp.bfloat16
    )
    kernel_sum = filter_sum[:KM]
    scaling_sum = filter_sum[KM]
    stencil_sum = filter_sum[KM + 1 :]
    normalizer = math.sqrt(total_rows)
    return (
        result,
        stream_grad,
        shutter_grad,
        feeder_grad,
        stencil_sum / normalizer,
        valves_grad,
        intake_grad,
        kernel_sum / normalizer,
        scaling_sum / normalizer,
        queries_grad,
        matchers_grad,
    )


def solution(mesh):
    placed = (
        P("ctx", "tp"),
        P("ctx", "tp"),
        P("ctx", "tp"),
        P(None, "tp"),
        P("ctx", "tp"),
        P("ctx", "tp"),
        P(None, "tp"),
        P("tp"),
        P("ctx", "tp"),
        P("ctx", "tp"),
        P(),
        P("ctx", "tp"),
    )
    return jax.shard_map(
        shards,
        mesh=mesh,
        in_specs=placed,
        out_specs=(
            P("ctx", "tp"),
            P("ctx", "tp"),
            P("ctx", "tp"),
            P("ctx", "tp"),
            P(None, "tp"),
            P("ctx", "tp"),
            P("ctx", "tp"),
            P(None, "tp"),
            P("tp"),
            P("ctx", "tp"),
            P("ctx", "tp"),
        ),
        check_vma=False,
    )
```

```python
import functools
import math

import jax
import jax.numpy as jnp
from jax import lax
from jax.experimental import pallas as pl
from jax.sharding import PartitionSpec as P

HD = 128
D = 4096
KS = 7
KM = 128


epsilon = 1e-06


def as_sent(shard):

    def short(part):
        return part.astype(jnp.bfloat16) if part.dtype == jnp.float32 else part

    return jax.tree.map(short, shard)


def passed_along(value, axis, steps):
    count = lax.axis_size(axis)
    leading, last = (max(0, -steps), min(count, count - steps))
    return lax.ppermute(value, axis, [(source, source + steps) for source in range(leading, last)])


def depthwise(padded, tap_rows):
    return lax.conv_general_dilated(
        padded[None],
        tap_rows[:, None, :],
        (1,),
        "VALID",
        dimension_numbers=("NWC", "WIO", "NWC"),
        feature_group_count=padded.shape[1],
        precision=lax.Precision.HIGHEST,
    )[0]


def neighbor_rows(edge_rows, offset):
    return passed_along(as_sent(edge_rows), "ctx", offset).astype(edge_rows.dtype)


def butterfly_total(value, axis, sent_type=None):
    count = lax.axis_size(axis)
    if count & (count - 1):
        if sent_type is None:
            return lax.psum(value, axis)
        return lax.psum(value.astype(sent_type), axis).astype(value.dtype)
    step = 1
    while step < count:
        pairs = [(source, source ^ step) for source in range(count)]
        if sent_type is None:
            value = value + lax.ppermute(value, axis, pairs)
        else:
            rounded = value.astype(sent_type)
            value = rounded.astype(value.dtype) + lax.ppermute(rounded, axis, pairs).astype(value.dtype)
        step *= 2
    return value


def exchange_total(value, axis):
    count = lax.axis_size(axis)
    index = lax.axis_index(axis)
    stacked = jnp.zeros((count,) + value.shape, value.dtype)
    stacked = lax.dynamic_update_index_in_dim(stacked, value, index, 0)
    for shift in range(1, count):
        pairs = [(source, (source + shift) % count) for source in range(count)]
        arrived = lax.ppermute(value, axis, pairs)
        stacked = lax.dynamic_update_index_in_dim(stacked, arrived, (index - shift) % count, 0)
    return jnp.sum(stacked, axis=0)


def channel_total(partial_value):
    if lax.axis_size("tp") <= 4:
        return exchange_total(partial_value, "tp")
    return butterfly_total(partial_value, "tp")


def head_weights(scale_factor, query_head, key_head, visible):
    contract_last = (((1,), (1,)), ((), ()))
    scores = (
        lax.dot_general(query_head, key_head, contract_last, preferred_element_type=jnp.float32)
        * scale_factor
    )
    scores = jnp.where(visible > 0.5, scores, -jnp.inf)
    row_max = jnp.max(scores, axis=1, keepdims=True)
    logsum = row_max + jnp.log(jnp.sum(jnp.exp(scores - row_max), axis=1, keepdims=True))
    return jnp.exp(scores - logsum).astype(jnp.bfloat16)


def value_block(scale_factor, q_ref, k_ref, cot_ref, vis_ref, dv_ref):
    contract_first = (((0,), (0,)), ((), ()))
    weights = head_weights(scale_factor, q_ref[...], k_ref[...], vis_ref[...])
    dv_ref[...] = lax.dot_general(
        weights, cot_ref[...], contract_first, preferred_element_type=jnp.float32
    ).astype(jnp.bfloat16)


def attention_block(scale_factor, q_ref, k_ref, v_ref, cot_ref, vis_ref, dk_ref, att_ref, dq_ref):
    contract_last = (((1,), (1,)), ((), ()))
    contract_first = (((0,), (0,)), ((), ()))
    query_head = q_ref[...]
    key_head = k_ref[...]
    value_head = v_ref[...]
    cotangent_head = cot_ref[...]
    weights = head_weights(scale_factor, query_head, key_head, vis_ref[...])
    attended = jnp.dot(weights, value_head, preferred_element_type=jnp.float32)
    weight_grad = lax.dot_general(
        cotangent_head, value_head, contract_last, preferred_element_type=jnp.float32
    )
    row_delta = jnp.sum(cotangent_head.astype(jnp.float32) * attended, axis=1, keepdims=True)
    dscore = (scale_factor * weights.astype(jnp.float32) * (weight_grad - row_delta)).astype(
        jnp.bfloat16
    )
    att_ref[...] = attended
    dq_ref[...] = jnp.dot(dscore, key_head, preferred_element_type=jnp.float32).astype(jnp.bfloat16)
    dk_ref[...] = lax.dot_general(
        dscore, query_head, contract_first, preferred_element_type=jnp.float32
    ).astype(jnp.bfloat16)


def head_specs(local_rows, total_rows):
    local_spec = pl.BlockSpec((local_rows, HD), lambda h: (0, h))
    whole_spec = pl.BlockSpec((total_rows, HD), lambda h: (0, h))
    mask_spec = pl.BlockSpec((local_rows, total_rows), lambda h: (0, 0))
    return local_spec, whole_spec, mask_spec


def head_values_grad(queries, keys_whole, cotangent, visible, scale_factor):
    local_rows, width_local = queries.shape
    total_rows = keys_whole.shape[0]
    local_spec, whole_spec, mask_spec = head_specs(local_rows, total_rows)
    return pl.pallas_call(
        functools.partial(value_block, scale_factor),
        grid=(width_local // HD,),
        in_specs=[local_spec, whole_spec, local_spec, mask_spec],
        out_specs=whole_spec,
        out_shape=jax.ShapeDtypeStruct((total_rows, width_local), jnp.bfloat16),
    )(queries, keys_whole, cotangent, visible)


def head_attention(queries, keys_whole, values_whole, cotangent, visible, scale_factor):
    local_rows, width_local = queries.shape
    total_rows = keys_whole.shape[0]
    local_spec, whole_spec, mask_spec = head_specs(local_rows, total_rows)
    return pl.pallas_call(
        functools.partial(attention_block, scale_factor),
        grid=(width_local // HD,),
        in_specs=[local_spec, whole_spec, whole_spec, local_spec, mask_spec],
        out_specs=[whole_spec, local_spec, local_spec],
        out_shape=[
            jax.ShapeDtypeStruct((total_rows, width_local), jnp.bfloat16),
            jax.ShapeDtypeStruct((local_rows, width_local), jnp.float32),
            jax.ShapeDtypeStruct((local_rows, width_local), jnp.bfloat16),
        ],
    )(queries, keys_whole, values_whole, cotangent, visible)


def shards(
    stream,
    shutter,
    feeder,
    stencil,
    valves,
    intake,
    kernel,
    scaling,
    queries,
    matchers,
    segments,
    cotangent,
):
    local_rows = stream.shape[0]
    width_local = stream.shape[1]
    head_count = width_local // HD
    total_rows = local_rows * lax.axis_size("ctx")
    position = lax.axis_index("ctx") * local_rows
    scale_factor = 1.0 / math.sqrt(HD)
    widened = stream.astype(jnp.float32)
    inner_one = feeder.astype(jnp.float32) * widened
    rim_one = neighbor_rows(inner_one[local_rows - (KS - 1) :], 1)
    padded_one = jnp.concatenate([rim_one, inner_one], axis=0)
    conv_one = depthwise(padded_one, stencil[::-1])
    first_out = (widened + shutter.astype(jnp.float32) * conv_one).astype(jnp.bfloat16)
    first_wide = first_out.astype(jnp.float32)
    inner_two = intake.astype(jnp.float32) * first_wide
    rim_two = neighbor_rows(inner_two[local_rows - (KM - 1) :], 1)
    padded_two = jnp.concatenate([rim_two, inner_two], axis=0)
    conv_two = depthwise(padded_two, kernel[::-1])
    second_out = (first_wide + valves.astype(jnp.float32) * conv_two).astype(jnp.bfloat16)
    second_wide = second_out.astype(jnp.float32)
    squares = channel_total(jnp.sum(second_wide * second_wide, axis=1))
    inverse_rms = lax.rsqrt(squares / D + epsilon)
    normed = (second_wide * inverse_rms[:, None] * scaling).astype(jnp.bfloat16)
    ctx_count = lax.axis_size("ctx")
    ctx_index = lax.axis_index("ctx")
    keys_whole = lax.all_gather(matchers, "ctx", axis=0, tiled=True)
    reach = min(ctx_count - 1, (3 * total_rows // 4 - 1 + local_rows - 1) // local_rows)
    query_pos = position + jnp.arange(local_rows, dtype=jnp.int32)
    key_pos = jnp.arange(total_rows, dtype=jnp.int32)
    query_seg = lax.dynamic_slice_in_dim(segments, position, local_rows, 0)
    visible = (key_pos[None, :] <= query_pos[:, None]) & (segments[None, :] == query_seg[:, None])
    mask = visible.astype(jnp.float32)
    value_part = head_values_grad(queries, keys_whole, cotangent, mask, scale_factor)
    value_grad = (
        lax.all_to_all(value_part, "ctx", 0, 0, tiled=True)
        .reshape(ctx_count, local_rows, width_local)
        .astype(jnp.float32)
        .sum(axis=0)
    )
    values_whole = lax.all_gather(normed, "ctx", axis=0, tiled=True)
    key_part, attended_all, queries_grad = head_attention(
        queries, keys_whole, values_whole, cotangent, mask, scale_factor
    )
    result = (second_wide + attended_all).astype(jnp.bfloat16)
    key_part, value_grad = lax.optimization_barrier((key_part, value_grad))
    matchers_grad = (
        lax.all_to_all(key_part, "ctx", 0, 0, tiled=True)
        .reshape(ctx_count, local_rows, width_local)
        .astype(jnp.float32)
        .sum(axis=0)
        .astype(jnp.bfloat16)
    )
    gain_part = value_grad * scaling
    projected = channel_total(jnp.sum(gain_part * second_wide, axis=1))
    scaling_part = jnp.sum(value_grad * second_wide * inverse_rms[:, None], axis=0)
    second_grad = (
        cotangent.astype(jnp.float32)
        + inverse_rms[:, None] * gain_part
        - second_wide * (inverse_rms**3 * projected / D)[:, None]
    )
    valves_grad = (second_grad * conv_two).astype(jnp.bfloat16)
    dconv_two = second_grad * valves.astype(jnp.float32)
    back_two = neighbor_rows(dconv_two[: KM - 1], -1)
    dinner_two = depthwise(jnp.concatenate([dconv_two, back_two], axis=0), kernel)
    intake_grad = (dinner_two * first_wide).astype(jnp.bfloat16)
    kernel_part = depthwise(padded_two, dconv_two)[::-1]
    first_grad = second_grad + dinner_two * intake.astype(jnp.float32)
    matchers_grad, first_grad = lax.optimization_barrier((matchers_grad, first_grad))
    shutter_grad = (first_grad * conv_one).astype(jnp.bfloat16)
    dconv_one = first_grad * shutter.astype(jnp.float32)
    back_one = neighbor_rows(dconv_one[: KS - 1], -1)
    dinner_one = depthwise(jnp.concatenate([dconv_one, back_one], axis=0), stencil)
    feeder_grad = (dinner_one * widened).astype(jnp.bfloat16)
    stencil_part = depthwise(padded_one, dconv_one)[::-1]
    stream_grad = (first_grad + dinner_one * feeder.astype(jnp.float32)).astype(jnp.bfloat16)
    filter_sum = butterfly_total(
        jnp.concatenate([kernel_part, scaling_part[None], stencil_part], axis=0), "ctx", jnp.bfloat16
    )
    kernel_sum = filter_sum[:KM]
    scaling_sum = filter_sum[KM]
    stencil_sum = filter_sum[KM + 1 :]
    normalizer = math.sqrt(total_rows)
    return (
        result,
        stream_grad,
        shutter_grad,
        feeder_grad,
        stencil_sum / normalizer,
        valves_grad,
        intake_grad,
        kernel_sum / normalizer,
        scaling_sum / normalizer,
        queries_grad,
        matchers_grad,
    )


def solution(mesh):
    placed = (
        P("ctx", "tp"),
        P("ctx", "tp"),
        P("ctx", "tp"),
        P(None, "tp"),
        P("ctx", "tp"),
        P("ctx", "tp"),
        P(None, "tp"),
        P("tp"),
        P("ctx", "tp"),
        P("ctx", "tp"),
        P(),
        P("ctx", "tp"),
    )
    return jax.shard_map(
        shards,
        mesh=mesh,
        in_specs=placed,
        out_specs=(
            P("ctx", "tp"),
            P("ctx", "tp"),
            P("ctx", "tp"),
            P("ctx", "tp"),
            P(None, "tp"),
            P("ctx", "tp"),
            P("ctx", "tp"),
            P(None, "tp"),
            P("tp"),
            P("ctx", "tp"),
            P("ctx", "tp"),
        ),
        check_vma=False,
    )
```

```python
import functools
import math

import jax
import jax.numpy as jnp
from jax import lax
from jax.experimental import pallas as pl
from jax.sharding import PartitionSpec as P

HD = 128
D = 4096
KS = 7
KM = 128


epsilon = 1e-06


def as_sent(shard):

    def short(part):
        return part.astype(jnp.bfloat16) if part.dtype == jnp.float32 else part

    return jax.tree.map(short, shard)


def passed_along(value, axis, steps):
    count = lax.axis_size(axis)
    leading, last = (max(0, -steps), min(count, count - steps))
    return lax.ppermute(value, axis, [(source, source + steps) for source in range(leading, last)])


def depthwise(padded, tap_rows):
    return lax.conv_general_dilated(
        padded[None],
        tap_rows[:, None, :],
        (1,),
        "VALID",
        dimension_numbers=("NWC", "WIO", "NWC"),
        feature_group_count=padded.shape[1],
        precision=lax.Precision.HIGHEST,
    )[0]


def neighbor_rows(edge_rows, offset):
    return passed_along(as_sent(edge_rows), "ctx", offset).astype(edge_rows.dtype)


def butterfly_total(value, axis, sent_type=None):
    count = lax.axis_size(axis)
    if count & (count - 1):
        if sent_type is None:
            return lax.psum(value, axis)
        return lax.psum(value.astype(sent_type), axis).astype(value.dtype)
    step = 1
    while step < count:
        pairs = [(source, source ^ step) for source in range(count)]
        if sent_type is None:
            value = value + lax.ppermute(value, axis, pairs)
        else:
            rounded = value.astype(sent_type)
            value = rounded.astype(value.dtype) + lax.ppermute(rounded, axis, pairs).astype(value.dtype)
        step *= 2
    return value


def exchange_total(value, axis):
    count = lax.axis_size(axis)
    index = lax.axis_index(axis)
    stacked = jnp.zeros((count,) + value.shape, value.dtype)
    stacked = lax.dynamic_update_index_in_dim(stacked, value, index, 0)
    for shift in range(1, count):
        pairs = [(source, (source + shift) % count) for source in range(count)]
        arrived = lax.ppermute(value, axis, pairs)
        stacked = lax.dynamic_update_index_in_dim(stacked, arrived, (index - shift) % count, 0)
    return jnp.sum(stacked.astype(jnp.float32), axis=0)


def channel_total(partial_value):
    if lax.axis_size("tp") <= 4:
        return exchange_total(partial_value, "tp")
    return butterfly_total(partial_value, "tp")


def head_weights(scale_factor, query_head, key_head, visible):
    contract_last = (((1,), (1,)), ((), ()))
    scores = (
        lax.dot_general(query_head, key_head, contract_last, preferred_element_type=jnp.float32)
        * scale_factor
    )
    scores = jnp.where(visible > 0.5, scores, -jnp.inf)
    row_max = jnp.max(scores, axis=1, keepdims=True)
    logsum = row_max + jnp.log(jnp.sum(jnp.exp(scores - row_max), axis=1, keepdims=True))
    return jnp.exp(scores - logsum).astype(jnp.bfloat16)


def value_block(scale_factor, q_ref, k_ref, cot_ref, vis_ref, dv_ref):
    contract_first = (((0,), (0,)), ((), ()))
    weights = head_weights(scale_factor, q_ref[...], k_ref[...], vis_ref[...])
    dv_ref[...] = lax.dot_general(
        weights, cot_ref[...], contract_first, preferred_element_type=jnp.float32
    ).astype(jnp.bfloat16)


def attention_block(scale_factor, q_ref, k_ref, v_ref, cot_ref, vis_ref, dk_ref, att_ref, dq_ref):
    contract_last = (((1,), (1,)), ((), ()))
    contract_first = (((0,), (0,)), ((), ()))
    query_head = q_ref[...]
    key_head = k_ref[...]
    value_head = v_ref[...]
    cotangent_head = cot_ref[...]
    weights = head_weights(scale_factor, query_head, key_head, vis_ref[...])
    attended = jnp.dot(weights, value_head, preferred_element_type=jnp.float32)
    weight_grad = lax.dot_general(
        cotangent_head, value_head, contract_last, preferred_element_type=jnp.float32
    )
    row_delta = jnp.sum(cotangent_head.astype(jnp.float32) * attended, axis=1, keepdims=True)
    dscore = (scale_factor * weights.astype(jnp.float32) * (weight_grad - row_delta)).astype(
        jnp.bfloat16
    )
    att_ref[...] = attended
    dq_ref[...] = jnp.dot(dscore, key_head, preferred_element_type=jnp.float32).astype(jnp.bfloat16)
    dk_ref[...] = lax.dot_general(
        dscore, query_head, contract_first, preferred_element_type=jnp.float32
    ).astype(jnp.bfloat16)


def head_specs(local_rows, total_rows):
    local_spec = pl.BlockSpec((local_rows, HD), lambda h: (0, h))
    whole_spec = pl.BlockSpec((total_rows, HD), lambda h: (0, h))
    mask_spec = pl.BlockSpec((local_rows, total_rows), lambda h: (0, 0))
    return local_spec, whole_spec, mask_spec


def head_values_grad(queries, keys_whole, cotangent, visible, scale_factor):
    local_rows, width_local = queries.shape
    total_rows = keys_whole.shape[0]
    local_spec, whole_spec, mask_spec = head_specs(local_rows, total_rows)
    return pl.pallas_call(
        functools.partial(value_block, scale_factor),
        grid=(width_local // HD,),
        in_specs=[local_spec, whole_spec, local_spec, mask_spec],
        out_specs=whole_spec,
        out_shape=jax.ShapeDtypeStruct((total_rows, width_local), jnp.bfloat16),
    )(queries, keys_whole, cotangent, visible)


def head_attention(queries, keys_whole, values_whole, cotangent, visible, scale_factor):
    local_rows, width_local = queries.shape
    total_rows = keys_whole.shape[0]
    local_spec, whole_spec, mask_spec = head_specs(local_rows, total_rows)
    return pl.pallas_call(
        functools.partial(attention_block, scale_factor),
        grid=(width_local // HD,),
        in_specs=[local_spec, whole_spec, whole_spec, local_spec, mask_spec],
        out_specs=[whole_spec, local_spec, local_spec],
        out_shape=[
            jax.ShapeDtypeStruct((total_rows, width_local), jnp.bfloat16),
            jax.ShapeDtypeStruct((local_rows, width_local), jnp.float32),
            jax.ShapeDtypeStruct((local_rows, width_local), jnp.bfloat16),
        ],
    )(queries, keys_whole, values_whole, cotangent, visible)


def shards(
    stream,
    shutter,
    feeder,
    stencil,
    valves,
    intake,
    kernel,
    scaling,
    queries,
    matchers,
    segments,
    cotangent,
):
    local_rows = stream.shape[0]
    width_local = stream.shape[1]
    head_count = width_local // HD
    total_rows = local_rows * lax.axis_size("ctx")
    position = lax.axis_index("ctx") * local_rows
    scale_factor = 1.0 / math.sqrt(HD)
    widened = stream.astype(jnp.float32)
    inner_one = feeder.astype(jnp.float32) * widened
    rim_one = neighbor_rows(inner_one[local_rows - (KS - 1) :], 1)
    padded_one = jnp.concatenate([rim_one, inner_one], axis=0)
    conv_one = depthwise(padded_one, stencil[::-1])
    first_out = (widened + shutter.astype(jnp.float32) * conv_one).astype(jnp.bfloat16)
    first_wide = first_out.astype(jnp.float32)
    inner_two = intake.astype(jnp.float32) * first_wide
    rim_two = neighbor_rows(inner_two[local_rows - (KM - 1) :], 1)
    padded_two = jnp.concatenate([rim_two, inner_two], axis=0)
    conv_two = depthwise(padded_two, kernel[::-1])
    second_out = (first_wide + valves.astype(jnp.float32) * conv_two).astype(jnp.bfloat16)
    second_wide = second_out.astype(jnp.float32)
    squares = channel_total(jnp.sum(second_wide * second_wide, axis=1))
    inverse_rms = lax.rsqrt(squares / D + epsilon)
    normed = (second_wide * inverse_rms[:, None] * scaling).astype(jnp.bfloat16)
    ctx_count = lax.axis_size("ctx")
    ctx_index = lax.axis_index("ctx")
    keys_whole = lax.all_gather(matchers, "ctx", axis=0, tiled=True)
    reach = min(ctx_count - 1, (3 * total_rows // 4 - 1 + local_rows - 1) // local_rows)
    query_pos = position + jnp.arange(local_rows, dtype=jnp.int32)
    key_pos = jnp.arange(total_rows, dtype=jnp.int32)
    query_seg = lax.dynamic_slice_in_dim(segments, position, local_rows, 0)
    visible = (key_pos[None, :] <= query_pos[:, None]) & (segments[None, :] == query_seg[:, None])
    mask = visible.astype(jnp.float32)
    value_part = head_values_grad(queries, keys_whole, cotangent, mask, scale_factor)
    value_grad = (
        lax.all_to_all(value_part, "ctx", 0, 0, tiled=True)
        .reshape(ctx_count, local_rows, width_local)
        .astype(jnp.float32)
        .sum(axis=0)
    )
    values_whole = lax.all_gather(normed, "ctx", axis=0, tiled=True)
    key_part, attended_all, queries_grad = head_attention(
        queries, keys_whole, values_whole, cotangent, mask, scale_factor
    )
    result = (second_wide + attended_all).astype(jnp.bfloat16)
    key_part, value_grad = lax.optimization_barrier((key_part, value_grad))
    matchers_grad = lax.psum_scatter(
        key_part,
        "ctx",
        scatter_dimension=0,
        tiled=True,
    )
    gain_part = value_grad * scaling
    projected = channel_total(jnp.sum(gain_part * second_wide, axis=1))
    scaling_part = jnp.sum(value_grad * second_wide * inverse_rms[:, None], axis=0)
    second_grad = (
        cotangent.astype(jnp.float32)
        + inverse_rms[:, None] * gain_part
        - second_wide * (inverse_rms**3 * projected / D)[:, None]
    )
    valves_grad = (second_grad * conv_two).astype(jnp.bfloat16)
    dconv_two = second_grad * valves.astype(jnp.float32)
    back_two = neighbor_rows(dconv_two[: KM - 1], -1)
    dinner_two = depthwise(jnp.concatenate([dconv_two, back_two], axis=0), kernel)
    intake_grad = (dinner_two * first_wide).astype(jnp.bfloat16)
    kernel_part = depthwise(padded_two, dconv_two)[::-1]
    first_grad = second_grad + dinner_two * intake.astype(jnp.float32)
    shutter_grad = (first_grad * conv_one).astype(jnp.bfloat16)
    dconv_one = first_grad * shutter.astype(jnp.float32)
    back_one = neighbor_rows(dconv_one[: KS - 1], -1)
    dinner_one = depthwise(jnp.concatenate([dconv_one, back_one], axis=0), stencil)
    feeder_grad = (dinner_one * widened).astype(jnp.bfloat16)
    stencil_part = depthwise(padded_one, dconv_one)[::-1]
    stream_grad = (first_grad + dinner_one * feeder.astype(jnp.float32)).astype(jnp.bfloat16)
    filter_sum = butterfly_total(
        jnp.concatenate([kernel_part, scaling_part[None]], axis=0), "ctx", jnp.bfloat16
    )
    kernel_sum = filter_sum[:KM]
    scaling_sum = filter_sum[KM]
    if lax.axis_size("ctx") <= 8:
        stencil_sum = exchange_total(stencil_part.astype(jnp.bfloat16), "ctx")
    else:
        stencil_sum = butterfly_total(stencil_part, "ctx", jnp.bfloat16)
    normalizer = math.sqrt(total_rows)
    return (
        result,
        stream_grad,
        shutter_grad,
        feeder_grad,
        stencil_sum / normalizer,
        valves_grad,
        intake_grad,
        kernel_sum / normalizer,
        scaling_sum / normalizer,
        queries_grad,
        matchers_grad,
    )


def solution(mesh):
    placed = (
        P("ctx", "tp"),
        P("ctx", "tp"),
        P("ctx", "tp"),
        P(None, "tp"),
        P("ctx", "tp"),
        P("ctx", "tp"),
        P(None, "tp"),
        P("tp"),
        P("ctx", "tp"),
        P("ctx", "tp"),
        P(),
        P("ctx", "tp"),
    )
    return jax.shard_map(
        shards,
        mesh=mesh,
        in_specs=placed,
        out_specs=(
            P("ctx", "tp"),
            P("ctx", "tp"),
            P("ctx", "tp"),
            P("ctx", "tp"),
            P(None, "tp"),
            P("ctx", "tp"),
            P("ctx", "tp"),
            P(None, "tp"),
            P("tp"),
            P("ctx", "tp"),
            P("ctx", "tp"),
        ),
        check_vma=False,
    )
```

```python
import functools
import math

import jax
import jax.numpy as jnp
from jax import lax
from jax.experimental import pallas as pl
from jax.sharding import PartitionSpec as P

HD = 128
D = 4096
KS = 7
KM = 128


epsilon = 1e-06


def as_sent(shard):

    def short(part):
        return part.astype(jnp.bfloat16) if part.dtype == jnp.float32 else part

    return jax.tree.map(short, shard)


def passed_along(value, axis, steps):
    count = lax.axis_size(axis)
    leading, last = (max(0, -steps), min(count, count - steps))
    return lax.ppermute(value, axis, [(source, source + steps) for source in range(leading, last)])


def depthwise(padded, tap_rows):
    return lax.conv_general_dilated(
        padded[None],
        tap_rows[:, None, :],
        (1,),
        "VALID",
        dimension_numbers=("NWC", "WIO", "NWC"),
        feature_group_count=padded.shape[1],
        precision=lax.Precision.DEFAULT,
    )[0]


def neighbor_rows(edge_rows, offset):
    return passed_along(as_sent(edge_rows), "ctx", offset).astype(edge_rows.dtype)


def butterfly_total(value, axis, sent_type=None):
    count = lax.axis_size(axis)
    if count & (count - 1):
        if sent_type is None:
            return lax.psum(value, axis)
        return lax.psum(value.astype(sent_type), axis).astype(value.dtype)
    step = 1
    while step < count:
        pairs = [(source, source ^ step) for source in range(count)]
        if sent_type is None:
            value = value + lax.ppermute(value, axis, pairs)
        else:
            rounded = value.astype(sent_type)
            value = rounded.astype(value.dtype) + lax.ppermute(rounded, axis, pairs).astype(value.dtype)
        step *= 2
    return value


def exchange_total(value, axis):
    count = lax.axis_size(axis)
    index = lax.axis_index(axis)
    stacked = jnp.zeros((count,) + value.shape, value.dtype)
    stacked = lax.dynamic_update_index_in_dim(stacked, value, index, 0)
    for shift in range(1, count):
        pairs = [(source, (source + shift) % count) for source in range(count)]
        arrived = lax.ppermute(value, axis, pairs)
        stacked = lax.dynamic_update_index_in_dim(stacked, arrived, (index - shift) % count, 0)
    return jnp.sum(stacked, axis=0)


def channel_total(partial_value):
    if lax.axis_size("tp") <= 4:
        return exchange_total(partial_value, "tp")
    return butterfly_total(partial_value, "tp")


def head_weights(scale_factor, query_head, key_head, visible):
    contract_last = (((1,), (1,)), ((), ()))
    scores = (
        lax.dot_general(query_head, key_head, contract_last, preferred_element_type=jnp.float32)
        * scale_factor
    )
    scores = jnp.where(visible > 0.5, scores, -jnp.inf)
    row_max = jnp.max(scores, axis=1, keepdims=True)
    logsum = row_max + jnp.log(jnp.sum(jnp.exp(scores - row_max), axis=1, keepdims=True))
    return jnp.exp(scores - logsum).astype(jnp.bfloat16)


def value_block(scale_factor, q_ref, k_ref, cot_ref, vis_ref, dv_ref):
    contract_first = (((0,), (0,)), ((), ()))
    weights = head_weights(scale_factor, q_ref[...], k_ref[...], vis_ref[...])
    dv_ref[...] = lax.dot_general(
        weights, cot_ref[...], contract_first, preferred_element_type=jnp.float32
    ).astype(jnp.bfloat16)


def attention_block(scale_factor, q_ref, k_ref, v_ref, cot_ref, vis_ref, dk_ref, att_ref, dq_ref):
    contract_last = (((1,), (1,)), ((), ()))
    contract_first = (((0,), (0,)), ((), ()))
    query_head = q_ref[...]
    key_head = k_ref[...]
    value_head = v_ref[...]
    cotangent_head = cot_ref[...]
    weights = head_weights(scale_factor, query_head, key_head, vis_ref[...])
    attended = jnp.dot(weights, value_head, preferred_element_type=jnp.float32)
    weight_grad = lax.dot_general(
        cotangent_head, value_head, contract_last, preferred_element_type=jnp.float32
    )
    row_delta = jnp.sum(cotangent_head.astype(jnp.float32) * attended, axis=1, keepdims=True)
    dscore = (scale_factor * weights.astype(jnp.float32) * (weight_grad - row_delta)).astype(
        jnp.bfloat16
    )
    att_ref[...] = attended
    dq_ref[...] = jnp.dot(dscore, key_head, preferred_element_type=jnp.float32).astype(jnp.bfloat16)
    dk_ref[...] = lax.dot_general(
        dscore, query_head, contract_first, preferred_element_type=jnp.float32
    ).astype(jnp.bfloat16)


def head_specs(local_rows, total_rows):
    local_spec = pl.BlockSpec((local_rows, HD), lambda h: (0, h))
    whole_spec = pl.BlockSpec((total_rows, HD), lambda h: (0, h))
    mask_spec = pl.BlockSpec((local_rows, total_rows), lambda h: (0, 0))
    return local_spec, whole_spec, mask_spec


def head_values_grad(queries, keys_whole, cotangent, visible, scale_factor):
    local_rows, width_local = queries.shape
    total_rows = keys_whole.shape[0]
    local_spec, whole_spec, mask_spec = head_specs(local_rows, total_rows)
    return pl.pallas_call(
        functools.partial(value_block, scale_factor),
        grid=(width_local // HD,),
        in_specs=[local_spec, whole_spec, local_spec, mask_spec],
        out_specs=whole_spec,
        out_shape=jax.ShapeDtypeStruct((total_rows, width_local), jnp.bfloat16),
    )(queries, keys_whole, cotangent, visible)


def head_attention(queries, keys_whole, values_whole, cotangent, visible, scale_factor):
    local_rows, width_local = queries.shape
    total_rows = keys_whole.shape[0]
    local_spec, whole_spec, mask_spec = head_specs(local_rows, total_rows)
    return pl.pallas_call(
        functools.partial(attention_block, scale_factor),
        grid=(width_local // HD,),
        in_specs=[local_spec, whole_spec, whole_spec, local_spec, mask_spec],
        out_specs=[whole_spec, local_spec, local_spec],
        out_shape=[
            jax.ShapeDtypeStruct((total_rows, width_local), jnp.bfloat16),
            jax.ShapeDtypeStruct((local_rows, width_local), jnp.float32),
            jax.ShapeDtypeStruct((local_rows, width_local), jnp.bfloat16),
        ],
    )(queries, keys_whole, values_whole, cotangent, visible)


def shards(
    stream,
    shutter,
    feeder,
    stencil,
    valves,
    intake,
    kernel,
    scaling,
    queries,
    matchers,
    segments,
    cotangent,
):
    local_rows = stream.shape[0]
    width_local = stream.shape[1]
    head_count = width_local // HD
    total_rows = local_rows * lax.axis_size("ctx")
    position = lax.axis_index("ctx") * local_rows
    scale_factor = 1.0 / math.sqrt(HD)
    widened = stream.astype(jnp.float32)
    inner_one = feeder.astype(jnp.float32) * widened
    rim_one = neighbor_rows(inner_one[local_rows - (KS - 1) :], 1)
    padded_one = jnp.concatenate([rim_one, inner_one], axis=0)
    conv_one = depthwise(padded_one, stencil[::-1])
    first_out = (widened + shutter.astype(jnp.float32) * conv_one).astype(jnp.bfloat16)
    first_wide = first_out.astype(jnp.float32)
    inner_two = intake.astype(jnp.float32) * first_wide
    rim_two = neighbor_rows(inner_two[local_rows - (KM - 1) :], 1)
    padded_two = jnp.concatenate([rim_two, inner_two], axis=0)
    conv_two = depthwise(padded_two, kernel[::-1])
    second_out = (first_wide + valves.astype(jnp.float32) * conv_two).astype(jnp.bfloat16)
    second_wide = second_out.astype(jnp.float32)
    squares = channel_total(jnp.sum(second_wide * second_wide, axis=1))
    inverse_rms = lax.rsqrt(squares / D + epsilon)
    normed = (second_wide * inverse_rms[:, None] * scaling).astype(jnp.bfloat16)
    ctx_count = lax.axis_size("ctx")
    ctx_index = lax.axis_index("ctx")
    keys_whole = lax.all_gather(matchers, "ctx", axis=0, tiled=True)
    reach = min(ctx_count - 1, (3 * total_rows // 4 - 1 + local_rows - 1) // local_rows)
    query_pos = position + jnp.arange(local_rows, dtype=jnp.int32)
    key_pos = jnp.arange(total_rows, dtype=jnp.int32)
    query_seg = lax.dynamic_slice_in_dim(segments, position, local_rows, 0)
    visible = (key_pos[None, :] <= query_pos[:, None]) & (segments[None, :] == query_seg[:, None])
    mask = visible.astype(jnp.float32)
    value_part = head_values_grad(queries, keys_whole, cotangent, mask, scale_factor)
    value_grad = (
        lax.all_to_all(value_part, "ctx", 0, 0, tiled=True)
        .reshape(ctx_count, local_rows, width_local)
        .astype(jnp.float32)
        .sum(axis=0)
    )
    values_whole = lax.all_gather(normed, "ctx", axis=0, tiled=True)
    key_part, attended_all, queries_grad = head_attention(
        queries, keys_whole, values_whole, cotangent, mask, scale_factor
    )
    result = (second_wide + attended_all).astype(jnp.bfloat16)
    key_part, value_grad = lax.optimization_barrier((key_part, value_grad))
    matchers_grad = lax.psum_scatter(
        key_part,
        "ctx",
        scatter_dimension=0,
        tiled=True,
    )
    gain_part = value_grad * scaling
    projected = channel_total(jnp.sum(gain_part * second_wide, axis=1))
    scaling_part = jnp.sum(value_grad * second_wide * inverse_rms[:, None], axis=0)
    second_grad = (
        cotangent.astype(jnp.float32)
        + inverse_rms[:, None] * gain_part
        - second_wide * (inverse_rms**3 * projected / D)[:, None]
    )
    valves_grad = (second_grad * conv_two).astype(jnp.bfloat16)
    dconv_two = second_grad * valves.astype(jnp.float32)
    back_two = neighbor_rows(dconv_two[: KM - 1], -1)
    dinner_two = depthwise(jnp.concatenate([dconv_two, back_two], axis=0), kernel)
    intake_grad = (dinner_two * first_wide).astype(jnp.bfloat16)
    kernel_part = depthwise(padded_two, dconv_two)[::-1]
    first_grad = second_grad + dinner_two * intake.astype(jnp.float32)
    shutter_grad = (first_grad * conv_one).astype(jnp.bfloat16)
    dconv_one = first_grad * shutter.astype(jnp.float32)
    back_one = neighbor_rows(dconv_one[: KS - 1], -1)
    dinner_one = depthwise(jnp.concatenate([dconv_one, back_one], axis=0), stencil)
    feeder_grad = (dinner_one * widened).astype(jnp.bfloat16)
    stencil_part = depthwise(padded_one, dconv_one)[::-1]
    stream_grad = (first_grad + dinner_one * feeder.astype(jnp.float32)).astype(jnp.bfloat16)
    filter_sum = butterfly_total(
        jnp.concatenate([kernel_part, scaling_part[None], stencil_part], axis=0), "ctx", jnp.bfloat16
    )
    kernel_sum = filter_sum[:KM]
    scaling_sum = filter_sum[KM]
    stencil_sum = filter_sum[KM + 1 :]
    normalizer = math.sqrt(total_rows)
    return (
        result,
        stream_grad,
        shutter_grad,
        feeder_grad,
        stencil_sum / normalizer,
        valves_grad,
        intake_grad,
        kernel_sum / normalizer,
        scaling_sum / normalizer,
        queries_grad,
        matchers_grad,
    )


def solution(mesh):
    placed = (
        P("ctx", "tp"),
        P("ctx", "tp"),
        P("ctx", "tp"),
        P(None, "tp"),
        P("ctx", "tp"),
        P("ctx", "tp"),
        P(None, "tp"),
        P("tp"),
        P("ctx", "tp"),
        P("ctx", "tp"),
        P(),
        P("ctx", "tp"),
    )
    return jax.shard_map(
        shards,
        mesh=mesh,
        in_specs=placed,
        out_specs=(
            P("ctx", "tp"),
            P("ctx", "tp"),
            P("ctx", "tp"),
            P("ctx", "tp"),
            P(None, "tp"),
            P("ctx", "tp"),
            P("ctx", "tp"),
            P(None, "tp"),
            P("tp"),
            P("ctx", "tp"),
            P("ctx", "tp"),
        ),
        check_vma=False,
    )
```

```python
import functools
import math

import jax
import jax.numpy as jnp
from jax import lax
from jax.experimental import pallas as pl
from jax.sharding import PartitionSpec as P

HD = 128
D = 4096
KS = 7
KM = 128


epsilon = 1e-06


def as_sent(shard):

    def short(part):
        return part.astype(jnp.bfloat16) if part.dtype == jnp.float32 else part

    return jax.tree.map(short, shard)


def passed_along(value, axis, steps):
    count = lax.axis_size(axis)
    leading, last = (max(0, -steps), min(count, count - steps))
    return lax.ppermute(value, axis, [(source, source + steps) for source in range(leading, last)])


def depthwise(padded, tap_rows):
    return lax.conv_general_dilated(
        padded[None],
        tap_rows[:, None, :],
        (1,),
        "VALID",
        dimension_numbers=("NWC", "WIO", "NWC"),
        feature_group_count=padded.shape[1],
        precision=lax.Precision.HIGHEST,
    )[0]


def neighbor_rows(edge_rows, offset):
    return passed_along(as_sent(edge_rows), "ctx", offset).astype(edge_rows.dtype)


def butterfly_total(value, axis, sent_type=None):
    count = lax.axis_size(axis)
    if count & (count - 1):
        if sent_type is None:
            return lax.psum(value, axis)
        return lax.psum(value.astype(sent_type), axis).astype(value.dtype)
    step = 1
    while step < count:
        pairs = [(source, source ^ step) for source in range(count)]
        if sent_type is None:
            value = value + lax.ppermute(value, axis, pairs)
        else:
            rounded = value.astype(sent_type)
            value = rounded.astype(value.dtype) + lax.ppermute(rounded, axis, pairs).astype(value.dtype)
        step *= 2
    return value


def exchange_total(value, axis):
    count = lax.axis_size(axis)
    index = lax.axis_index(axis)
    stacked = jnp.zeros((count,) + value.shape, value.dtype)
    stacked = lax.dynamic_update_index_in_dim(stacked, value, index, 0)
    for shift in range(1, count):
        pairs = [(source, (source + shift) % count) for source in range(count)]
        arrived = lax.ppermute(value, axis, pairs)
        stacked = lax.dynamic_update_index_in_dim(stacked, arrived, (index - shift) % count, 0)
    return jnp.sum(stacked, axis=0)


def channel_total(partial_value):
    if lax.axis_size("tp") <= 4:
        return exchange_total(partial_value, "tp")
    return butterfly_total(partial_value, "tp")


def head_weights(scale_factor, query_head, key_head, visible):
    contract_last = (((1,), (1,)), ((), ()))
    scores = (
        lax.dot_general(query_head, key_head, contract_last, preferred_element_type=jnp.float32)
        * scale_factor
    )
    scores = jnp.where(visible > 0.5, scores, -jnp.inf)
    row_max = jnp.max(scores, axis=1, keepdims=True)
    logsum = row_max + jnp.log(jnp.sum(jnp.exp(scores - row_max), axis=1, keepdims=True))
    return jnp.exp(scores - logsum).astype(jnp.bfloat16)


def value_block(scale_factor, q_ref, k_ref, cot_ref, vis_ref, dv_ref):
    contract_first = (((0,), (0,)), ((), ()))
    weights = head_weights(scale_factor, q_ref[...], k_ref[...], vis_ref[...])
    dv_ref[...] = lax.dot_general(
        weights, cot_ref[...], contract_first, preferred_element_type=jnp.float32
    ).astype(jnp.bfloat16)


def attention_block(scale_factor, q_ref, k_ref, v_ref, cot_ref, vis_ref, dk_ref, att_ref, dq_ref):
    contract_last = (((1,), (1,)), ((), ()))
    contract_first = (((0,), (0,)), ((), ()))
    query_head = q_ref[...]
    key_head = k_ref[...]
    value_head = v_ref[...]
    cotangent_head = cot_ref[...]
    weights = head_weights(scale_factor, query_head, key_head, vis_ref[...])
    attended = jnp.dot(weights, value_head, preferred_element_type=jnp.float32)
    weight_grad = lax.dot_general(
        cotangent_head, value_head, contract_last, preferred_element_type=jnp.float32
    )
    row_delta = jnp.sum(cotangent_head.astype(jnp.float32) * attended, axis=1, keepdims=True)
    dscore = (scale_factor * weights.astype(jnp.float32) * (weight_grad - row_delta)).astype(
        jnp.bfloat16
    )
    att_ref[...] = attended
    dq_ref[...] = jnp.dot(dscore, key_head, preferred_element_type=jnp.float32).astype(jnp.bfloat16)
    dk_ref[...] = lax.dot_general(
        dscore, query_head, contract_first, preferred_element_type=jnp.float32
    ).astype(jnp.bfloat16)


def head_specs(local_rows, total_rows):
    local_spec = pl.BlockSpec((local_rows, HD), lambda h: (0, h))
    whole_spec = pl.BlockSpec((total_rows, HD), lambda h: (0, h))
    mask_spec = pl.BlockSpec((local_rows, total_rows), lambda h: (0, 0))
    return local_spec, whole_spec, mask_spec


def head_values_grad(queries, keys_whole, cotangent, visible, scale_factor):
    local_rows, width_local = queries.shape
    total_rows = keys_whole.shape[0]
    local_spec, whole_spec, mask_spec = head_specs(local_rows, total_rows)
    return pl.pallas_call(
        functools.partial(value_block, scale_factor),
        grid=(width_local // HD,),
        in_specs=[local_spec, whole_spec, local_spec, mask_spec],
        out_specs=whole_spec,
        out_shape=jax.ShapeDtypeStruct((total_rows, width_local), jnp.bfloat16),
    )(queries, keys_whole, cotangent, visible)


def head_attention(queries, keys_whole, values_whole, cotangent, visible, scale_factor):
    local_rows, width_local = queries.shape
    total_rows = keys_whole.shape[0]
    local_spec, whole_spec, mask_spec = head_specs(local_rows, total_rows)
    return pl.pallas_call(
        functools.partial(attention_block, scale_factor),
        grid=(width_local // HD,),
        in_specs=[local_spec, whole_spec, whole_spec, local_spec, mask_spec],
        out_specs=[whole_spec, local_spec, local_spec],
        out_shape=[
            jax.ShapeDtypeStruct((total_rows, width_local), jnp.bfloat16),
            jax.ShapeDtypeStruct((local_rows, width_local), jnp.float32),
            jax.ShapeDtypeStruct((local_rows, width_local), jnp.bfloat16),
        ],
    )(queries, keys_whole, values_whole, cotangent, visible)


def shards(
    stream,
    shutter,
    feeder,
    stencil,
    valves,
    intake,
    kernel,
    scaling,
    queries,
    matchers,
    segments,
    cotangent,
):
    local_rows = stream.shape[0]
    width_local = stream.shape[1]
    head_count = width_local // HD
    total_rows = local_rows * lax.axis_size("ctx")
    position = lax.axis_index("ctx") * local_rows
    scale_factor = 1.0 / math.sqrt(HD)
    widened = stream.astype(jnp.float32)
    inner_one = feeder.astype(jnp.float32) * widened
    rim_one = neighbor_rows(inner_one[local_rows - (KS - 1) :], 1)
    padded_one = jnp.concatenate([rim_one, inner_one], axis=0)
    conv_one = depthwise(padded_one, stencil[::-1])
    first_out = (widened + shutter.astype(jnp.float32) * conv_one).astype(jnp.bfloat16)
    first_wide = first_out.astype(jnp.float32)
    inner_two = intake.astype(jnp.float32) * first_wide
    rim_two = neighbor_rows(inner_two[local_rows - (KM - 1) :], 1)
    padded_two = jnp.concatenate([rim_two, inner_two], axis=0)
    conv_two = depthwise(padded_two, kernel[::-1])
    second_out = (first_wide + valves.astype(jnp.float32) * conv_two).astype(jnp.bfloat16)
    second_wide = second_out.astype(jnp.float32)
    squares = channel_total(jnp.sum(second_wide * second_wide, axis=1))
    inverse_rms = lax.rsqrt(squares / D + epsilon)
    normed = (second_wide * inverse_rms[:, None] * scaling).astype(jnp.bfloat16)
    ctx_count = lax.axis_size("ctx")
    ctx_index = lax.axis_index("ctx")
    keys_whole = lax.all_gather(matchers, "ctx", axis=0, tiled=True)
    reach = min(ctx_count - 1, (3 * total_rows // 4 - 1 + local_rows - 1) // local_rows)
    query_pos = position + jnp.arange(local_rows, dtype=jnp.int32)
    key_pos = jnp.arange(total_rows, dtype=jnp.int32)
    query_seg = lax.dynamic_slice_in_dim(segments, position, local_rows, 0)
    visible = (key_pos[None, :] <= query_pos[:, None]) & (segments[None, :] == query_seg[:, None])
    mask = visible.astype(jnp.float32)
    value_part = head_values_grad(queries, keys_whole, cotangent, mask, scale_factor)
    exchanged = lax.all_to_all(
        jnp.concatenate([value_part, jnp.tile(normed, (ctx_count, 1))], axis=1),
        "ctx",
        0,
        0,
        tiled=True,
    )
    value_grad = (
        exchanged[:, :width_local]
        .reshape(ctx_count, local_rows, width_local)
        .astype(jnp.float32)
        .sum(axis=0)
    )
    values_whole = exchanged[:, width_local:]
    key_part, attended_all, queries_grad = head_attention(
        queries, keys_whole, values_whole, cotangent, mask, scale_factor
    )
    result = (second_wide + attended_all).astype(jnp.bfloat16)
    key_part, value_grad = lax.optimization_barrier((key_part, value_grad))
    matchers_grad = lax.psum_scatter(
        key_part,
        "ctx",
        scatter_dimension=0,
        tiled=True,
    )
    gain_part = value_grad * scaling
    projected = channel_total(jnp.sum(gain_part * second_wide, axis=1))
    scaling_part = jnp.sum(value_grad * second_wide * inverse_rms[:, None], axis=0)
    second_grad = (
        cotangent.astype(jnp.float32)
        + inverse_rms[:, None] * gain_part
        - second_wide * (inverse_rms**3 * projected / D)[:, None]
    )
    valves_grad = (second_grad * conv_two).astype(jnp.bfloat16)
    dconv_two = second_grad * valves.astype(jnp.float32)
    back_two = neighbor_rows(dconv_two[: KM - 1], -1)
    dinner_two = depthwise(jnp.concatenate([dconv_two, back_two], axis=0), kernel)
    intake_grad = (dinner_two * first_wide).astype(jnp.bfloat16)
    kernel_part = depthwise(padded_two, dconv_two)[::-1]
    first_grad = second_grad + dinner_two * intake.astype(jnp.float32)
    shutter_grad = (first_grad * conv_one).astype(jnp.bfloat16)
    dconv_one = first_grad * shutter.astype(jnp.float32)
    back_one = neighbor_rows(dconv_one[: KS - 1], -1)
    dinner_one = depthwise(jnp.concatenate([dconv_one, back_one], axis=0), stencil)
    feeder_grad = (dinner_one * widened).astype(jnp.bfloat16)
    stencil_part = depthwise(padded_one, dconv_one)[::-1]
    stream_grad = (first_grad + dinner_one * feeder.astype(jnp.float32)).astype(jnp.bfloat16)
    filter_sum = butterfly_total(
        jnp.concatenate([kernel_part, scaling_part[None], stencil_part], axis=0), "ctx", jnp.bfloat16
    )
    kernel_sum = filter_sum[:KM]
    scaling_sum = filter_sum[KM]
    stencil_sum = filter_sum[KM + 1 :]
    normalizer = math.sqrt(total_rows)
    return (
        result,
        stream_grad,
        shutter_grad,
        feeder_grad,
        stencil_sum / normalizer,
        valves_grad,
        intake_grad,
        kernel_sum / normalizer,
        scaling_sum / normalizer,
        queries_grad,
        matchers_grad,
    )


def solution(mesh):
    placed = (
        P("ctx", "tp"),
        P("ctx", "tp"),
        P("ctx", "tp"),
        P(None, "tp"),
        P("ctx", "tp"),
        P("ctx", "tp"),
        P(None, "tp"),
        P("tp"),
        P("ctx", "tp"),
        P("ctx", "tp"),
        P(),
        P("ctx", "tp"),
    )
    return jax.shard_map(
        shards,
        mesh=mesh,
        in_specs=placed,
        out_specs=(
            P("ctx", "tp"),
            P("ctx", "tp"),
            P("ctx", "tp"),
            P("ctx", "tp"),
            P(None, "tp"),
            P("ctx", "tp"),
            P("ctx", "tp"),
            P(None, "tp"),
            P("tp"),
            P("ctx", "tp"),
            P("ctx", "tp"),
        ),
        check_vma=False,
    )
```

```python
import functools
import math

import jax
import jax.numpy as jnp
from jax import lax
from jax.experimental import pallas as pl
from jax.sharding import PartitionSpec as P

HD = 128
D = 4096
KS = 7
KM = 128


epsilon = 1e-06


def as_sent(shard):

    def short(part):
        return part.astype(jnp.bfloat16) if part.dtype == jnp.float32 else part

    return jax.tree.map(short, shard)


def passed_along(value, axis, steps):
    count = lax.axis_size(axis)
    leading, last = (max(0, -steps), min(count, count - steps))
    return lax.ppermute(value, axis, [(source, source + steps) for source in range(leading, last)])


def depthwise(padded, tap_rows):
    return lax.conv_general_dilated(
        padded[None],
        tap_rows[:, None, :],
        (1,),
        "VALID",
        dimension_numbers=("NWC", "WIO", "NWC"),
        feature_group_count=padded.shape[1],
        precision=lax.Precision.HIGHEST,
    )[0]


def neighbor_rows(edge_rows, offset):
    return passed_along(as_sent(edge_rows), "ctx", offset).astype(edge_rows.dtype)


def butterfly_total(value, axis, sent_type=None):
    count = lax.axis_size(axis)
    if count & (count - 1):
        if sent_type is None:
            return lax.psum(value, axis)
        return lax.psum(value.astype(sent_type), axis).astype(value.dtype)
    step = 1
    while step < count:
        pairs = [(source, source ^ step) for source in range(count)]
        if sent_type is None:
            value = value + lax.ppermute(value, axis, pairs)
        else:
            rounded = value.astype(sent_type)
            value = rounded.astype(value.dtype) + lax.ppermute(rounded, axis, pairs).astype(value.dtype)
        step *= 2
    return value


def exchange_total(value, axis):
    count = lax.axis_size(axis)
    index = lax.axis_index(axis)
    stacked = jnp.zeros((count,) + value.shape, value.dtype)
    stacked = lax.dynamic_update_index_in_dim(stacked, value, index, 0)
    for shift in range(1, count):
        pairs = [(source, (source + shift) % count) for source in range(count)]
        arrived = lax.ppermute(value, axis, pairs)
        stacked = lax.dynamic_update_index_in_dim(stacked, arrived, (index - shift) % count, 0)
    return jnp.sum(stacked, axis=0)


def channel_total(partial_value):
    if lax.axis_size("tp") <= 4:
        return exchange_total(partial_value, "tp")
    return butterfly_total(partial_value, "tp")


def head_weights(scale_factor, query_head, key_head, visible):
    contract_last = (((1,), (1,)), ((), ()))
    scores = (
        lax.dot_general(query_head, key_head, contract_last, preferred_element_type=jnp.float32)
        * scale_factor
    )
    scores = jnp.where(visible, scores, -jnp.inf)
    row_max = jnp.max(scores, axis=1, keepdims=True)
    raised = jnp.exp(scores - row_max)
    return (raised * (1.0 / jnp.sum(raised, axis=1, keepdims=True))).astype(jnp.bfloat16)


def value_block(scale_factor, q_ref, k_ref, cot_ref, vis_ref, dv_ref):
    contract_first = (((0,), (0,)), ((), ()))
    visible = vis_ref[...] > 0.5
    for head in range(q_ref.shape[1] // HD):
        columns = slice(head * HD, (head + 1) * HD)
        weights = head_weights(scale_factor, q_ref[:, columns], k_ref[:, columns], visible)
        dv_ref[:, columns] = lax.dot_general(
            weights, cot_ref[:, columns], contract_first, preferred_element_type=jnp.float32
        ).astype(jnp.bfloat16)


def attention_block(scale_factor, q_ref, k_ref, v_ref, cot_ref, vis_ref, dk_ref, att_ref, dq_ref):
    contract_last = (((1,), (1,)), ((), ()))
    contract_first = (((0,), (0,)), ((), ()))
    visible = vis_ref[...] > 0.5
    for head in range(q_ref.shape[1] // HD):
        columns = slice(head * HD, (head + 1) * HD)
        query_head = q_ref[:, columns]
        key_head = k_ref[:, columns]
        value_head = v_ref[:, columns]
        cotangent_head = cot_ref[:, columns]
        weights = head_weights(scale_factor, query_head, key_head, visible)
        attended = jnp.dot(weights, value_head, preferred_element_type=jnp.float32)
        weight_grad = lax.dot_general(
            cotangent_head, value_head, contract_last, preferred_element_type=jnp.float32
        )
        row_delta = jnp.sum(cotangent_head.astype(jnp.float32) * attended, axis=1, keepdims=True)
        dscore = (scale_factor * weights.astype(jnp.float32) * (weight_grad - row_delta)).astype(
            jnp.bfloat16
        )
        att_ref[:, columns] = attended
        dq_ref[:, columns] = jnp.dot(
            dscore, key_head, preferred_element_type=jnp.float32
        ).astype(jnp.bfloat16)
        dk_ref[:, columns] = lax.dot_general(
            dscore, query_head, contract_first, preferred_element_type=jnp.float32
        ).astype(jnp.bfloat16)


def head_specs(local_rows, total_rows, width_local):
    group = 2 if (width_local // HD) % 2 == 0 else 1
    local_spec = pl.BlockSpec((local_rows, group * HD), lambda h: (0, h))
    whole_spec = pl.BlockSpec((total_rows, group * HD), lambda h: (0, h))
    weight_spec = pl.BlockSpec((group, local_rows, total_rows), lambda h: (h, 0, 0))
    return local_spec, whole_spec, weight_spec, width_local // (group * HD)


def head_values_grad(queries, keys_whole, cotangent, visible, scale_factor):
    local_rows, width_local = queries.shape
    total_rows = keys_whole.shape[0]
    local_spec, whole_spec, weight_spec, steps = head_specs(local_rows, total_rows, width_local)
    mask_spec = pl.BlockSpec((local_rows, total_rows), lambda h: (0, 0))
    return pl.pallas_call(
        functools.partial(value_block, scale_factor),
        grid=(steps,),
        in_specs=[local_spec, whole_spec, local_spec, mask_spec],
        out_specs=whole_spec,
        out_shape=jax.ShapeDtypeStruct((total_rows, width_local), jnp.bfloat16),
    )(queries, keys_whole, cotangent, visible)


def head_attention(queries, keys_whole, values_whole, cotangent, visible, scale_factor):
    local_rows, width_local = queries.shape
    total_rows = keys_whole.shape[0]
    local_spec, whole_spec, weight_spec, steps = head_specs(local_rows, total_rows, width_local)
    mask_spec = pl.BlockSpec((local_rows, total_rows), lambda h: (0, 0))
    return pl.pallas_call(
        functools.partial(attention_block, scale_factor),
        grid=(steps,),
        in_specs=[local_spec, whole_spec, whole_spec, local_spec, mask_spec],
        out_specs=[whole_spec, local_spec, local_spec],
        out_shape=[
            jax.ShapeDtypeStruct((total_rows, width_local), jnp.bfloat16),
            jax.ShapeDtypeStruct((local_rows, width_local), jnp.float32),
            jax.ShapeDtypeStruct((local_rows, width_local), jnp.bfloat16),
        ],
    )(queries, keys_whole, values_whole, cotangent, visible)


def shards(
    stream,
    shutter,
    feeder,
    stencil,
    valves,
    intake,
    kernel,
    scaling,
    queries,
    matchers,
    segments,
    cotangent,
):
    local_rows = stream.shape[0]
    width_local = stream.shape[1]
    head_count = width_local // HD
    total_rows = local_rows * lax.axis_size("ctx")
    position = lax.axis_index("ctx") * local_rows
    scale_factor = 1.0 / math.sqrt(HD)
    widened = stream.astype(jnp.float32)
    inner_one = feeder.astype(jnp.float32) * widened
    rim_one = neighbor_rows(inner_one[local_rows - (KS - 1) :], 1)
    padded_one = jnp.concatenate([rim_one, inner_one], axis=0)
    conv_one = depthwise(padded_one, stencil[::-1])
    first_out = (widened + shutter.astype(jnp.float32) * conv_one).astype(jnp.bfloat16)
    first_wide = first_out.astype(jnp.float32)
    inner_two = intake.astype(jnp.float32) * first_wide
    rim_two = neighbor_rows(inner_two[local_rows - (KM - 1) :], 1)
    padded_two = jnp.concatenate([rim_two, inner_two], axis=0)
    conv_two = depthwise(padded_two, kernel[::-1])
    second_out = (first_wide + valves.astype(jnp.float32) * conv_two).astype(jnp.bfloat16)
    second_wide = second_out.astype(jnp.float32)
    squares = channel_total(jnp.sum(second_wide * second_wide, axis=1))
    inverse_rms = lax.rsqrt(squares / D + epsilon)
    normed = (second_wide * inverse_rms[:, None] * scaling).astype(jnp.bfloat16)
    ctx_count = lax.axis_size("ctx")
    ctx_index = lax.axis_index("ctx")
    keys_whole = lax.all_gather(matchers, "ctx", axis=0, tiled=True)
    reach = min(ctx_count - 1, (3 * total_rows // 4 - 1 + local_rows - 1) // local_rows)
    query_pos = position + jnp.arange(local_rows, dtype=jnp.int32)
    key_pos = jnp.arange(total_rows, dtype=jnp.int32)
    query_seg = lax.dynamic_slice_in_dim(segments, position, local_rows, 0)
    visible = (key_pos[None, :] <= query_pos[:, None]) & (segments[None, :] == query_seg[:, None])
    mask = visible.astype(jnp.float32)
    value_part = head_values_grad(queries, keys_whole, cotangent, mask, scale_factor)
    value_grad = (
        lax.all_to_all(value_part, "ctx", 0, 0, tiled=True)
        .reshape(ctx_count, local_rows, width_local)
        .astype(jnp.float32)
        .sum(axis=0)
    )
    values_whole = lax.all_gather(normed, "ctx", axis=0, tiled=True)
    key_part, attended_all, queries_grad = head_attention(
        queries, keys_whole, values_whole, cotangent, mask, scale_factor
    )
    result = (second_wide + attended_all).astype(jnp.bfloat16)
    key_part, value_grad = lax.optimization_barrier((key_part, value_grad))
    matchers_grad = lax.psum_scatter(
        key_part,
        "ctx",
        scatter_dimension=0,
        tiled=True,
    )
    gain_part = value_grad * scaling
    projected = channel_total(jnp.sum(gain_part * second_wide, axis=1))
    scaling_part = jnp.sum(value_grad * second_wide * inverse_rms[:, None], axis=0)
    second_grad = (
        cotangent.astype(jnp.float32)
        + inverse_rms[:, None] * gain_part
        - second_wide * (inverse_rms**3 * projected / D)[:, None]
    )
    valves_grad = (second_grad * conv_two).astype(jnp.bfloat16)
    dconv_two = second_grad * valves.astype(jnp.float32)
    back_two = neighbor_rows(dconv_two[: KM - 1], -1)
    dinner_two = depthwise(jnp.concatenate([dconv_two, back_two], axis=0), kernel)
    intake_grad = (dinner_two * first_wide).astype(jnp.bfloat16)
    kernel_part = depthwise(padded_two, dconv_two)[::-1]
    first_grad = second_grad + dinner_two * intake.astype(jnp.float32)
    shutter_grad = (first_grad * conv_one).astype(jnp.bfloat16)
    dconv_one = first_grad * shutter.astype(jnp.float32)
    back_one = neighbor_rows(dconv_one[: KS - 1], -1)
    dinner_one = depthwise(jnp.concatenate([dconv_one, back_one], axis=0), stencil)
    feeder_grad = (dinner_one * widened).astype(jnp.bfloat16)
    stencil_part = depthwise(padded_one, dconv_one)[::-1]
    stream_grad = (first_grad + dinner_one * feeder.astype(jnp.float32)).astype(jnp.bfloat16)
    filter_sum = butterfly_total(
        jnp.concatenate([kernel_part, scaling_part[None], stencil_part], axis=0), "ctx", jnp.bfloat16
    )
    kernel_sum = filter_sum[:KM]
    scaling_sum = filter_sum[KM]
    stencil_sum = filter_sum[KM + 1 :]
    normalizer = math.sqrt(total_rows)
    return (
        result,
        stream_grad,
        shutter_grad,
        feeder_grad,
        stencil_sum / normalizer,
        valves_grad,
        intake_grad,
        kernel_sum / normalizer,
        scaling_sum / normalizer,
        queries_grad,
        matchers_grad,
    )


def solution(mesh):
    placed = (
        P("ctx", "tp"),
        P("ctx", "tp"),
        P("ctx", "tp"),
        P(None, "tp"),
        P("ctx", "tp"),
        P("ctx", "tp"),
        P(None, "tp"),
        P("tp"),
        P("ctx", "tp"),
        P("ctx", "tp"),
        P(),
        P("ctx", "tp"),
    )
    return jax.shard_map(
        shards,
        mesh=mesh,
        in_specs=placed,
        out_specs=(
            P("ctx", "tp"),
            P("ctx", "tp"),
            P("ctx", "tp"),
            P("ctx", "tp"),
            P(None, "tp"),
            P("ctx", "tp"),
            P("ctx", "tp"),
            P(None, "tp"),
            P("tp"),
            P("ctx", "tp"),
            P("ctx", "tp"),
        ),
        check_vma=False,
    )
```
